32 devices in a mesh: cand: 2 (over core), test: 8 (over z, x), feat: 2 (over y).
Axes of the slice: x: 2, y: 2, z: 4, core: 2. Of those that a mesh axis runs over, the one named last changes fastest.
Arguments:
- x_test: float32 [32768, 256], P(('test', 'cand'), 'feat'), may hold values from -6 to 6
- x_cand: float32 [8192, 256], P(('cand', 'test'), 'feat'), may hold values from -6 to 6
- w_self: float32 [256, 256], replicated, may hold values from -0.375 to 0.375
- w_neigh: float32 [256, 256], replicated, may hold values from -1.5 to 1.5
- d_out: float32 [8192, 256], P(('cand', 'test'), 'feat'), may hold values from -6 to 6
- block_row: int32 [2, 8, 512], P('cand', 'test'), may hold values from 0 to 31, as said below
- block_col: int32 [2, 8, 512], P('cand', 'test'), may hold values from 0 to 31, as said below
- block_mask: int32 [2, 8, 512, 16, 128], P('cand', 'test'), may hold values from 0 to 255, as said below
- block_live: int32 [2, 8], P('cand', 'test'), may hold values from 170 to 512, as said below
Outputs:
- output: float32 [8192, 256], P(('cand', 'test'), 'feat')
- grad_w_self: float32 [256, 256], P('feat')
- grad_w_neigh: float32 [256, 256], P('feat')
- grad_x_cand: float32 [8192, 256], P(('cand', 'test'), 'feat')
- grad_x_test: float32 [32768, 256], P(('test', 'cand'), 'feat')
The draws below stay inside these ranges and needn't reach their ends.
Inputs may be any that keep to these rules, and one draw needn't show every extreme that they name: `block_row`: within one device's list the 512 slots name distinct (row block, column block) positions. `block_col`: within one device's list the 512 slots name distinct (row block, column block) positions. `block_mask`: each word holds 8 bits. `block_live`: some device has all 512 slots live in every draw.
All inputs are finite; a program needn't handle non-finite values.
Results may differ from the reference program's by a relative error of at most 0.0003.
Values sent between devices are 32-bit elements; how exact they have to be, the bound alone decides.
No kernel may reach another device: no remote copies, remote signals or barrier semaphores. Data moves between devices by JAX's collectives and lax.ppermute only.
A program may use at most 64 MiB of HBM per device.

```python
import math
import jax
import jax.numpy as jnp
from jax import lax

H = 256
BS = 128
RB = 32
CB = 32
NB = 512
ROWGRID = 2
COLGRID = 8
NCAND = 8192
NTEST = 32768
N_CAND = 2
N_TEST = 8


def block_places(key):
    device_total = ROWGRID * COLGRID
    place_keys = jax.random.split(jax.random.fold_in(key, 11), device_total)
    chosen = jax.vmap(lambda one_key: jax.random.permutation(one_key, RB * CB)[:NB])(place_keys)
    return chosen.reshape(ROWGRID, COLGRID, NB).astype(jnp.int32)


def draw_block_row(key, part):
    return (block_places(key) // CB).astype(jnp.int32)


def draw_block_col(key, part):
    return (block_places(key) % CB).astype(jnp.int32)


def draw_block_mask(key, part):
    packed = jnp.zeros((ROWGRID, COLGRID, NB, BS // 8, BS), jnp.int32)
    for bit_index in range(8):
        rolled = jax.random.randint(jax.random.fold_in(key, 23 + bit_index), (ROWGRID, COLGRID, NB, BS // 8, BS), 0, 1000)
        packed = packed + (rolled < 23).astype(jnp.int32) * 2 ** bit_index
    packed = packed.at[0, 0, 0, 0, 0].set(255)
    return packed


def draw_block_live(key, part):
    lowest = NB // 3
    positions = jnp.arange(COLGRID, dtype=jnp.int32)
    rising = lowest + (NB - lowest) * positions // (COLGRID - 1)
    jitter = jax.random.randint(jax.random.fold_in(key, 37), (ROWGRID, COLGRID), 0, NB // 8 + 1)
    fixed_ends = jnp.logical_or(positions[None, :] == COLGRID - 1, positions[None, :] == 0)
    jitter = jnp.where(fixed_ends, 0, jitter)
    return jnp.maximum(rising[None, :] - jitter, lowest).astype(jnp.int32)


def block_levels(stream_key, extent, pieces, low, top_value):
    level, own = 1.0, jax.random.fold_in(stream_key, 6)
    for axis_at, blocks in pieces:
        heights = jnp.exp(jax.random.uniform(jax.random.fold_in(own, axis_at), (blocks,), jnp.float32, low / len(pieces), top_value / len(pieces)))
        level = level * jnp.repeat(heights, extent[axis_at] // blocks).reshape([-1 if axis == axis_at else 1 for axis in range(len(extent))])
    return level


def noise(own_key, shape, spread, limit, shards=(), held_as=jnp.bfloat16):
    drawn = jax.random.normal(own_key, shape, jnp.float32) * spread
    if len(shards) > 0:
        drawn = block_levels(own_key, shape, shards, -0.22, 0.18) * drawn
    return jnp.clip(drawn, min=-limit, max=limit).astype(held_as)


def setup_inputs(seed: int = 0) -> dict:
    splits = jax.random.split(jax.random.key(seed), 10)
    return {
        "x_test": noise(splits[0], (NTEST, H), 1.0, 6.0, ((0, 16), (1, 2)), jnp.float32),
        "x_cand": noise(splits[1], (NCAND, H), 1.0, 6.0, ((0, 16), (1, 2)), jnp.float32),
        "w_self": noise(splits[2], (H, H), H ** -0.5, 0.375, (), jnp.float32),
        "w_neigh": noise(splits[3], (H, H), (H // 16) ** -0.5, 1.5, (), jnp.float32),
        "d_out": noise(splits[4], (NCAND, H), 1.0, 6.0, ((0, 16), (1, 2)), jnp.float32),
        "block_row": draw_block_row(jax.random.fold_in(splits[9], 71), 0),
        "block_col": draw_block_col(jax.random.fold_in(splits[9], 71), 0),
        "block_mask": draw_block_mask(jax.random.fold_in(splits[9], 71), 0),
        "block_live": draw_block_live(jax.random.fold_in(splits[9], 71), 0),
    }


HIGHEST = lax.Precision.HIGHEST

def unpack_masks(packed):
    shifts = jnp.arange(8, dtype=jnp.int32)
    bit_cube = jnp.bitwise_and(jnp.right_shift(packed[..., :, None, :], shifts[:, None]), 1)
    return bit_cube.reshape(packed.shape[:-2] + (packed.shape[-2] * 8, packed.shape[-1])).astype(jnp.float32)

def reference(x_test, x_cand, w_self, w_neigh, d_out, block_row, block_col, block_mask, block_live):
    panel_rows = RB * BS
    panel_cols = CB * BS
    slot_ids = jnp.arange(NB, dtype=jnp.int32)

    def forward_panel(cand_index):

        def over_tests(running, test_index):
            row_totals, row_counts = running
            dense_masks = unpack_masks(block_mask[cand_index, test_index])
            weights = (slot_ids < block_live[cand_index, test_index]).astype(jnp.float32)
            panel = lax.dynamic_slice_in_dim(x_test, test_index * panel_cols, panel_cols, 0)
            feature_tiles = panel.reshape(CB, BS, H)[block_col[cand_index, test_index]]
            products = jnp.einsum('bij,bjh->bih', dense_masks, feature_tiles, precision=HIGHEST) * weights[:, None, None]
            targets = block_row[cand_index, test_index]
            row_totals = row_totals + jax.ops.segment_sum(products, targets, num_segments=RB)
            row_counts = row_counts + jax.ops.segment_sum(lax.optimization_barrier(jnp.sum(dense_masks, axis=2)) * weights[:, None], targets, num_segments=RB)
            return ((row_totals, row_counts), None)
        initial = (jnp.zeros((RB, BS, H), jnp.float32), jnp.zeros((RB, BS), jnp.float32))
        (row_totals, row_counts), _ = lax.scan(over_tests, initial, jnp.arange(N_TEST, dtype=jnp.int32))
        return (row_totals.reshape(panel_rows, H), row_counts.reshape(panel_rows))
    raw_totals, raw_counts = lax.map(forward_panel, jnp.arange(N_CAND, dtype=jnp.int32))
    degree = raw_counts.reshape(NCAND)
    aggregated = raw_totals.reshape(NCAND, H) / (1.0 + degree)[:, None]
    pre_act = jnp.dot(x_cand, w_self, precision=HIGHEST) + jnp.dot(aggregated, w_neigh, precision=HIGHEST)
    output = jax.nn.silu(pre_act)
    sigmoid_z = jax.nn.sigmoid(pre_act)
    grad_pre = d_out * (sigmoid_z * (1.0 + pre_act * (1.0 - sigmoid_z)))
    root_count = math.sqrt(NCAND)
    grad_w_self = jnp.einsum('rk,rh->kh', x_cand, grad_pre, precision=HIGHEST) / root_count
    grad_w_neigh = jnp.einsum('rk,rh->kh', aggregated, grad_pre, precision=HIGHEST) / root_count
    grad_x_cand = jnp.dot(grad_pre, w_self.T, precision=HIGHEST)
    grad_agg = jnp.dot(grad_pre, w_neigh.T, precision=HIGHEST)
    lifted = grad_agg / (1.0 + degree)[:, None]

    def backward_panel(test_index):

        def over_cands(running, cand_index):
            dense_masks = unpack_masks(block_mask[cand_index, test_index])
            weights = (slot_ids < block_live[cand_index, test_index]).astype(jnp.float32)
            rows_slab = lax.dynamic_slice_in_dim(lifted, cand_index * panel_rows, panel_rows, 0)
            picked = rows_slab.reshape(RB, BS, H)[block_row[cand_index, test_index]]
            products = jnp.einsum('bji,bjh->bih', dense_masks, picked, precision=HIGHEST) * weights[:, None, None]
            return (running + jax.ops.segment_sum(products, block_col[cand_index, test_index], num_segments=CB), None)
        running, _ = lax.scan(over_cands, jnp.zeros((CB, BS, H), jnp.float32), jnp.arange(N_CAND, dtype=jnp.int32))
        return running.reshape(panel_cols, H)
    grad_x_test = lax.map(backward_panel, jnp.arange(N_TEST, dtype=jnp.int32)).reshape(NTEST, H)
    return (output, grad_w_self, grad_w_neigh, grad_x_cand, grad_x_test)
```

```python
import math

import jax
import jax.numpy as jnp
from jax import lax
from jax.experimental import pallas as pl
from jax.experimental.pallas import tpu as pltpu
from jax.sharding import PartitionSpec as P

HIGHEST = lax.Precision.HIGHEST
SLOT_GROUP = 64


def split_hi_lo(values):
    high = lax.reduce_precision(values, exponent_bits=8, mantissa_bits=7)
    low = values - high
    return jnp.concatenate([high, low], axis=1).astype(jnp.bfloat16)


def unpack_block(words):
    word_rows, edge = words.shape
    cube = jnp.broadcast_to(words[:, None, :], (word_rows, 8, edge))
    shifts = lax.broadcasted_iota(jnp.int32, (word_rows, 8, edge), 1)
    bits = jnp.bitwise_and(jnp.right_shift(cube, shifts), 1)
    return bits.reshape(word_rows * 8, edge).astype(jnp.float32)


def slot_range(live_ref, group):
    base = pl.program_id(0) * group
    count = jnp.clip(live_ref[0] - base, 0, group)
    return base, count


def forward_kernel(live_ref, rows_ref, cols_ref, masks_ref, panel_ref, totals_ref, counts_ref):
    group, _, edge = masks_ref.shape
    row_limit = counts_ref.shape[0] - 1
    col_limit = panel_ref.shape[0] // edge - 1

    @pl.when(pl.program_id(0) == 0)
    def _():
        totals_ref[...] = jnp.zeros_like(totals_ref)
        counts_ref[...] = jnp.zeros_like(counts_ref)

    base, count = slot_range(live_ref, group)
    ones = jnp.ones((8, edge), jnp.bfloat16)
    half = totals_ref.shape[1]

    def body(k, carry):
        slot = base + k
        row = jnp.clip(rows_ref[slot], 0, row_limit)
        col = jnp.clip(cols_ref[slot], 0, col_limit)
        dense = unpack_block(masks_ref[k]).astype(jnp.bfloat16)
        tile = panel_ref[pl.ds(pl.multiple_of(col * edge, edge), edge), :]
        prod = jnp.dot(dense, tile, preferred_element_type=jnp.float32)
        start = pl.multiple_of(row * edge, edge)
        totals_ref[pl.ds(start, edge), :] += prod[:, :half] + prod[:, half:]
        counts_ref[row] += lax.dot_general(
            ones, dense, (((1,), (1,)), ((), ())), preferred_element_type=jnp.float32
        )
        return carry

    lax.fori_loop(0, count, body, 0)


def backward_kernel(live_ref, rows_ref, cols_ref, masks_ref, lifted_ref, out_ref):
    group, _, edge = masks_ref.shape
    row_limit = lifted_ref.shape[0] // edge - 1
    col_limit = out_ref.shape[0] // edge - 1

    @pl.when(pl.program_id(0) == 0)
    def _():
        out_ref[...] = jnp.zeros_like(out_ref)

    base, count = slot_range(live_ref, group)
    half = out_ref.shape[1]

    def body(k, carry):
        slot = base + k
        row = jnp.clip(rows_ref[slot], 0, row_limit)
        col = jnp.clip(cols_ref[slot], 0, col_limit)
        dense_t = unpack_block(masks_ref[k]).T.astype(jnp.bfloat16)
        tile = lifted_ref[pl.ds(pl.multiple_of(row * edge, edge), edge), :]
        prod = jnp.dot(dense_t, tile, preferred_element_type=jnp.float32)
        start = pl.multiple_of(col * edge, edge)
        out_ref[pl.ds(start, edge), :] += prod[:, :half] + prod[:, half:]
        return carry

    lax.fori_loop(0, count, body, 0)


def mask_spec(packed_masks, group):
    word_rows, edge = packed_masks.shape[1:]

    def index_map(chunk, live_ref, rows_ref, cols_ref):
        last = jnp.maximum(live_ref[0] - 1, 0) // group
        return (jnp.minimum(chunk, last), 0, 0)

    return pl.BlockSpec((group, word_rows, edge), index_map)


def whole_spec(shape):
    return pl.BlockSpec(shape, lambda chunk, live_ref, rows_ref, cols_ref: (0,) * len(shape))


def block_aggregate(live, block_rows, block_cols, packed_masks, panel_split, row_blocks):
    slot_total, _, edge = packed_masks.shape
    group = min(SLOT_GROUP, slot_total)
    half = panel_split.shape[1] // 2
    totals_shape = (row_blocks * edge, half)
    counts_shape = (row_blocks, 8, edge)
    grid_spec = pltpu.PrefetchScalarGridSpec(
        num_scalar_prefetch=3,
        grid=(slot_total // group,),
        in_specs=[mask_spec(packed_masks, group), whole_spec(panel_split.shape)],
        out_specs=[whole_spec(totals_shape), whole_spec(counts_shape)],
    )
    totals, counts = pl.pallas_call(
        forward_kernel,
        grid_spec=grid_spec,
        out_shape=[
            jax.ShapeDtypeStruct(totals_shape, jnp.float32),
            jax.ShapeDtypeStruct(counts_shape, jnp.float32),
        ],
        compiler_params=pltpu.CompilerParams(dimension_semantics=("arbitrary",)),
    )(live, block_rows, block_cols, packed_masks, panel_split)
    return totals, counts[:, 0, :].reshape(-1)


def block_transpose(live, block_rows, block_cols, packed_masks, lifted_split, col_blocks):
    slot_total, _, edge = packed_masks.shape
    group = min(SLOT_GROUP, slot_total)
    half = lifted_split.shape[1] // 2
    out_shape = (col_blocks * edge, half)
    grid_spec = pltpu.PrefetchScalarGridSpec(
        num_scalar_prefetch=3,
        grid=(slot_total // group,),
        in_specs=[mask_spec(packed_masks, group), whole_spec(lifted_split.shape)],
        out_specs=whole_spec(out_shape),
    )
    return pl.pallas_call(
        backward_kernel,
        grid_spec=grid_spec,
        out_shape=jax.ShapeDtypeStruct(out_shape, jnp.float32),
        compiler_params=pltpu.CompilerParams(dimension_semantics=("arbitrary",)),
    )(live, block_rows, block_cols, packed_masks, lifted_split)


def local(x_test, x_cand, w_self, w_neigh, d_out, block_row, block_col, block_mask, block_live):
    packed_masks = block_mask.reshape(block_mask.shape[2:])
    block_rows = block_row.reshape(-1)
    block_cols = block_col.reshape(-1)
    live = jnp.clip(block_live.reshape(1), 0, packed_masks.shape[0])
    block_edge = packed_masks.shape[-1]
    cand_count = lax.axis_size("cand")
    test_count = lax.axis_size("test")
    feat_index = lax.axis_index("feat")
    half_width = x_cand.shape[1]
    row_blocks = x_cand.shape[0] * test_count // block_edge
    col_blocks = x_test.shape[0] * cand_count // block_edge
    panel = lax.all_gather(x_test, "cand", axis=0, tiled=True)
    row_totals, row_counts = block_aggregate(
        live, block_rows, block_cols, packed_masks, split_hi_lo(panel), row_blocks
    )
    own_totals, degree = (
        lax.psum_scatter(row_totals, "test", scatter_dimension=0, tiled=True),
        lax.psum_scatter(row_counts, "test", scatter_dimension=0, tiled=True),
    )
    aggregated = own_totals / (1.0 + degree)[:, None]
    self_cols = lax.dynamic_slice_in_dim(w_self, feat_index * half_width, half_width, 1)
    neigh_cols = lax.dynamic_slice_in_dim(w_neigh, feat_index * half_width, half_width, 1)
    self_rows = lax.dynamic_slice_in_dim(w_self, feat_index * half_width, half_width, 0)
    neigh_rows = lax.dynamic_slice_in_dim(w_neigh, feat_index * half_width, half_width, 0)
    cand_full, aggregated_full = (
        lax.all_gather(x_cand, "feat", axis=1, tiled=True),
        lax.all_gather(aggregated, "feat", axis=1, tiled=True),
    )
    pre_act = jnp.dot(cand_full, self_cols, precision=HIGHEST) + jnp.dot(
        aggregated_full, neigh_cols, precision=HIGHEST
    )
    output = jax.nn.silu(pre_act)
    sigmoid_z = jax.nn.sigmoid(pre_act)
    grad_pre = d_out * (sigmoid_z * (1.0 + pre_act * (1.0 - sigmoid_z)))
    grad_full = lax.all_gather(grad_pre, "feat", axis=1, tiled=True)
    self_part = jnp.einsum("rk,rh->kh", x_cand, grad_full, precision=HIGHEST)
    neigh_part = jnp.einsum("rk,rh->kh", aggregated, grad_full, precision=HIGHEST)
    self_sum, neigh_sum = lax.psum((self_part, neigh_part), ("cand", "test"))
    root_count = math.sqrt(x_cand.shape[0] * cand_count * test_count)
    grad_w_self = self_sum / root_count
    grad_w_neigh = neigh_sum / root_count
    grad_x_cand = jnp.dot(grad_full, self_rows.T, precision=HIGHEST)
    grad_agg = jnp.dot(grad_full, neigh_rows.T, precision=HIGHEST)
    lifted = grad_agg / (1.0 + degree)[:, None]
    gathered_rows = lax.all_gather(lifted, "test", axis=0, tiled=True)
    column_terms = block_transpose(
        live, block_rows, block_cols, packed_masks, split_hi_lo(gathered_rows), col_blocks
    )
    grad_x_test = lax.psum_scatter(column_terms, "cand", scatter_dimension=0, tiled=True)
    return (output, grad_w_self, grad_w_neigh, grad_x_cand, grad_x_test)


def solution(mesh):
    return jax.shard_map(
        local,
        mesh=mesh,
        in_specs=(
            P(("test", "cand"), "feat"),
            P(("cand", "test"), "feat"),
            P(),
            P(),
            P(("cand", "test"), "feat"),
            P("cand", "test", None),
            P("cand", "test", None),
            P("cand", "test", None, None, None),
            P("cand", "test"),
        ),
        out_specs=(
            P(("cand", "test"), "feat"),
            P("feat", None),
            P("feat", None),
            P(("cand", "test"), "feat"),
            P(("test", "cand"), "feat"),
        ),
        check_vma=False,
    )
```

```python
import math

import jax
import jax.numpy as jnp
from jax import lax
from jax.experimental import pallas as pl
from jax.experimental.pallas import tpu as pltpu
from jax.sharding import PartitionSpec as P

HIGHEST = lax.Precision.HIGHEST
SLOT_GROUP = 64


def split_hi_lo(values):
    high = lax.reduce_precision(values, exponent_bits=8, mantissa_bits=7)
    low = values - high
    return jnp.concatenate([high, low], axis=1).astype(jnp.bfloat16)


def unpack_block(words):
    word_rows, edge = words.shape
    cube = jnp.broadcast_to(words[:, None, :], (word_rows, 8, edge))
    shifts = lax.broadcasted_iota(jnp.int32, (word_rows, 8, edge), 1)
    bits = jnp.bitwise_and(jnp.right_shift(cube, shifts), 1)
    return bits.reshape(word_rows * 8, edge).astype(jnp.float32)


def slot_range(live_ref, group):
    base = pl.program_id(0) * group
    count = jnp.clip(live_ref[0] - base, 0, group)
    return base, count


def forward_kernel(live_ref, rows_ref, cols_ref, masks_ref, panel_ref, totals_ref, counts_ref):
    group, _, edge = masks_ref.shape
    row_limit = counts_ref.shape[0] - 1
    col_limit = panel_ref.shape[0] // edge - 1

    @pl.when(pl.program_id(0) == 0)
    def _():
        totals_ref[...] = jnp.zeros_like(totals_ref)
        counts_ref[...] = jnp.zeros_like(counts_ref)

    base, count = slot_range(live_ref, group)
    ones = jnp.ones((8, edge), jnp.bfloat16)
    half = totals_ref.shape[1]

    def body(k, carry):
        slot = base + k
        row = jnp.clip(rows_ref[slot], 0, row_limit)
        col = jnp.clip(cols_ref[slot], 0, col_limit)
        dense = unpack_block(masks_ref[k]).astype(jnp.bfloat16)
        tile = panel_ref[pl.ds(pl.multiple_of(col * edge, edge), edge), :]
        prod = jnp.dot(dense, tile, preferred_element_type=jnp.float32)
        start = pl.multiple_of(row * edge, edge)
        totals_ref[pl.ds(start, edge), :] += prod[:, :half] + prod[:, half:]
        counts_ref[row] += lax.dot_general(
            ones, dense, (((1,), (1,)), ((), ())), preferred_element_type=jnp.float32
        )
        return carry

    lax.fori_loop(0, count, body, 0)


def backward_kernel(live_ref, rows_ref, cols_ref, masks_ref, lifted_ref, out_ref):
    group, _, edge = masks_ref.shape
    row_limit = lifted_ref.shape[0] // edge - 1
    col_limit = out_ref.shape[0] // edge - 1

    @pl.when(pl.program_id(0) == 0)
    def _():
        out_ref[...] = jnp.zeros_like(out_ref)

    base, count = slot_range(live_ref, group)
    half = out_ref.shape[1]

    def body(k, carry):
        slot = base + k
        row = jnp.clip(rows_ref[slot], 0, row_limit)
        col = jnp.clip(cols_ref[slot], 0, col_limit)
        dense_t = unpack_block(masks_ref[k]).T.astype(jnp.bfloat16)
        tile = lifted_ref[pl.ds(pl.multiple_of(row * edge, edge), edge), :]
        prod = jnp.dot(dense_t, tile, preferred_element_type=jnp.float32)
        start = pl.multiple_of(col * edge, edge)
        out_ref[pl.ds(start, edge), :] += prod[:, :half] + prod[:, half:]
        return carry

    lax.fori_loop(0, count, body, 0)


def mask_spec(packed_masks, group):
    word_rows, edge = packed_masks.shape[1:]

    def index_map(chunk, live_ref, rows_ref, cols_ref):
        last = jnp.maximum(live_ref[0] - 1, 0) // group
        return (jnp.minimum(chunk, last), 0, 0)

    return pl.BlockSpec((group, word_rows, edge), index_map)


def whole_spec(shape):
    return pl.BlockSpec(shape, lambda chunk, live_ref, rows_ref, cols_ref: (0,) * len(shape))


def block_aggregate(live, block_rows, block_cols, packed_masks, panel_split, row_blocks):
    slot_total, _, edge = packed_masks.shape
    group = min(SLOT_GROUP, slot_total)
    half = panel_split.shape[1] // 2
    totals_shape = (row_blocks * edge, half)
    counts_shape = (row_blocks, 8, edge)
    grid_spec = pltpu.PrefetchScalarGridSpec(
        num_scalar_prefetch=3,
        grid=(slot_total // group,),
        in_specs=[mask_spec(packed_masks, group), whole_spec(panel_split.shape)],
        out_specs=[whole_spec(totals_shape), whole_spec(counts_shape)],
    )
    totals, counts = pl.pallas_call(
        forward_kernel,
        grid_spec=grid_spec,
        out_shape=[
            jax.ShapeDtypeStruct(totals_shape, jnp.float32),
            jax.ShapeDtypeStruct(counts_shape, jnp.float32),
        ],
        compiler_params=pltpu.CompilerParams(dimension_semantics=("arbitrary",)),
    )(live, block_rows, block_cols, packed_masks, panel_split)
    return totals, counts[:, 0, :].reshape(-1)


def block_transpose(live, block_rows, block_cols, packed_masks, lifted_split, col_blocks):
    slot_total, _, edge = packed_masks.shape
    group = min(SLOT_GROUP, slot_total)
    half = lifted_split.shape[1] // 2
    out_shape = (col_blocks * edge, half)
    grid_spec = pltpu.PrefetchScalarGridSpec(
        num_scalar_prefetch=3,
        grid=(slot_total // group,),
        in_specs=[mask_spec(packed_masks, group), whole_spec(lifted_split.shape)],
        out_specs=whole_spec(out_shape),
    )
    return pl.pallas_call(
        backward_kernel,
        grid_spec=grid_spec,
        out_shape=jax.ShapeDtypeStruct(out_shape, jnp.float32),
        compiler_params=pltpu.CompilerParams(dimension_semantics=("arbitrary",)),
    )(live, block_rows, block_cols, packed_masks, lifted_split)


def swap(values, axis):
    return lax.ppermute(values, axis, [(0, 1), (1, 0)])


def gather_axis(values, axis, dim):
    if lax.axis_size(axis) != 2:
        return lax.all_gather(values, axis, axis=dim, tiled=True)
    other = swap(values, axis)
    first = lax.axis_index(axis) == 0
    return jnp.concatenate(
        [jnp.where(first, values, other), jnp.where(first, other, values)], axis=dim
    )


def scatter_sum_axis(values, axis):
    if lax.axis_size(axis) != 2:
        return lax.psum_scatter(values, axis, scatter_dimension=0, tiled=True)
    rows = values.shape[0] // 2
    index = lax.axis_index(axis)
    own = lax.dynamic_slice_in_dim(values, index * rows, rows, 0)
    other = lax.dynamic_slice_in_dim(values, (1 - index) * rows, rows, 0)
    return own + swap(other, axis)


def scatter_totals_and_counts(row_totals, row_counts, test_count):
    width = row_totals.shape[1]
    chunk_rows = row_totals.shape[0] // test_count
    count_rows = chunk_rows // width
    padded = -(-count_rows // 16) * 16
    pieces = [
        row_totals.reshape(test_count, chunk_rows, width),
        row_counts.reshape(test_count, count_rows, width),
    ]
    if padded > count_rows:
        pieces.append(jnp.zeros((test_count, padded - count_rows, width), jnp.float32))
    combined = jnp.concatenate(pieces, axis=1).reshape(-1, width)
    own = lax.psum_scatter(combined, "test", scatter_dimension=0, tiled=True)
    return own[:chunk_rows], own[chunk_rows : chunk_rows + count_rows].reshape(-1)


def local(x_test, x_cand, w_self, w_neigh, d_out, block_row, block_col, block_mask, block_live):
    packed_masks = block_mask.reshape(block_mask.shape[2:])
    block_rows = block_row.reshape(-1)
    block_cols = block_col.reshape(-1)
    live = jnp.clip(block_live.reshape(1), 0, packed_masks.shape[0])
    block_edge = packed_masks.shape[-1]
    cand_count = lax.axis_size("cand")
    test_count = lax.axis_size("test")
    feat_index = lax.axis_index("feat")
    half_width = x_cand.shape[1]
    row_blocks = x_cand.shape[0] * test_count // block_edge
    col_blocks = x_test.shape[0] * cand_count // block_edge
    panel = gather_axis(x_test, "cand", 0)
    cand_full = gather_axis(x_cand, "feat", 1)
    row_totals, row_counts = block_aggregate(
        live, block_rows, block_cols, packed_masks, split_hi_lo(panel), row_blocks
    )
    own_totals, degree = scatter_totals_and_counts(row_totals, row_counts, test_count)
    aggregated = own_totals / (1.0 + degree)[:, None]
    self_cols = lax.dynamic_slice_in_dim(w_self, feat_index * half_width, half_width, 1)
    neigh_cols = lax.dynamic_slice_in_dim(w_neigh, feat_index * half_width, half_width, 1)
    self_rows = lax.dynamic_slice_in_dim(w_self, feat_index * half_width, half_width, 0)
    neigh_rows = lax.dynamic_slice_in_dim(w_neigh, feat_index * half_width, half_width, 0)
    aggregated_full = gather_axis(aggregated, "feat", 1)
    pre_act = jnp.dot(cand_full, self_cols, precision=HIGHEST) + jnp.dot(
        aggregated_full, neigh_cols, precision=HIGHEST
    )
    output = jax.nn.silu(pre_act)
    sigmoid_z = jax.nn.sigmoid(pre_act)
    grad_pre = d_out * (sigmoid_z * (1.0 + pre_act * (1.0 - sigmoid_z)))
    grad_full = gather_axis(grad_pre, "feat", 1)
    self_part = jnp.einsum("rk,rh->kh", x_cand, grad_full, precision=HIGHEST)
    neigh_part = jnp.einsum("rk,rh->kh", aggregated, grad_full, precision=HIGHEST)
    self_sum, neigh_sum = lax.psum((self_part, neigh_part), ("cand", "test"))
    root_count = math.sqrt(x_cand.shape[0] * cand_count * test_count)
    grad_w_self = self_sum / root_count
    grad_w_neigh = neigh_sum / root_count
    grad_x_cand = jnp.dot(grad_full, self_rows.T, precision=HIGHEST)
    grad_agg = jnp.dot(grad_full, neigh_rows.T, precision=HIGHEST)
    lifted = grad_agg / (1.0 + degree)[:, None]
    gathered_rows = lax.all_gather(lifted, "test", axis=0, tiled=True)
    column_terms = block_transpose(
        live, block_rows, block_cols, packed_masks, split_hi_lo(gathered_rows), col_blocks
    )
    grad_x_test = scatter_sum_axis(column_terms, "cand")
    return (output, grad_w_self, grad_w_neigh, grad_x_cand, grad_x_test)


def solution(mesh):
    return jax.shard_map(
        local,
        mesh=mesh,
        in_specs=(
            P(("test", "cand"), "feat"),
            P(("cand", "test"), "feat"),
            P(),
            P(),
            P(("cand", "test"), "feat"),
            P("cand", "test", None),
            P("cand", "test", None),
            P("cand", "test", None, None, None),
            P("cand", "test"),
        ),
        out_specs=(
            P(("cand", "test"), "feat"),
            P("feat", None),
            P("feat", None),
            P(("cand", "test"), "feat"),
            P(("test", "cand"), "feat"),
        ),
        check_vma=False,
    )
```

```python
import math

import jax
import jax.numpy as jnp
from jax import lax
from jax.experimental import pallas as pl
from jax.experimental.pallas import tpu as pltpu
from jax.sharding import PartitionSpec as P

HIGHEST = lax.Precision.HIGHEST
SLOT_GROUP = 64


def split_hi_lo(values):
    high = lax.reduce_precision(values, exponent_bits=8, mantissa_bits=7)
    low = values - high
    return jnp.concatenate([high, low], axis=1).astype(jnp.bfloat16)


def unpack_block(words):
    word_rows, edge = words.shape
    cube = jnp.broadcast_to(words[:, None, :], (word_rows, 8, edge))
    shifts = lax.broadcasted_iota(jnp.int32, (word_rows, 8, edge), 1)
    bits = jnp.bitwise_and(jnp.right_shift(cube, shifts), 1)
    return bits.reshape(word_rows * 8, edge).astype(jnp.float32)


def slot_range(live_ref, group):
    base = pl.program_id(0) * group
    count = jnp.clip(live_ref[0] - base, 0, group)
    return base, count


def forward_kernel(live_ref, rows_ref, cols_ref, masks_ref, panel_ref, totals_ref, counts_ref):
    group, _, edge = masks_ref.shape
    row_limit = counts_ref.shape[0] - 1
    col_limit = panel_ref.shape[0] // edge - 1

    @pl.when(pl.program_id(0) == 0)
    def _():
        totals_ref[...] = jnp.zeros_like(totals_ref)
        counts_ref[...] = jnp.zeros_like(counts_ref)

    base, count = slot_range(live_ref, group)
    ones = jnp.ones((8, edge), jnp.bfloat16)
    half = totals_ref.shape[1]

    def body(k, carry):
        slot = base + k
        row = jnp.clip(rows_ref[slot], 0, row_limit)
        col = jnp.clip(cols_ref[slot], 0, col_limit)
        dense = unpack_block(masks_ref[k]).astype(jnp.bfloat16)
        tile = panel_ref[pl.ds(pl.multiple_of(col * edge, edge), edge), :]
        prod = jnp.dot(dense, tile, preferred_element_type=jnp.float32)
        start = pl.multiple_of(row * edge, edge)
        totals_ref[pl.ds(start, edge), :] += prod[:, :half] + prod[:, half:]
        counts_ref[row] += lax.dot_general(
            ones, dense, (((1,), (1,)), ((), ())), preferred_element_type=jnp.float32
        )
        return carry

    lax.fori_loop(0, count, body, 0)


def backward_kernel(live_ref, rows_ref, cols_ref, masks_ref, lifted_ref, out_ref):
    group, _, edge = masks_ref.shape
    row_limit = lifted_ref.shape[0] // edge - 1
    col_limit = out_ref.shape[0] // edge - 1

    @pl.when(pl.program_id(0) == 0)
    def _():
        out_ref[...] = jnp.zeros_like(out_ref)

    base, count = slot_range(live_ref, group)
    half = out_ref.shape[1]

    def body(k, carry):
        slot = base + k
        row = jnp.clip(rows_ref[slot], 0, row_limit)
        col = jnp.clip(cols_ref[slot], 0, col_limit)
        dense_t = unpack_block(masks_ref[k]).T.astype(jnp.bfloat16)
        tile = lifted_ref[pl.ds(pl.multiple_of(row * edge, edge), edge), :]
        prod = jnp.dot(dense_t, tile, preferred_element_type=jnp.float32)
        start = pl.multiple_of(col * edge, edge)
        out_ref[pl.ds(start, edge), :] += prod[:, :half] + prod[:, half:]
        return carry

    lax.fori_loop(0, count, body, 0)


def mask_spec(packed_masks, group):
    word_rows, edge = packed_masks.shape[1:]

    def index_map(chunk, live_ref, rows_ref, cols_ref):
        last = jnp.maximum(live_ref[0] - 1, 0) // group
        return (jnp.minimum(chunk, last), 0, 0)

    return pl.BlockSpec((group, word_rows, edge), index_map)


def whole_spec(shape):
    return pl.BlockSpec(shape, lambda chunk, live_ref, rows_ref, cols_ref: (0,) * len(shape))


def block_aggregate(live, block_rows, block_cols, packed_masks, panel_split, row_blocks):
    slot_total, _, edge = packed_masks.shape
    group = min(SLOT_GROUP, slot_total)
    half = panel_split.shape[1] // 2
    totals_shape = (row_blocks * edge, half)
    counts_shape = (row_blocks, 8, edge)
    grid_spec = pltpu.PrefetchScalarGridSpec(
        num_scalar_prefetch=3,
        grid=(slot_total // group,),
        in_specs=[mask_spec(packed_masks, group), whole_spec(panel_split.shape)],
        out_specs=[whole_spec(totals_shape), whole_spec(counts_shape)],
    )
    totals, counts = pl.pallas_call(
        forward_kernel,
        grid_spec=grid_spec,
        out_shape=[
            jax.ShapeDtypeStruct(totals_shape, jnp.float32),
            jax.ShapeDtypeStruct(counts_shape, jnp.float32),
        ],
        compiler_params=pltpu.CompilerParams(dimension_semantics=("arbitrary",)),
    )(live, block_rows, block_cols, packed_masks, panel_split)
    return totals, counts[:, 0, :].reshape(-1)


def block_transpose(live, block_rows, block_cols, packed_masks, lifted_split, col_blocks):
    slot_total, _, edge = packed_masks.shape
    group = min(SLOT_GROUP, slot_total)
    half = lifted_split.shape[1] // 2
    out_shape = (col_blocks * edge, half)
    grid_spec = pltpu.PrefetchScalarGridSpec(
        num_scalar_prefetch=3,
        grid=(slot_total // group,),
        in_specs=[mask_spec(packed_masks, group), whole_spec(lifted_split.shape)],
        out_specs=whole_spec(out_shape),
    )
    return pl.pallas_call(
        backward_kernel,
        grid_spec=grid_spec,
        out_shape=jax.ShapeDtypeStruct(out_shape, jnp.float32),
        compiler_params=pltpu.CompilerParams(dimension_semantics=("arbitrary",)),
    )(live, block_rows, block_cols, packed_masks, lifted_split)


def axis_bits(axis):
    count = lax.axis_size(axis)
    bits = count.bit_length() - 1
    assert count == 1 << bits
    return bits


def exchange(values, axis, bit):
    count = lax.axis_size(axis)
    return lax.ppermute(values, axis, [(i, i ^ (1 << bit)) for i in range(count)])


def axis_bit(axis, bit):
    return (lax.axis_index(axis) >> bit) & 1


def gather_axis(values, axis, dim):
    if lax.axis_size(axis) != 2:
        return lax.all_gather(values, axis, axis=dim, tiled=True)
    other = exchange(values, axis, 0)
    first = lax.axis_index(axis) == 0
    return jnp.concatenate(
        [jnp.where(first, values, other), jnp.where(first, other, values)], axis=dim
    )


def halving_scatter(values, axis):
    bits = axis_bits(axis)
    chunk = values.shape[0] >> bits
    data = values.reshape((2,) * bits + (chunk,) + values.shape[1:])
    for bit in range(bits):
        position = bits - 1 - bit
        mine = axis_bit(axis, bit)
        keep = lax.dynamic_index_in_dim(data, mine, position, keepdims=False)
        send = lax.dynamic_index_in_dim(data, 1 - mine, position, keepdims=False)
        data = keep + exchange(send, axis, bit)
    return data


def doubling_gather(values, axis):
    bits = axis_bits(axis)
    data = values
    for stacked, bit in enumerate(reversed(range(bits))):
        other = exchange(data, axis, bit)
        first = axis_bit(axis, bit) == 0
        data = jnp.where(
            first, jnp.stack([data, other], axis=stacked), jnp.stack([other, data], axis=stacked)
        )
    return data.reshape((-1,) + values.shape[1:])


def butterfly_sum(values, axes):
    for axis in axes:
        for bit in range(axis_bits(axis)):
            values = values + exchange(values, axis, bit)
    return values


def scatter_totals_and_counts(row_totals, row_counts, test_count):
    width = row_totals.shape[1]
    chunk_rows = row_totals.shape[0] // test_count
    count_rows = chunk_rows // width
    padded = -(-count_rows // 8) * 8
    pieces = [
        row_totals.reshape(test_count, chunk_rows, width),
        row_counts.reshape(test_count, count_rows, width),
    ]
    if padded > count_rows:
        pieces.append(jnp.zeros((test_count, padded - count_rows, width), jnp.float32))
    combined = jnp.concatenate(pieces, axis=1).reshape(-1, width)
    own = halving_scatter(combined, "test")
    return own[:chunk_rows], own[chunk_rows : chunk_rows + count_rows].reshape(-1)


def local(x_test, x_cand, w_self, w_neigh, d_out, block_row, block_col, block_mask, block_live):
    packed_masks = block_mask.reshape(block_mask.shape[2:])
    block_rows = block_row.reshape(-1)
    block_cols = block_col.reshape(-1)
    live = jnp.clip(block_live.reshape(1), 0, packed_masks.shape[0])
    block_edge = packed_masks.shape[-1]
    cand_count = lax.axis_size("cand")
    test_count = lax.axis_size("test")
    feat_index = lax.axis_index("feat")
    half_width = x_cand.shape[1]
    row_blocks = x_cand.shape[0] * test_count // block_edge
    col_blocks = x_test.shape[0] * cand_count // block_edge
    panel = doubling_gather(x_test, "cand")
    cand_full = gather_axis(x_cand, "feat", 1)
    row_totals, row_counts = block_aggregate(
        live, block_rows, block_cols, packed_masks, split_hi_lo(panel), row_blocks
    )
    own_totals, degree = scatter_totals_and_counts(row_totals, row_counts, test_count)
    aggregated = own_totals / (1.0 + degree)[:, None]
    self_cols = lax.dynamic_slice_in_dim(w_self, feat_index * half_width, half_width, 1)
    neigh_cols = lax.dynamic_slice_in_dim(w_neigh, feat_index * half_width, half_width, 1)
    self_rows = lax.dynamic_slice_in_dim(w_self, feat_index * half_width, half_width, 0)
    neigh_rows = lax.dynamic_slice_in_dim(w_neigh, feat_index * half_width, half_width, 0)
    aggregated_full = gather_axis(aggregated, "feat", 1)
    pre_act = jnp.dot(cand_full, self_cols, precision=HIGHEST) + jnp.dot(
        aggregated_full, neigh_cols, precision=HIGHEST
    )
    output = jax.nn.silu(pre_act)
    sigmoid_z = jax.nn.sigmoid(pre_act)
    grad_pre = d_out * (sigmoid_z * (1.0 + pre_act * (1.0 - sigmoid_z)))
    grad_full = gather_axis(grad_pre, "feat", 1)
    self_part = jnp.einsum("rk,rh->kh", x_cand, grad_full, precision=HIGHEST)
    neigh_part = jnp.einsum("rk,rh->kh", aggregated, grad_full, precision=HIGHEST)
    self_sum, neigh_sum = butterfly_sum(jnp.stack([self_part, neigh_part]), ("cand", "test"))
    root_count = math.sqrt(x_cand.shape[0] * cand_count * test_count)
    grad_w_self = self_sum / root_count
    grad_w_neigh = neigh_sum / root_count
    grad_x_cand = jnp.dot(grad_full, self_rows.T, precision=HIGHEST)
    grad_agg = jnp.dot(grad_full, neigh_rows.T, precision=HIGHEST)
    lifted = grad_agg / (1.0 + degree)[:, None]
    gathered_rows = doubling_gather(lifted, "test")
    column_terms = block_transpose(
        live, block_rows, block_cols, packed_masks, split_hi_lo(gathered_rows), col_blocks
    )
    grad_x_test = halving_scatter(column_terms, "cand")
    return (output, grad_w_self, grad_w_neigh, grad_x_cand, grad_x_test)


def solution(mesh):
    return jax.shard_map(
        local,
        mesh=mesh,
        in_specs=(
            P(("test", "cand"), "feat"),
            P(("cand", "test"), "feat"),
            P(),
            P(),
            P(("cand", "test"), "feat"),
            P("cand", "test", None),
            P("cand", "test", None),
            P("cand", "test", None, None, None),
            P("cand", "test"),
        ),
        out_specs=(
            P(("cand", "test"), "feat"),
            P("feat", None),
            P("feat", None),
            P(("cand", "test"), "feat"),
            P(("test", "cand"), "feat"),
        ),
        check_vma=False,
    )
```

```python
import math

import jax
import jax.numpy as jnp
from jax import lax
from jax.experimental import pallas as pl
from jax.experimental.pallas import tpu as pltpu
from jax.sharding import PartitionSpec as P

HIGHEST = lax.Precision.HIGHEST
SLOT_GROUP = 64


def split_hi_lo(values):
    high = lax.reduce_precision(values, exponent_bits=8, mantissa_bits=7)
    low = values - high
    return jnp.concatenate([high, low], axis=1).astype(jnp.bfloat16)


def unpack_block(words):
    word_rows, edge = words.shape
    cube = jnp.broadcast_to(words[:, None, :], (word_rows, 8, edge))
    shifts = lax.broadcasted_iota(jnp.int32, (word_rows, 8, edge), 1)
    bits = jnp.bitwise_and(jnp.right_shift(cube, shifts), 1)
    return bits.reshape(word_rows * 8, edge).astype(jnp.float32)


UNROLL = 8


def live_chunk(live_ref, group):
    base = pl.program_id(0) * group
    return base, base < live_ref[0]


def slot_words(masks_ref, live_ref, base, k):
    keep = jnp.where(base + k < live_ref[0], -1, 0).astype(jnp.int32)
    return unpack_block(jnp.bitwise_and(masks_ref[k], keep)).astype(jnp.bfloat16)


def forward_kernel(live_ref, rows_ref, cols_ref, masks_ref, panel_ref, totals_ref):
    group, _, edge = masks_ref.shape
    row_limit = totals_ref.shape[0] // edge - 1
    col_limit = panel_ref.shape[0] // edge - 1
    half = totals_ref.shape[1]

    @pl.when(pl.program_id(0) == 0)
    def _():
        totals_ref[...] = jnp.zeros_like(totals_ref)

    base, active = live_chunk(live_ref, group)

    @pl.when(active)
    def _():
        def body(k, carry):
            slot = base + k
            row = jnp.clip(rows_ref[slot], 0, row_limit)
            col = jnp.clip(cols_ref[slot], 0, col_limit)
            dense = slot_words(masks_ref, live_ref, base, k)
            tile = panel_ref[pl.ds(pl.multiple_of(col * edge, edge), edge), :]
            prod = jnp.dot(dense, tile, preferred_element_type=jnp.float32)
            start = pl.multiple_of(row * edge, edge)
            totals_ref[pl.ds(start, edge), :] += prod[:, :half] + prod[:, half:]
            return carry

        lax.fori_loop(0, group, body, 0, unroll=UNROLL)


def backward_kernel(live_ref, rows_ref, cols_ref, masks_ref, lifted_ref, out_ref):
    group, _, edge = masks_ref.shape
    row_limit = lifted_ref.shape[1] // edge - 1
    col_limit = out_ref.shape[1] // edge - 1
    half = out_ref.shape[0]

    @pl.when(pl.program_id(0) == 0)
    def _():
        out_ref[...] = jnp.zeros_like(out_ref)

    base, active = live_chunk(live_ref, group)

    @pl.when(active)
    def _():
        def body(k, carry):
            slot = base + k
            row = jnp.clip(rows_ref[slot], 0, row_limit)
            col = jnp.clip(cols_ref[slot], 0, col_limit)
            dense = slot_words(masks_ref, live_ref, base, k)
            tile = lifted_ref[:, pl.ds(pl.multiple_of(row * edge, edge), edge)]
            prod = jnp.dot(tile, dense, preferred_element_type=jnp.float32)
            start = pl.multiple_of(col * edge, edge)
            out_ref[:, pl.ds(start, edge)] += prod[:half] + prod[half:]
            return carry

        lax.fori_loop(0, group, body, 0, unroll=UNROLL)


def mask_spec(packed_masks, group):
    word_rows, edge = packed_masks.shape[1:]

    def index_map(chunk, live_ref, rows_ref, cols_ref):
        last = jnp.maximum(live_ref[0] - 1, 0) // group
        return (jnp.minimum(chunk, last), 0, 0)

    return pl.BlockSpec((group, word_rows, edge), index_map)


def whole_spec(shape):
    return pl.BlockSpec(shape, lambda chunk, live_ref, rows_ref, cols_ref: (0,) * len(shape))


def slot_pallas(kernel, live, block_rows, block_cols, packed_masks, dense_input, out_shape):
    slot_total = packed_masks.shape[0]
    group = min(SLOT_GROUP, slot_total)
    grid_spec = pltpu.PrefetchScalarGridSpec(
        num_scalar_prefetch=3,
        grid=(slot_total // group,),
        in_specs=[mask_spec(packed_masks, group), whole_spec(dense_input.shape)],
        out_specs=whole_spec(out_shape),
    )
    return pl.pallas_call(
        kernel,
        grid_spec=grid_spec,
        out_shape=jax.ShapeDtypeStruct(out_shape, jnp.float32),
        compiler_params=pltpu.CompilerParams(dimension_semantics=("arbitrary",)),
    )(live, block_rows, block_cols, packed_masks, dense_input)


def block_row_counts(live, block_rows, packed_masks, row_blocks):
    slot_total, word_rows, edge = packed_masks.shape
    shifts = jnp.arange(8, dtype=jnp.int32)
    bits = jnp.bitwise_and(jnp.right_shift(packed_masks[:, :, None, :], shifts[:, None]), 1)
    slot_counts = jnp.sum(bits, axis=-1).reshape(slot_total, word_rows * 8).astype(jnp.float32)
    live_slots = jnp.arange(slot_total, dtype=jnp.int32) < live[0]
    selector = jnp.logical_and(
        block_rows[:, None] == jnp.arange(row_blocks, dtype=jnp.int32)[None, :], live_slots[:, None]
    ).astype(jnp.float32)
    counts = jnp.einsum("sb,sr->br", selector, slot_counts, precision=HIGHEST)
    return counts.reshape(-1)


def block_aggregate(live, block_rows, block_cols, packed_masks, panel_split, row_blocks):
    edge = packed_masks.shape[-1]
    totals_shape = (row_blocks * edge, panel_split.shape[1] // 2)
    totals = slot_pallas(
        forward_kernel, live, block_rows, block_cols, packed_masks, panel_split, totals_shape
    )
    return totals, block_row_counts(live, block_rows, packed_masks, row_blocks)


def block_transpose(live, block_rows, block_cols, packed_masks, lifted_rows, col_blocks):
    edge = packed_masks.shape[-1]
    lifted_t = lifted_rows.T
    high = lax.reduce_precision(lifted_t, exponent_bits=8, mantissa_bits=7)
    split_t = jnp.concatenate([high, lifted_t - high], axis=0).astype(jnp.bfloat16)
    out_shape = (lifted_rows.shape[1], col_blocks * edge)
    out_t = slot_pallas(
        backward_kernel, live, block_rows, block_cols, packed_masks, split_t, out_shape
    )
    return out_t.T


def axis_bits(axis):
    count = lax.axis_size(axis)
    bits = count.bit_length() - 1
    assert count == 1 << bits
    return bits


def exchange(values, axis, bit):
    count = lax.axis_size(axis)
    return lax.ppermute(values, axis, [(i, i ^ (1 << bit)) for i in range(count)])


def axis_bit(axis, bit):
    return (lax.axis_index(axis) >> bit) & 1


def gather_axis(values, axis, dim):
    if lax.axis_size(axis) != 2:
        return lax.all_gather(values, axis, axis=dim, tiled=True)
    other = exchange(values, axis, 0)
    first = lax.axis_index(axis) == 0
    return jnp.concatenate(
        [jnp.where(first, values, other), jnp.where(first, other, values)], axis=dim
    )


def halving_scatter(values, axis):
    bits = axis_bits(axis)
    chunk = values.shape[0] >> bits
    data = values.reshape((2,) * bits + (chunk,) + values.shape[1:])
    for bit in range(bits):
        position = bits - 1 - bit
        mine = axis_bit(axis, bit)
        keep = lax.dynamic_index_in_dim(data, mine, position, keepdims=False)
        send = lax.dynamic_index_in_dim(data, 1 - mine, position, keepdims=False)
        data = keep + exchange(send, axis, bit)
    return data


def doubling_gather(values, axis):
    bits = axis_bits(axis)
    data = values
    for stacked, bit in enumerate(reversed(range(bits))):
        other = exchange(data, axis, bit)
        first = axis_bit(axis, bit) == 0
        data = jnp.where(
            first, jnp.stack([data, other], axis=stacked), jnp.stack([other, data], axis=stacked)
        )
    return data.reshape((-1,) + values.shape[1:])


def butterfly_sum(values, axes):
    for axis in axes:
        for bit in range(axis_bits(axis)):
            values = values + exchange(values, axis, bit)
    return values


def scatter_totals_and_counts(row_totals, row_counts, test_count):
    width = row_totals.shape[1]
    chunk_rows = row_totals.shape[0] // test_count
    count_rows = chunk_rows // width
    padded = -(-count_rows // 8) * 8
    pieces = [
        row_totals.reshape(test_count, chunk_rows, width),
        row_counts.reshape(test_count, count_rows, width),
    ]
    if padded > count_rows:
        pieces.append(jnp.zeros((test_count, padded - count_rows, width), jnp.float32))
    combined = jnp.concatenate(pieces, axis=1).reshape(-1, width)
    own = halving_scatter(combined, "test")
    return own[:chunk_rows], own[chunk_rows : chunk_rows + count_rows].reshape(-1)


def local(x_test, x_cand, w_self, w_neigh, d_out, block_row, block_col, block_mask, block_live):
    packed_masks = block_mask.reshape(block_mask.shape[2:])
    block_rows = block_row.reshape(-1)
    block_cols = block_col.reshape(-1)
    live = jnp.clip(block_live.reshape(1), 0, packed_masks.shape[0])
    block_edge = packed_masks.shape[-1]
    cand_count = lax.axis_size("cand")
    test_count = lax.axis_size("test")
    feat_index = lax.axis_index("feat")
    half_width = x_cand.shape[1]
    row_blocks = x_cand.shape[0] * test_count // block_edge
    col_blocks = x_test.shape[0] * cand_count // block_edge
    panel = doubling_gather(x_test, "cand")
    cand_full = gather_axis(x_cand, "feat", 1)
    row_totals, row_counts = block_aggregate(
        live, block_rows, block_cols, packed_masks, split_hi_lo(panel), row_blocks
    )
    own_totals, degree = scatter_totals_and_counts(row_totals, row_counts, test_count)
    aggregated = own_totals / (1.0 + degree)[:, None]
    self_cols = lax.dynamic_slice_in_dim(w_self, feat_index * half_width, half_width, 1)
    neigh_cols = lax.dynamic_slice_in_dim(w_neigh, feat_index * half_width, half_width, 1)
    self_rows = lax.dynamic_slice_in_dim(w_self, feat_index * half_width, half_width, 0)
    neigh_rows = lax.dynamic_slice_in_dim(w_neigh, feat_index * half_width, half_width, 0)
    aggregated_full = gather_axis(aggregated, "feat", 1)
    pre_act = jnp.dot(cand_full, self_cols, precision=HIGHEST) + jnp.dot(
        aggregated_full, neigh_cols, precision=HIGHEST
    )
    output = jax.nn.silu(pre_act)
    sigmoid_z = jax.nn.sigmoid(pre_act)
    grad_pre = d_out * (sigmoid_z * (1.0 + pre_act * (1.0 - sigmoid_z)))
    grad_full = gather_axis(grad_pre, "feat", 1)
    self_part = jnp.einsum("rk,rh->kh", x_cand, grad_full, precision=HIGHEST)
    neigh_part = jnp.einsum("rk,rh->kh", aggregated, grad_full, precision=HIGHEST)
    self_sum, neigh_sum = butterfly_sum(jnp.stack([self_part, neigh_part]), ("cand", "test"))
    root_count = math.sqrt(x_cand.shape[0] * cand_count * test_count)
    grad_w_self = self_sum / root_count
    grad_w_neigh = neigh_sum / root_count
    grad_x_cand = jnp.dot(grad_full, self_rows.T, precision=HIGHEST)
    grad_agg = jnp.dot(grad_full, neigh_rows.T, precision=HIGHEST)
    lifted = grad_agg / (1.0 + degree)[:, None]
    gathered_rows = doubling_gather(lifted, "test")
    column_terms = block_transpose(
        live, block_rows, block_cols, packed_masks, gathered_rows, col_blocks
    )
    grad_x_test = halving_scatter(column_terms, "cand")
    return (output, grad_w_self, grad_w_neigh, grad_x_cand, grad_x_test)


def solution(mesh):
    return jax.shard_map(
        local,
        mesh=mesh,
        in_specs=(
            P(("test", "cand"), "feat"),
            P(("cand", "test"), "feat"),
            P(),
            P(),
            P(("cand", "test"), "feat"),
            P("cand", "test", None),
            P("cand", "test", None),
            P("cand", "test", None, None, None),
            P("cand", "test"),
        ),
        out_specs=(
            P(("cand", "test"), "feat"),
            P("feat", None),
            P("feat", None),
            P(("cand", "test"), "feat"),
            P(("test", "cand"), "feat"),
        ),
        check_vma=False,
    )
```

```python
import math

import jax
import jax.numpy as jnp
from jax import lax
from jax.experimental import pallas as pl
from jax.experimental.pallas import tpu as pltpu
from jax.sharding import PartitionSpec as P

HIGHEST = lax.Precision.HIGHEST
SLOT_GROUP = 64


def split_hi_lo(values):
    high = lax.reduce_precision(values, exponent_bits=8, mantissa_bits=7)
    low = values - high
    return jnp.concatenate([high, low], axis=1).astype(jnp.bfloat16)


def unpack_bits(words):
    word_rows, edge = words.shape
    cube = jnp.broadcast_to(words[:, None, :], (word_rows, 8, edge))
    shifts = lax.broadcasted_iota(jnp.int32, (word_rows, 8, edge), 1)
    bits = jnp.bitwise_and(jnp.right_shift(cube, shifts), 1)
    return bits.reshape(word_rows * 8, edge)


def unpack_block(words):
    return unpack_bits(words).astype(jnp.float32)


UNROLL = 8


def live_chunk(live_ref, group):
    base = pl.program_id(0) * group
    return base, base < live_ref[0]


def slot_words(masks_ref, live_ref, base, k):
    keep = jnp.where(base + k < live_ref[0], -1, 0).astype(jnp.int32)
    return unpack_block(jnp.bitwise_and(masks_ref[k], keep)).astype(jnp.bfloat16)


def forward_kernel(live_ref, rows_ref, cols_ref, masks_ref, panel_ref, totals_ref, bits_ref):
    group, _, edge = masks_ref.shape
    row_limit = totals_ref.shape[0] // edge - 1
    col_limit = panel_ref.shape[0] // edge - 1
    half = totals_ref.shape[1]

    @pl.when(pl.program_id(0) == 0)
    def _():
        totals_ref[...] = jnp.zeros_like(totals_ref)
        bits_ref[...] = jnp.zeros_like(bits_ref)

    base, active = live_chunk(live_ref, group)

    @pl.when(active)
    def _():
        def body(k, carry):
            slot = base + k
            row = jnp.clip(rows_ref[slot], 0, row_limit)
            col = jnp.clip(cols_ref[slot], 0, col_limit)
            keep = jnp.where(slot < live_ref[0], -1, 0).astype(jnp.int32)
            bits = unpack_bits(jnp.bitwise_and(masks_ref[k], keep))
            bits_ref[row] += bits
            dense = bits.astype(jnp.float32).astype(jnp.bfloat16)
            tile = panel_ref[pl.ds(pl.multiple_of(col * edge, edge), edge), :]
            prod = jnp.dot(dense, tile, preferred_element_type=jnp.float32)
            start = pl.multiple_of(row * edge, edge)
            totals_ref[pl.ds(start, edge), :] += prod[:, :half] + prod[:, half:]
            return carry

        lax.fori_loop(0, group, body, 0, unroll=UNROLL)


def backward_kernel(live_ref, rows_ref, cols_ref, masks_ref, lifted_ref, out_ref):
    group, _, edge = masks_ref.shape
    row_limit = lifted_ref.shape[1] // edge - 1
    col_limit = out_ref.shape[1] // edge - 1
    half = out_ref.shape[0]

    @pl.when(pl.program_id(0) == 0)
    def _():
        out_ref[...] = jnp.zeros_like(out_ref)

    base, active = live_chunk(live_ref, group)

    @pl.when(active)
    def _():
        def body(k, carry):
            slot = base + k
            row = jnp.clip(rows_ref[slot], 0, row_limit)
            col = jnp.clip(cols_ref[slot], 0, col_limit)
            dense = slot_words(masks_ref, live_ref, base, k)
            tile = lifted_ref[:, pl.ds(pl.multiple_of(row * edge, edge), edge)]
            prod = jnp.dot(tile, dense, preferred_element_type=jnp.float32)
            start = pl.multiple_of(col * edge, edge)
            out_ref[:, pl.ds(start, edge)] += prod[:half] + prod[half:]
            return carry

        lax.fori_loop(0, group, body, 0, unroll=UNROLL)


def mask_spec(packed_masks, group):
    word_rows, edge = packed_masks.shape[1:]

    def index_map(chunk, live_ref, rows_ref, cols_ref):
        last = jnp.maximum(live_ref[0] - 1, 0) // group
        return (jnp.minimum(chunk, last), 0, 0)

    return pl.BlockSpec((group, word_rows, edge), index_map)


def whole_spec(shape):
    return pl.BlockSpec(shape, lambda chunk, live_ref, rows_ref, cols_ref: (0,) * len(shape))


def slot_pallas(kernel, live, block_rows, block_cols, packed_masks, dense_input, out_shapes):
    slot_total = packed_masks.shape[0]
    group = min(SLOT_GROUP, slot_total)
    grid_spec = pltpu.PrefetchScalarGridSpec(
        num_scalar_prefetch=3,
        grid=(slot_total // group,),
        in_specs=[mask_spec(packed_masks, group), whole_spec(dense_input.shape)],
        out_specs=[whole_spec(shape.shape) for shape in out_shapes],
    )
    return pl.pallas_call(
        kernel,
        grid_spec=grid_spec,
        out_shape=out_shapes,
        compiler_params=pltpu.CompilerParams(dimension_semantics=("arbitrary",)),
    )(live, block_rows, block_cols, packed_masks, dense_input)


def block_aggregate(live, block_rows, block_cols, packed_masks, panel_split, row_blocks):
    edge = packed_masks.shape[-1]
    totals_shape = jax.ShapeDtypeStruct((row_blocks * edge, panel_split.shape[1] // 2), jnp.float32)
    bits_shape = jax.ShapeDtypeStruct((row_blocks, edge, edge), jnp.int32)
    totals, bit_sums = slot_pallas(
        forward_kernel, live, block_rows, block_cols, packed_masks, panel_split,
        [totals_shape, bits_shape],
    )
    return totals, jnp.sum(bit_sums, axis=-1).astype(jnp.float32).reshape(-1)


def block_transpose(live, block_rows, block_cols, packed_masks, lifted_rows, col_blocks):
    edge = packed_masks.shape[-1]
    lifted_t = lifted_rows.T
    high = lax.reduce_precision(lifted_t, exponent_bits=8, mantissa_bits=7)
    split_t = jnp.concatenate([high, lifted_t - high], axis=0).astype(jnp.bfloat16)
    out_shape = jax.ShapeDtypeStruct((lifted_rows.shape[1], col_blocks * edge), jnp.float32)
    (out_t,) = slot_pallas(
        backward_kernel, live, block_rows, block_cols, packed_masks, split_t, [out_shape]
    )
    return out_t.T


def axis_bits(axis):
    count = lax.axis_size(axis)
    bits = count.bit_length() - 1
    assert count == 1 << bits
    return bits


def exchange(values, axis, bit):
    count = lax.axis_size(axis)
    return lax.ppermute(values, axis, [(i, i ^ (1 << bit)) for i in range(count)])


def axis_bit(axis, bit):
    return (lax.axis_index(axis) >> bit) & 1


def gather_axis(values, axis, dim):
    if lax.axis_size(axis) != 2:
        return lax.all_gather(values, axis, axis=dim, tiled=True)
    other = exchange(values, axis, 0)
    first = lax.axis_index(axis) == 0
    return jnp.concatenate(
        [jnp.where(first, values, other), jnp.where(first, other, values)], axis=dim
    )


def halving_scatter(values, axis):
    bits = axis_bits(axis)
    chunk = values.shape[0] >> bits
    data = values.reshape((2,) * bits + (chunk,) + values.shape[1:])
    for bit in range(bits):
        position = bits - 1 - bit
        mine = axis_bit(axis, bit)
        keep = lax.dynamic_index_in_dim(data, mine, position, keepdims=False)
        send = lax.dynamic_index_in_dim(data, 1 - mine, position, keepdims=False)
        data = keep + exchange(send, axis, bit)
    return data


def doubling_gather(values, axis):
    bits = axis_bits(axis)
    data = values
    for stacked, bit in enumerate(reversed(range(bits))):
        other = exchange(data, axis, bit)
        first = axis_bit(axis, bit) == 0
        data = jnp.where(
            first, jnp.stack([data, other], axis=stacked), jnp.stack([other, data], axis=stacked)
        )
    return data.reshape((-1,) + values.shape[1:])


def butterfly_sum(values, axes):
    for axis in axes:
        for bit in range(axis_bits(axis)):
            values = values + exchange(values, axis, bit)
    return values


def scatter_totals_and_counts(row_totals, row_counts, test_count):
    width = row_totals.shape[1]
    chunk_rows = row_totals.shape[0] // test_count
    count_rows = chunk_rows // width
    padded = -(-count_rows // 8) * 8
    pieces = [
        row_totals.reshape(test_count, chunk_rows, width),
        row_counts.reshape(test_count, count_rows, width),
    ]
    if padded > count_rows:
        pieces.append(jnp.zeros((test_count, padded - count_rows, width), jnp.float32))
    combined = jnp.concatenate(pieces, axis=1).reshape(-1, width)
    own = halving_scatter(combined, "test")
    return own[:chunk_rows], own[chunk_rows : chunk_rows + count_rows].reshape(-1)


def local(x_test, x_cand, w_self, w_neigh, d_out, block_row, block_col, block_mask, block_live):
    packed_masks = block_mask.reshape(block_mask.shape[2:])
    block_rows = block_row.reshape(-1)
    block_cols = block_col.reshape(-1)
    live = jnp.clip(block_live.reshape(1), 0, packed_masks.shape[0])
    block_edge = packed_masks.shape[-1]
    cand_count = lax.axis_size("cand")
    test_count = lax.axis_size("test")
    feat_index = lax.axis_index("feat")
    half_width = x_cand.shape[1]
    row_blocks = x_cand.shape[0] * test_count // block_edge
    col_blocks = x_test.shape[0] * cand_count // block_edge
    panel = doubling_gather(x_test, "cand")
    cand_full = gather_axis(x_cand, "feat", 1)
    row_totals, row_counts = block_aggregate(
        live, block_rows, block_cols, packed_masks, split_hi_lo(panel), row_blocks
    )
    own_totals, degree = scatter_totals_and_counts(row_totals, row_counts, test_count)
    aggregated = own_totals / (1.0 + degree)[:, None]
    self_cols = lax.dynamic_slice_in_dim(w_self, feat_index * half_width, half_width, 1)
    neigh_cols = lax.dynamic_slice_in_dim(w_neigh, feat_index * half_width, half_width, 1)
    self_rows = lax.dynamic_slice_in_dim(w_self, feat_index * half_width, half_width, 0)
    neigh_rows = lax.dynamic_slice_in_dim(w_neigh, feat_index * half_width, half_width, 0)
    aggregated_full = gather_axis(aggregated, "feat", 1)
    pre_act = jnp.dot(cand_full, self_cols, precision=HIGHEST) + jnp.dot(
        aggregated_full, neigh_cols, precision=HIGHEST
    )
    output = jax.nn.silu(pre_act)
    sigmoid_z = jax.nn.sigmoid(pre_act)
    grad_pre = d_out * (sigmoid_z * (1.0 + pre_act * (1.0 - sigmoid_z)))
    grad_full = gather_axis(grad_pre, "feat", 1)
    self_part = jnp.einsum("rk,rh->kh", x_cand, grad_full, precision=HIGHEST)
    neigh_part = jnp.einsum("rk,rh->kh", aggregated, grad_full, precision=HIGHEST)
    self_sum, neigh_sum = butterfly_sum(jnp.stack([self_part, neigh_part]), ("cand", "test"))
    root_count = math.sqrt(x_cand.shape[0] * cand_count * test_count)
    grad_w_self = self_sum / root_count
    grad_w_neigh = neigh_sum / root_count
    grad_x_cand = jnp.dot(grad_full, self_rows.T, precision=HIGHEST)
    grad_agg = jnp.dot(grad_full, neigh_rows.T, precision=HIGHEST)
    lifted = grad_agg / (1.0 + degree)[:, None]
    gathered_rows = doubling_gather(lifted, "test")
    column_terms = block_transpose(
        live, block_rows, block_cols, packed_masks, gathered_rows, col_blocks
    )
    grad_x_test = halving_scatter(column_terms, "cand")
    return (output, grad_w_self, grad_w_neigh, grad_x_cand, grad_x_test)


def solution(mesh):
    return jax.shard_map(
        local,
        mesh=mesh,
        in_specs=(
            P(("test", "cand"), "feat"),
            P(("cand", "test"), "feat"),
            P(),
            P(),
            P(("cand", "test"), "feat"),
            P("cand", "test", None),
            P("cand", "test", None),
            P("cand", "test", None, None, None),
            P("cand", "test"),
        ),
        out_specs=(
            P(("cand", "test"), "feat"),
            P("feat", None),
            P("feat", None),
            P(("cand", "test"), "feat"),
            P(("test", "cand"), "feat"),
        ),
        check_vma=False,
    )
```

```python
import math

import jax
import jax.numpy as jnp
from jax import lax
from jax.experimental import pallas as pl
from jax.experimental.pallas import tpu as pltpu
from jax.sharding import PartitionSpec as P

HIGHEST = lax.Precision.HIGHEST
SLOT_GROUP = 64


def split_hi_lo(values):
    high = lax.reduce_precision(values, exponent_bits=8, mantissa_bits=7)
    low = values - high
    return jnp.concatenate([high, low], axis=1).astype(jnp.bfloat16)


def unpack_bits(words):
    word_rows, edge = words.shape
    cube = jnp.broadcast_to(words[:, None, :], (word_rows, 8, edge))
    shifts = lax.broadcasted_iota(jnp.int32, (word_rows, 8, edge), 1)
    bits = jnp.bitwise_and(jnp.right_shift(cube, shifts), 1)
    return bits.reshape(word_rows * 8, edge)


def unpack_block(words):
    return unpack_bits(words).astype(jnp.float32)


UNROLL = 8


def live_chunk(live_ref, group):
    base = pl.program_id(0) * group
    return base, base < live_ref[0]


def slot_words(masks_ref, live_ref, base, k):
    keep = jnp.where(base + k < live_ref[0], -1, 0).astype(jnp.int32)
    return unpack_block(jnp.bitwise_and(masks_ref[k], keep)).astype(jnp.bfloat16)


def forward_kernel(live_ref, rows_ref, cols_ref, masks_ref, panel_ref, totals_ref, bits_ref):
    group, _, edge = masks_ref.shape
    row_limit = totals_ref.shape[0] // edge - 1
    col_limit = panel_ref.shape[0] // edge - 1
    half = totals_ref.shape[1]

    @pl.when(pl.program_id(0) == 0)
    def _():
        totals_ref[...] = jnp.zeros_like(totals_ref)
        bits_ref[...] = jnp.zeros_like(bits_ref)

    base, active = live_chunk(live_ref, group)

    @pl.when(active)
    def _():
        def body(k, carry):
            slot = base + k
            row = jnp.clip(rows_ref[slot], 0, row_limit)
            col = jnp.clip(cols_ref[slot], 0, col_limit)
            keep = jnp.where(slot < live_ref[0], -1, 0).astype(jnp.int32)
            bits = unpack_bits(jnp.bitwise_and(masks_ref[k], keep))
            bits_ref[row] += bits
            dense = bits.astype(jnp.float32).astype(jnp.bfloat16)
            tile = panel_ref[pl.ds(pl.multiple_of(col * edge, edge), edge), :]
            prod = jnp.dot(dense, tile, preferred_element_type=jnp.float32)
            start = pl.multiple_of(row * edge, edge)
            totals_ref[pl.ds(start, edge), :] += prod[:, :half] + prod[:, half:]
            return carry

        lax.fori_loop(0, group, body, 0, unroll=UNROLL)


def backward_kernel(live_ref, rows_ref, cols_ref, masks_ref, lifted_ref, out_ref):
    group, _, edge = masks_ref.shape
    row_limit = lifted_ref.shape[1] // edge - 1
    col_limit = out_ref.shape[1] // edge - 1
    half = out_ref.shape[0]

    @pl.when(pl.program_id(0) == 0)
    def _():
        out_ref[...] = jnp.zeros_like(out_ref)

    base, active = live_chunk(live_ref, group)

    @pl.when(active)
    def _():
        def body(k, carry):
            slot = base + k
            row = jnp.clip(rows_ref[slot], 0, row_limit)
            col = jnp.clip(cols_ref[slot], 0, col_limit)
            dense = slot_words(masks_ref, live_ref, base, k)
            tile = lifted_ref[:, pl.ds(pl.multiple_of(row * edge, edge), edge)]
            prod = jnp.dot(tile, dense, preferred_element_type=jnp.float32)
            start = pl.multiple_of(col * edge, edge)
            out_ref[:, pl.ds(start, edge)] += prod[:half] + prod[half:]
            return carry

        lax.fori_loop(0, group, body, 0, unroll=UNROLL)


def mask_spec(packed_masks, group):
    word_rows, edge = packed_masks.shape[1:]

    def index_map(chunk, live_ref, rows_ref, cols_ref):
        last = jnp.maximum(live_ref[0] - 1, 0) // group
        return (jnp.minimum(chunk, last), 0, 0)

    return pl.BlockSpec((group, word_rows, edge), index_map)


def whole_spec(shape):
    return pl.BlockSpec(shape, lambda chunk, live_ref, rows_ref, cols_ref: (0,) * len(shape))


def slot_pallas(kernel, live, block_rows, block_cols, packed_masks, dense_input, out_shapes):
    slot_total = packed_masks.shape[0]
    group = min(SLOT_GROUP, slot_total)
    grid_spec = pltpu.PrefetchScalarGridSpec(
        num_scalar_prefetch=3,
        grid=(slot_total // group,),
        in_specs=[mask_spec(packed_masks, group), whole_spec(dense_input.shape)],
        out_specs=[whole_spec(shape.shape) for shape in out_shapes],
    )
    return pl.pallas_call(
        kernel,
        grid_spec=grid_spec,
        out_shape=out_shapes,
        compiler_params=pltpu.CompilerParams(dimension_semantics=("arbitrary",)),
    )(live, block_rows, block_cols, packed_masks, dense_input)


def block_aggregate(live, block_rows, block_cols, packed_masks, panel_split, row_blocks):
    edge = packed_masks.shape[-1]
    totals_shape = jax.ShapeDtypeStruct((row_blocks * edge, panel_split.shape[1] // 2), jnp.float32)
    bits_shape = jax.ShapeDtypeStruct((row_blocks, edge, edge), jnp.int32)
    totals, bit_sums = slot_pallas(
        forward_kernel, live, block_rows, block_cols, packed_masks, panel_split,
        [totals_shape, bits_shape],
    )
    return totals, jnp.sum(bit_sums, axis=-1).astype(jnp.float32).reshape(-1)


def block_transpose(live, block_rows, block_cols, packed_masks, lifted_rows, col_blocks):
    edge = packed_masks.shape[-1]
    lifted_t = lifted_rows.T
    high = lax.reduce_precision(lifted_t, exponent_bits=8, mantissa_bits=7)
    split_t = jnp.concatenate([high, lifted_t - high], axis=0).astype(jnp.bfloat16)
    out_shape = jax.ShapeDtypeStruct((lifted_rows.shape[1], col_blocks * edge), jnp.float32)
    (out_t,) = slot_pallas(
        backward_kernel, live, block_rows, block_cols, packed_masks, split_t, [out_shape]
    )
    return out_t.T


def axis_bits(axis):
    count = lax.axis_size(axis)
    bits = count.bit_length() - 1
    assert count == 1 << bits
    return bits


def exchange(values, axis, bit):
    count = lax.axis_size(axis)
    return lax.ppermute(values, axis, [(i, i ^ (1 << bit)) for i in range(count)])


def axis_bit(axis, bit):
    return (lax.axis_index(axis) >> bit) & 1


def gather_axis(values, axis, dim):
    if lax.axis_size(axis) != 2:
        return lax.all_gather(values, axis, axis=dim, tiled=True)
    other = exchange(values, axis, 0)
    first = lax.axis_index(axis) == 0
    return jnp.concatenate(
        [jnp.where(first, values, other), jnp.where(first, other, values)], axis=dim
    )


def halving_steps(values, axis, order):
    bits = axis_bits(axis)
    chunk = values.shape[0] >> bits
    data = values.reshape((2,) * bits + (chunk,) + values.shape[1:])
    remaining = list(reversed(range(bits)))
    for bit in order:
        position = remaining.index(bit)
        remaining.remove(bit)
        mine = axis_bit(axis, bit)
        keep = lax.dynamic_index_in_dim(data, mine, position, keepdims=False)
        send = lax.dynamic_index_in_dim(data, 1 - mine, position, keepdims=False)
        data = keep + exchange(send, axis, bit)
    return data


def doubling_steps(values, axis, order):
    data = values
    present = []
    for bit in order:
        position = sum(1 for other in present if other > bit)
        present.insert(position, bit)
        other = exchange(data, axis, bit)
        first = axis_bit(axis, bit) == 0
        data = jnp.where(
            first, jnp.stack([data, other], axis=position), jnp.stack([other, data], axis=position)
        )
    return data


def bit_orders(axis):
    bits = axis_bits(axis)
    ascending = list(range(bits))
    if bits < 2:
        return [ascending]
    return [ascending, [1, 0] + ascending[2:]]


def halving_scatter(values, axis):
    orders = bit_orders(axis)
    bits = axis_bits(axis)
    shaped = values.reshape((1 << bits, -1) + values.shape[1:])
    pieces = jnp.split(shaped, len(orders), axis=1)
    results = [
        halving_steps(piece.reshape((-1,) + values.shape[1:]), axis, order)
        for piece, order in zip(pieces, orders)
    ]
    return jnp.concatenate(results, axis=0)


def doubling_gather(values, axis):
    orders = [list(reversed(order)) for order in bit_orders(axis)]
    pieces = jnp.split(values, len(orders), axis=0)
    results = [doubling_steps(piece, axis, order) for piece, order in zip(pieces, orders)]
    stacked = jnp.concatenate(
        [result.reshape((-1,) + result.shape[-2:]) for result in results], axis=1
    )
    return stacked.reshape((-1,) + values.shape[1:])


def butterfly_sum(values, axes):
    for axis in axes:
        for bit in range(axis_bits(axis)):
            values = values + exchange(values, axis, bit)
    return values


def scatter_totals_and_counts(row_totals, row_counts, test_count):
    width = row_totals.shape[1]
    chunk_rows = row_totals.shape[0] // test_count
    count_rows = chunk_rows // width
    padded = -(-count_rows // 16) * 16
    pieces = [
        row_totals.reshape(test_count, chunk_rows, width),
        row_counts.reshape(test_count, count_rows, width),
    ]
    if padded > count_rows:
        pieces.append(jnp.zeros((test_count, padded - count_rows, width), jnp.float32))
    combined = jnp.concatenate(pieces, axis=1).reshape(-1, width)
    own = halving_scatter(combined, "test")
    return own[:chunk_rows], own[chunk_rows : chunk_rows + count_rows].reshape(-1)


def local(x_test, x_cand, w_self, w_neigh, d_out, block_row, block_col, block_mask, block_live):
    packed_masks = block_mask.reshape(block_mask.shape[2:])
    block_rows = block_row.reshape(-1)
    block_cols = block_col.reshape(-1)
    live = jnp.clip(block_live.reshape(1), 0, packed_masks.shape[0])
    block_edge = packed_masks.shape[-1]
    cand_count = lax.axis_size("cand")
    test_count = lax.axis_size("test")
    feat_index = lax.axis_index("feat")
    half_width = x_cand.shape[1]
    row_blocks = x_cand.shape[0] * test_count // block_edge
    col_blocks = x_test.shape[0] * cand_count // block_edge
    panel = doubling_gather(x_test, "cand")
    cand_full = gather_axis(x_cand, "feat", 1)
    row_totals, row_counts = block_aggregate(
        live, block_rows, block_cols, packed_masks, split_hi_lo(panel), row_blocks
    )
    own_totals, degree = scatter_totals_and_counts(row_totals, row_counts, test_count)
    aggregated = own_totals / (1.0 + degree)[:, None]
    self_cols = lax.dynamic_slice_in_dim(w_self, feat_index * half_width, half_width, 1)
    neigh_cols = lax.dynamic_slice_in_dim(w_neigh, feat_index * half_width, half_width, 1)
    self_rows = lax.dynamic_slice_in_dim(w_self, feat_index * half_width, half_width, 0)
    neigh_rows = lax.dynamic_slice_in_dim(w_neigh, feat_index * half_width, half_width, 0)
    aggregated_full = gather_axis(aggregated, "feat", 1)
    pre_act = jnp.dot(cand_full, self_cols, precision=HIGHEST) + jnp.dot(
        aggregated_full, neigh_cols, precision=HIGHEST
    )
    output = jax.nn.silu(pre_act)
    sigmoid_z = jax.nn.sigmoid(pre_act)
    grad_pre = d_out * (sigmoid_z * (1.0 + pre_act * (1.0 - sigmoid_z)))
    grad_full = gather_axis(grad_pre, "feat", 1)
    self_part = jnp.einsum("rk,rh->kh", x_cand, grad_full, precision=HIGHEST)
    neigh_part = jnp.einsum("rk,rh->kh", aggregated, grad_full, precision=HIGHEST)
    self_sum, neigh_sum = butterfly_sum(jnp.stack([self_part, neigh_part]), ("cand", "test"))
    root_count = math.sqrt(x_cand.shape[0] * cand_count * test_count)
    grad_w_self = self_sum / root_count
    grad_w_neigh = neigh_sum / root_count
    grad_x_cand = jnp.dot(grad_full, self_rows.T, precision=HIGHEST)
    grad_agg = jnp.dot(grad_full, neigh_rows.T, precision=HIGHEST)
    lifted = grad_agg / (1.0 + degree)[:, None]
    gathered_rows = doubling_gather(lifted, "test")
    column_terms = block_transpose(
        live, block_rows, block_cols, packed_masks, gathered_rows, col_blocks
    )
    grad_x_test = halving_scatter(column_terms, "cand")
    return (output, grad_w_self, grad_w_neigh, grad_x_cand, grad_x_test)


def solution(mesh):
    return jax.shard_map(
        local,
        mesh=mesh,
        in_specs=(
            P(("test", "cand"), "feat"),
            P(("cand", "test"), "feat"),
            P(),
            P(),
            P(("cand", "test"), "feat"),
            P("cand", "test", None),
            P("cand", "test", None),
            P("cand", "test", None, None, None),
            P("cand", "test"),
        ),
        out_specs=(
            P(("cand", "test"), "feat"),
            P("feat", None),
            P("feat", None),
            P(("cand", "test"), "feat"),
            P(("test", "cand"), "feat"),
        ),
        check_vma=False,
    )
```

```python
import math

import jax
import jax.numpy as jnp
from jax import lax
from jax.experimental import pallas as pl
from jax.experimental.pallas import tpu as pltpu
from jax.sharding import PartitionSpec as P

HIGHEST = lax.Precision.HIGHEST
SLOT_GROUP = 64


def split_hi_lo(values):
    high = lax.reduce_precision(values, exponent_bits=8, mantissa_bits=7)
    low = values - high
    return jnp.concatenate([high, low], axis=1).astype(jnp.bfloat16)


def unpack_bits(words):
    word_rows, edge = words.shape
    cube = jnp.broadcast_to(words[:, None, :], (word_rows, 8, edge))
    shifts = lax.broadcasted_iota(jnp.int32, (word_rows, 8, edge), 1)
    bits = jnp.bitwise_and(jnp.right_shift(cube, shifts), 1)
    return bits.reshape(word_rows * 8, edge)


def unpack_block(words):
    return unpack_bits(words).astype(jnp.float32)


UNROLL = 8


def live_chunk(live_ref, group):
    base = pl.program_id(0) * group
    return base, base < live_ref[0]


def slot_words(masks_ref, live_ref, base, k):
    keep = jnp.where(base + k < live_ref[0], -1, 0).astype(jnp.int32)
    return unpack_block(jnp.bitwise_and(masks_ref[k], keep)).astype(jnp.bfloat16)


def forward_kernel(live_ref, rows_ref, cols_ref, masks_ref, panel_ref, totals_ref, bits_ref):
    group, _, edge = masks_ref.shape
    row_limit = totals_ref.shape[0] // edge - 1
    col_limit = panel_ref.shape[0] // edge - 1
    half = totals_ref.shape[1]

    @pl.when(pl.program_id(0) == 0)
    def _():
        totals_ref[...] = jnp.zeros_like(totals_ref)
        bits_ref[...] = jnp.zeros_like(bits_ref)

    base, active = live_chunk(live_ref, group)

    @pl.when(active)
    def _():
        def body(k, carry):
            slot = base + k
            row = jnp.clip(rows_ref[slot], 0, row_limit)
            col = jnp.clip(cols_ref[slot], 0, col_limit)
            keep = jnp.where(slot < live_ref[0], -1, 0).astype(jnp.int32)
            bits = unpack_bits(jnp.bitwise_and(masks_ref[k], keep))
            bits_ref[row] += bits
            dense = bits.astype(jnp.float32).astype(jnp.bfloat16)
            tile = panel_ref[pl.ds(pl.multiple_of(col * edge, edge), edge), :]
            prod = jnp.dot(dense, tile, preferred_element_type=jnp.float32)
            start = pl.multiple_of(row * edge, edge)
            totals_ref[pl.ds(start, edge), :] += prod[:, :half] + prod[:, half:]
            return carry

        lax.fori_loop(0, group, body, 0, unroll=UNROLL)


def backward_kernel(live_ref, rows_ref, cols_ref, masks_ref, lifted_ref, out_ref):
    group, _, edge = masks_ref.shape
    row_chunk = lifted_ref.shape[2] // edge
    col_chunk = out_ref.shape[2] // edge
    row_limit = lifted_ref.shape[0] * row_chunk - 1
    col_limit = out_ref.shape[0] * col_chunk - 1
    half = out_ref.shape[1]

    @pl.when(pl.program_id(0) == 0)
    def _():
        out_ref[...] = jnp.zeros_like(out_ref)

    base, active = live_chunk(live_ref, group)

    @pl.when(active)
    def _():
        def body(k, carry):
            slot = base + k
            row = jnp.clip(rows_ref[slot], 0, row_limit)
            col = jnp.clip(cols_ref[slot], 0, col_limit)
            dense = slot_words(masks_ref, live_ref, base, k)
            row_start = pl.multiple_of((row % row_chunk) * edge, edge)
            tile = lifted_ref[row // row_chunk, :, pl.ds(row_start, edge)]
            prod = jnp.dot(tile, dense, preferred_element_type=jnp.float32)
            col_start = pl.multiple_of((col % col_chunk) * edge, edge)
            out_ref[col // col_chunk, :, pl.ds(col_start, edge)] += prod[:half] + prod[half:]
            return carry

        lax.fori_loop(0, group, body, 0, unroll=UNROLL)


def mask_spec(packed_masks, group):
    word_rows, edge = packed_masks.shape[1:]

    def index_map(chunk, live_ref, rows_ref, cols_ref):
        last = jnp.maximum(live_ref[0] - 1, 0) // group
        return (jnp.minimum(chunk, last), 0, 0)

    return pl.BlockSpec((group, word_rows, edge), index_map)


def whole_spec(shape):
    return pl.BlockSpec(shape, lambda chunk, live_ref, rows_ref, cols_ref: (0,) * len(shape))


def slot_pallas(kernel, live, block_rows, block_cols, packed_masks, dense_input, out_shapes):
    slot_total = packed_masks.shape[0]
    group = min(SLOT_GROUP, slot_total)
    grid_spec = pltpu.PrefetchScalarGridSpec(
        num_scalar_prefetch=3,
        grid=(slot_total // group,),
        in_specs=[mask_spec(packed_masks, group), whole_spec(dense_input.shape)],
        out_specs=[whole_spec(shape.shape) for shape in out_shapes],
    )
    return pl.pallas_call(
        kernel,
        grid_spec=grid_spec,
        out_shape=out_shapes,
        compiler_params=pltpu.CompilerParams(dimension_semantics=("arbitrary",)),
    )(live, block_rows, block_cols, packed_masks, dense_input)


def block_aggregate(live, block_rows, block_cols, packed_masks, panel_split, row_blocks):
    edge = packed_masks.shape[-1]
    totals_shape = jax.ShapeDtypeStruct((row_blocks * edge, panel_split.shape[1] // 2), jnp.float32)
    bits_shape = jax.ShapeDtypeStruct((row_blocks, edge, edge), jnp.int32)
    totals, bit_sums = slot_pallas(
        forward_kernel, live, block_rows, block_cols, packed_masks, panel_split,
        [totals_shape, bits_shape],
    )
    return totals, jnp.sum(bit_sums, axis=-1).astype(jnp.float32).reshape(-1)


def block_transpose(live, block_rows, block_cols, packed_masks, lifted_chunks, cand_count):
    edge = packed_masks.shape[-1]
    high = lax.reduce_precision(lifted_chunks, exponent_bits=8, mantissa_bits=7)
    split_t = jnp.concatenate([high, lifted_chunks - high], axis=1).astype(jnp.bfloat16)
    width = lifted_chunks.shape[1]
    panel_cols = lifted_chunks.shape[0] * lifted_chunks.shape[2]
    out_shape = jax.ShapeDtypeStruct((cand_count, width, panel_cols // cand_count), jnp.float32)
    (out_t,) = slot_pallas(
        backward_kernel, live, block_rows, block_cols, packed_masks, split_t, [out_shape]
    )
    return out_t


def axis_bits(axis):
    count = lax.axis_size(axis)
    bits = count.bit_length() - 1
    assert count == 1 << bits
    return bits


def exchange(values, axis, bit):
    count = lax.axis_size(axis)
    return lax.ppermute(values, axis, [(i, i ^ (1 << bit)) for i in range(count)])


def axis_bit(axis, bit):
    return (lax.axis_index(axis) >> bit) & 1


def gather_axis(values, axis, dim):
    if lax.axis_size(axis) != 2:
        return lax.all_gather(values, axis, axis=dim, tiled=True)
    other = exchange(values, axis, 0)
    first = lax.axis_index(axis) == 0
    return jnp.concatenate(
        [jnp.where(first, values, other), jnp.where(first, other, values)], axis=dim
    )


def halving_steps(values, axis, order):
    bits = axis_bits(axis)
    chunk = values.shape[0] >> bits
    data = values.reshape((2,) * bits + (chunk,) + values.shape[1:])
    remaining = list(reversed(range(bits)))
    for bit in order:
        position = remaining.index(bit)
        remaining.remove(bit)
        mine = axis_bit(axis, bit)
        keep = lax.dynamic_index_in_dim(data, mine, position, keepdims=False)
        send = lax.dynamic_index_in_dim(data, 1 - mine, position, keepdims=False)
        data = keep + exchange(send, axis, bit)
    return data


def doubling_steps(values, axis, order):
    data = values
    present = []
    for bit in order:
        position = sum(1 for other in present if other > bit)
        present.insert(position, bit)
        other = exchange(data, axis, bit)
        first = axis_bit(axis, bit) == 0
        data = jnp.where(
            first, jnp.stack([data, other], axis=position), jnp.stack([other, data], axis=position)
        )
    return data


def bit_orders(axis):
    bits = axis_bits(axis)
    ascending = list(range(bits))
    if bits < 2:
        return [ascending]
    return [ascending, [1, 0] + ascending[2:]]


def halving_scatter(values, axis):
    orders = bit_orders(axis)
    bits = axis_bits(axis)
    shaped = values.reshape((1 << bits, -1) + values.shape[1:])
    pieces = jnp.split(shaped, len(orders), axis=1)
    results = [
        halving_steps(piece.reshape((-1,) + values.shape[1:]), axis, order)
        for piece, order in zip(pieces, orders)
    ]
    return jnp.concatenate(results, axis=0)


def doubling_gather(values, axis):
    orders = [list(reversed(order)) for order in bit_orders(axis)]
    pieces = jnp.split(values, len(orders), axis=0)
    results = [doubling_steps(piece, axis, order) for piece, order in zip(pieces, orders)]
    stacked = jnp.concatenate(
        [result.reshape((-1,) + result.shape[-2:]) for result in results], axis=1
    )
    return stacked.reshape((-1,) + values.shape[1:])


def doubling_gather_lanes(values, axis):
    orders = [list(reversed(order)) for order in bit_orders(axis)]
    pieces = jnp.split(values, len(orders), axis=1)
    results = [doubling_steps(piece, axis, order) for piece, order in zip(pieces, orders)]
    return jnp.concatenate(
        [result.reshape((-1,) + result.shape[-2:]) for result in results], axis=2
    )


def butterfly_sum(values, axes):
    for axis in axes:
        for bit in range(axis_bits(axis)):
            values = values + exchange(values, axis, bit)
    return values


def scatter_totals_and_counts(row_totals, row_counts, test_count):
    width = row_totals.shape[1]
    chunk_rows = row_totals.shape[0] // test_count
    count_rows = chunk_rows // width
    padded = -(-count_rows // 16) * 16
    pieces = [
        row_totals.reshape(test_count, chunk_rows, width),
        row_counts.reshape(test_count, count_rows, width),
    ]
    if padded > count_rows:
        pieces.append(jnp.zeros((test_count, padded - count_rows, width), jnp.float32))
    combined = jnp.concatenate(pieces, axis=1).reshape(-1, width)
    own = halving_scatter(combined, "test")
    return own[:chunk_rows], own[chunk_rows : chunk_rows + count_rows].reshape(-1)


def local(x_test, x_cand, w_self, w_neigh, d_out, block_row, block_col, block_mask, block_live):
    packed_masks = block_mask.reshape(block_mask.shape[2:])
    block_rows = block_row.reshape(-1)
    block_cols = block_col.reshape(-1)
    live = jnp.clip(block_live.reshape(1), 0, packed_masks.shape[0])
    block_edge = packed_masks.shape[-1]
    cand_count = lax.axis_size("cand")
    test_count = lax.axis_size("test")
    feat_index = lax.axis_index("feat")
    half_width = x_cand.shape[1]
    row_blocks = x_cand.shape[0] * test_count // block_edge
    col_blocks = x_test.shape[0] * cand_count // block_edge
    panel = doubling_gather(x_test, "cand")
    cand_full = gather_axis(x_cand, "feat", 1)
    row_totals, row_counts = block_aggregate(
        live, block_rows, block_cols, packed_masks, split_hi_lo(panel), row_blocks
    )
    own_totals, degree = scatter_totals_and_counts(row_totals, row_counts, test_count)
    aggregated = own_totals / (1.0 + degree)[:, None]
    self_cols = lax.dynamic_slice_in_dim(w_self, feat_index * half_width, half_width, 1)
    neigh_cols = lax.dynamic_slice_in_dim(w_neigh, feat_index * half_width, half_width, 1)
    self_rows = lax.dynamic_slice_in_dim(w_self, feat_index * half_width, half_width, 0)
    neigh_rows = lax.dynamic_slice_in_dim(w_neigh, feat_index * half_width, half_width, 0)
    aggregated_full = gather_axis(aggregated, "feat", 1)
    pre_act = jnp.dot(cand_full, self_cols, precision=HIGHEST) + jnp.dot(
        aggregated_full, neigh_cols, precision=HIGHEST
    )
    output = jax.nn.silu(pre_act)
    sigmoid_z = jax.nn.sigmoid(pre_act)
    grad_pre = d_out * (sigmoid_z * (1.0 + pre_act * (1.0 - sigmoid_z)))
    grad_full = gather_axis(grad_pre, "feat", 1)
    self_part = jnp.einsum("rk,rh->kh", x_cand, grad_full, precision=HIGHEST)
    neigh_part = jnp.einsum("rk,rh->kh", aggregated, grad_full, precision=HIGHEST)
    grad_w_pair = butterfly_sum(jnp.stack([self_part, neigh_part]), ("cand", "test"))
    root_count = math.sqrt(x_cand.shape[0] * cand_count * test_count)
    grad_x_cand = jnp.dot(grad_full, self_rows.T, precision=HIGHEST)
    grad_agg = jnp.dot(grad_full, neigh_rows.T, precision=HIGHEST)
    lifted = grad_agg / (1.0 + degree)[:, None]
    lifted_chunks = doubling_gather_lanes(lifted.T, "test")
    grad_w_pair, lifted_chunks = lax.optimization_barrier((grad_w_pair, lifted_chunks))
    grad_w_self = grad_w_pair[0] / root_count
    grad_w_neigh = grad_w_pair[1] / root_count
    out_t = block_transpose(live, block_rows, block_cols, packed_masks, lifted_chunks, cand_count)
    own_t = halving_scatter(out_t.reshape(-1, out_t.shape[2]), "cand")
    grad_x_test = own_t.T
    return (output, grad_w_self, grad_w_neigh, grad_x_cand, grad_x_test)


def solution(mesh):
    return jax.shard_map(
        local,
        mesh=mesh,
        in_specs=(
            P(("test", "cand"), "feat"),
            P(("cand", "test"), "feat"),
            P(),
            P(),
            P(("cand", "test"), "feat"),
            P("cand", "test", None),
            P("cand", "test", None),
            P("cand", "test", None, None, None),
            P("cand", "test"),
        ),
        out_specs=(
            P(("cand", "test"), "feat"),
            P("feat", None),
            P("feat", None),
            P(("cand", "test"), "feat"),
            P(("test", "cand"), "feat"),
        ),
        check_vma=False,
    )
```

```python
import math

import jax
import jax.numpy as jnp
from jax import lax
from jax.experimental import pallas as pl
from jax.experimental.pallas import tpu as pltpu
from jax.sharding import PartitionSpec as P

HIGHEST = lax.Precision.HIGHEST
SLOT_GROUP = 128


def split_hi_lo(values):
    high = lax.reduce_precision(values, exponent_bits=8, mantissa_bits=7)
    low = values - high
    return jnp.concatenate([high, low], axis=1).astype(jnp.bfloat16)


def unpack_bits(words):
    word_rows, edge = words.shape
    cube = jnp.broadcast_to(words[:, None, :], (word_rows, 8, edge))
    shifts = lax.broadcasted_iota(jnp.int32, (word_rows, 8, edge), 1)
    bits = jnp.bitwise_and(jnp.right_shift(cube, shifts), 1)
    return bits.reshape(word_rows * 8, edge)


def spread_bytes(words):
    low = jnp.zeros_like(words)
    high = jnp.zeros_like(words)
    for bit in range(4):
        low = low + jnp.left_shift(jnp.bitwise_and(jnp.right_shift(words, bit), 1), 8 * bit)
        high = high + jnp.left_shift(jnp.bitwise_and(jnp.right_shift(words, bit + 4), 1), 8 * bit)
    return jnp.concatenate([low, high], axis=0)


def unpack_block(words):
    return unpack_bits(words).astype(jnp.float32)


UNROLL = 8


def live_chunk(live_ref, group):
    base = pl.program_id(0) * group
    return base, base < live_ref[0]


def slot_words(masks_ref, live_ref, base, k):
    keep = jnp.where(base + k < live_ref[0], -1, 0).astype(jnp.int32)
    return unpack_block(jnp.bitwise_and(masks_ref[k], keep)).astype(jnp.bfloat16)


def forward_kernel(live_ref, rows_ref, cols_ref, masks_ref, panel_ref, totals_ref, bits_ref):
    group, _, edge = masks_ref.shape
    row_limit = totals_ref.shape[0] // edge - 1
    col_limit = panel_ref.shape[0] // edge - 1
    half = totals_ref.shape[1]

    @pl.when(pl.program_id(0) == 0)
    def _():
        totals_ref[...] = jnp.zeros_like(totals_ref)
        bits_ref[...] = jnp.zeros_like(bits_ref)

    base, active = live_chunk(live_ref, group)

    @pl.when(active)
    def _():
        def body(k, carry):
            slot = base + k
            row = jnp.clip(rows_ref[slot], 0, row_limit)
            col = jnp.clip(cols_ref[slot], 0, col_limit)
            keep = jnp.where(slot < live_ref[0], -1, 0).astype(jnp.int32)
            words = jnp.bitwise_and(masks_ref[k], keep)
            bits_ref[row] += spread_bytes(words)
            dense = unpack_bits(words).astype(jnp.float32).astype(jnp.bfloat16)
            tile = panel_ref[pl.ds(pl.multiple_of(col * edge, edge), edge), :]
            prod = jnp.dot(dense, tile, preferred_element_type=jnp.float32)
            start = pl.multiple_of(row * edge, edge)
            totals_ref[pl.ds(start, edge), :] += prod[:, :half] + prod[:, half:]
            return carry

        lax.fori_loop(0, group, body, 0, unroll=UNROLL)


def backward_kernel(live_ref, rows_ref, cols_ref, masks_ref, lifted_ref, out_ref):
    group, _, edge = masks_ref.shape
    row_chunk = lifted_ref.shape[2] // edge
    col_chunk = out_ref.shape[2] // edge
    row_limit = lifted_ref.shape[0] * row_chunk - 1
    col_limit = out_ref.shape[0] * col_chunk - 1
    half = out_ref.shape[1]

    @pl.when(pl.program_id(0) == 0)
    def _():
        out_ref[...] = jnp.zeros_like(out_ref)

    base, active = live_chunk(live_ref, group)

    @pl.when(active)
    def _():
        def body(k, carry):
            slot = base + k
            row = jnp.clip(rows_ref[slot], 0, row_limit)
            col = jnp.clip(cols_ref[slot], 0, col_limit)
            dense = slot_words(masks_ref, live_ref, base, k)
            row_start = pl.multiple_of((row % row_chunk) * edge, edge)
            tile = lifted_ref[row // row_chunk, :, pl.ds(row_start, edge)]
            prod = jnp.dot(tile, dense, preferred_element_type=jnp.float32)
            col_start = pl.multiple_of((col % col_chunk) * edge, edge)
            out_ref[col // col_chunk, :, pl.ds(col_start, edge)] += prod[:half] + prod[half:]
            return carry

        lax.fori_loop(0, group, body, 0, unroll=UNROLL)


def mask_spec(packed_masks, group):
    word_rows, edge = packed_masks.shape[1:]

    def index_map(chunk, live_ref, rows_ref, cols_ref):
        last = jnp.maximum(live_ref[0] - 1, 0) // group
        return (jnp.minimum(chunk, last), 0, 0)

    return pl.BlockSpec((group, word_rows, edge), index_map)


def whole_spec(shape):
    return pl.BlockSpec(shape, lambda chunk, live_ref, rows_ref, cols_ref: (0,) * len(shape))


def slot_pallas(kernel, live, block_rows, block_cols, packed_masks, dense_input, out_shapes):
    slot_total = packed_masks.shape[0]
    group = min(SLOT_GROUP, slot_total)
    grid_spec = pltpu.PrefetchScalarGridSpec(
        num_scalar_prefetch=3,
        grid=(slot_total // group,),
        in_specs=[mask_spec(packed_masks, group), whole_spec(dense_input.shape)],
        out_specs=[whole_spec(shape.shape) for shape in out_shapes],
    )
    return pl.pallas_call(
        kernel,
        grid_spec=grid_spec,
        out_shape=out_shapes,
        compiler_params=pltpu.CompilerParams(dimension_semantics=("arbitrary",)),
    )(live, block_rows, block_cols, packed_masks, dense_input)


def block_aggregate(live, block_rows, block_cols, packed_masks, panel_split, row_blocks):
    edge = packed_masks.shape[-1]
    totals_shape = jax.ShapeDtypeStruct((row_blocks * edge, panel_split.shape[1] // 2), jnp.float32)
    word_rows = packed_masks.shape[1]
    bits_shape = jax.ShapeDtypeStruct((row_blocks, 2 * word_rows, edge), jnp.int32)
    totals, byte_sums = slot_pallas(
        forward_kernel, live, block_rows, block_cols, packed_masks, panel_split,
        [totals_shape, bits_shape],
    )
    fields = [
        jnp.sum(jnp.bitwise_and(jnp.right_shift(byte_sums, 8 * field), 255), axis=2)
        for field in range(4)
    ]
    per_row = jnp.stack(fields, axis=-1).reshape(row_blocks, 2, word_rows, 4)
    counts = jnp.transpose(per_row, (0, 2, 1, 3)).reshape(-1).astype(jnp.float32)
    return totals, counts


def block_transpose(live, block_rows, block_cols, packed_masks, lifted_chunks, cand_count):
    edge = packed_masks.shape[-1]
    high = lax.reduce_precision(lifted_chunks, exponent_bits=8, mantissa_bits=7)
    split_t = jnp.concatenate([high, lifted_chunks - high], axis=1).astype(jnp.bfloat16)
    width = lifted_chunks.shape[1]
    panel_cols = lifted_chunks.shape[0] * lifted_chunks.shape[2]
    out_shape = jax.ShapeDtypeStruct((cand_count, width, panel_cols // cand_count), jnp.float32)
    (out_t,) = slot_pallas(
        backward_kernel, live, block_rows, block_cols, packed_masks, split_t, [out_shape]
    )
    return out_t


def axis_bits(axis):
    count = lax.axis_size(axis)
    bits = count.bit_length() - 1
    assert count == 1 << bits
    return bits


def exchange(values, axis, bit):
    count = lax.axis_size(axis)
    return lax.ppermute(values, axis, [(i, i ^ (1 << bit)) for i in range(count)])


def axis_bit(axis, bit):
    return (lax.axis_index(axis) >> bit) & 1


def gather_axis(values, axis, dim):
    if lax.axis_size(axis) != 2:
        return lax.all_gather(values, axis, axis=dim, tiled=True)
    other = exchange(values, axis, 0)
    first = lax.axis_index(axis) == 0
    return jnp.concatenate(
        [jnp.where(first, values, other), jnp.where(first, other, values)], axis=dim
    )


def halving_steps(values, axis, order):
    bits = axis_bits(axis)
    chunk = values.shape[0] >> bits
    data = values.reshape((2,) * bits + (chunk,) + values.shape[1:])
    remaining = list(reversed(range(bits)))
    for bit in order:
        position = remaining.index(bit)
        remaining.remove(bit)
        mine = axis_bit(axis, bit)
        keep = lax.dynamic_index_in_dim(data, mine, position, keepdims=False)
        send = lax.dynamic_index_in_dim(data, 1 - mine, position, keepdims=False)
        data = keep + exchange(send, axis, bit)
    return data


def doubling_steps(values, axis, order):
    data = values
    present = []
    for bit in order:
        position = sum(1 for other in present if other > bit)
        present.insert(position, bit)
        other = exchange(data, axis, bit)
        first = axis_bit(axis, bit) == 0
        data = jnp.where(
            first, jnp.stack([data, other], axis=position), jnp.stack([other, data], axis=position)
        )
    return data


def bit_orders(axis):
    bits = axis_bits(axis)
    ascending = list(range(bits))
    if bits < 2:
        return [ascending]
    return [ascending, [1, 0] + ascending[2:]]


def halving_scatter(values, axis):
    orders = bit_orders(axis)
    bits = axis_bits(axis)
    shaped = values.reshape((1 << bits, -1) + values.shape[1:])
    pieces = jnp.split(shaped, len(orders), axis=1)
    results = [
        halving_steps(piece.reshape((-1,) + values.shape[1:]), axis, order)
        for piece, order in zip(pieces, orders)
    ]
    return jnp.concatenate(results, axis=0)


def doubling_gather(values, axis):
    orders = [list(reversed(order)) for order in bit_orders(axis)]
    pieces = jnp.split(values, len(orders), axis=0)
    results = [doubling_steps(piece, axis, order) for piece, order in zip(pieces, orders)]
    stacked = jnp.concatenate(
        [result.reshape((-1,) + result.shape[-2:]) for result in results], axis=1
    )
    return stacked.reshape((-1,) + values.shape[1:])


def doubling_gather_lanes(values, axis):
    orders = [list(reversed(order)) for order in bit_orders(axis)]
    pieces = jnp.split(values, len(orders), axis=1)
    results = [doubling_steps(piece, axis, order) for piece, order in zip(pieces, orders)]
    return jnp.concatenate(
        [result.reshape((-1,) + result.shape[-2:]) for result in results], axis=2
    )


def butterfly_sum(values, axes):
    for axis in axes:
        for bit in range(axis_bits(axis)):
            values = values + exchange(values, axis, bit)
    return values


def scatter_totals_and_counts(row_totals, row_counts, test_count):
    width = row_totals.shape[1]
    chunk_rows = row_totals.shape[0] // test_count
    count_rows = chunk_rows // width
    padded = -(-count_rows // 16) * 16
    pieces = [
        row_totals.reshape(test_count, chunk_rows, width),
        row_counts.reshape(test_count, count_rows, width),
    ]
    if padded > count_rows:
        pieces.append(jnp.zeros((test_count, padded - count_rows, width), jnp.float32))
    combined = jnp.concatenate(pieces, axis=1).reshape(-1, width)
    own = halving_scatter(combined, "test")
    return own[:chunk_rows], own[chunk_rows : chunk_rows + count_rows].reshape(-1)


def local(x_test, x_cand, w_self, w_neigh, d_out, block_row, block_col, block_mask, block_live):
    packed_masks = block_mask.reshape(block_mask.shape[2:])
    block_rows = block_row.reshape(-1)
    block_cols = block_col.reshape(-1)
    live = jnp.clip(block_live.reshape(1), 0, packed_masks.shape[0])
    block_edge = packed_masks.shape[-1]
    cand_count = lax.axis_size("cand")
    test_count = lax.axis_size("test")
    feat_index = lax.axis_index("feat")
    half_width = x_cand.shape[1]
    row_blocks = x_cand.shape[0] * test_count // block_edge
    col_blocks = x_test.shape[0] * cand_count // block_edge
    panel = doubling_gather(x_test, "cand")
    cand_full = gather_axis(x_cand, "feat", 1)
    row_totals, row_counts = block_aggregate(
        live, block_rows, block_cols, packed_masks, split_hi_lo(panel), row_blocks
    )
    own_totals, degree = scatter_totals_and_counts(row_totals, row_counts, test_count)
    aggregated = own_totals / (1.0 + degree)[:, None]
    self_cols = lax.dynamic_slice_in_dim(w_self, feat_index * half_width, half_width, 1)
    neigh_cols = lax.dynamic_slice_in_dim(w_neigh, feat_index * half_width, half_width, 1)
    self_rows = lax.dynamic_slice_in_dim(w_self, feat_index * half_width, half_width, 0)
    neigh_rows = lax.dynamic_slice_in_dim(w_neigh, feat_index * half_width, half_width, 0)
    aggregated_full = gather_axis(aggregated, "feat", 1)
    pre_act = jnp.dot(cand_full, self_cols, precision=HIGHEST) + jnp.dot(
        aggregated_full, neigh_cols, precision=HIGHEST
    )
    output = jax.nn.silu(pre_act)
    sigmoid_z = jax.nn.sigmoid(pre_act)
    grad_pre = d_out * (sigmoid_z * (1.0 + pre_act * (1.0 - sigmoid_z)))
    grad_full = gather_axis(grad_pre, "feat", 1)
    self_part = jnp.einsum("rk,rh->kh", x_cand, grad_full, precision=HIGHEST)
    neigh_part = jnp.einsum("rk,rh->kh", aggregated, grad_full, precision=HIGHEST)
    grad_w_pair = butterfly_sum(jnp.stack([self_part, neigh_part]), ("cand", "test"))
    root_count = math.sqrt(x_cand.shape[0] * cand_count * test_count)
    grad_x_cand = jnp.dot(grad_full, self_rows.T, precision=HIGHEST)
    grad_agg = jnp.dot(grad_full, neigh_rows.T, precision=HIGHEST)
    lifted = grad_agg / (1.0 + degree)[:, None]
    lifted_chunks = doubling_gather_lanes(lifted.T, "test")
    grad_w_pair, lifted_chunks = lax.optimization_barrier((grad_w_pair, lifted_chunks))
    grad_w_self = grad_w_pair[0] / root_count
    grad_w_neigh = grad_w_pair[1] / root_count
    out_t = block_transpose(live, block_rows, block_cols, packed_masks, lifted_chunks, cand_count)
    own_t = halving_scatter(out_t.reshape(-1, out_t.shape[2]), "cand")
    grad_x_test = own_t.T
    return (output, grad_w_self, grad_w_neigh, grad_x_cand, grad_x_test)


def solution(mesh):
    return jax.shard_map(
        local,
        mesh=mesh,
        in_specs=(
            P(("test", "cand"), "feat"),
            P(("cand", "test"), "feat"),
            P(),
            P(),
            P(("cand", "test"), "feat"),
            P("cand", "test", None),
            P("cand", "test", None),
            P("cand", "test", None, None, None),
            P("cand", "test"),
        ),
        out_specs=(
            P(("cand", "test"), "feat"),
            P("feat", None),
            P("feat", None),
            P(("cand", "test"), "feat"),
            P(("test", "cand"), "feat"),
        ),
        check_vma=False,
    )
```

```python
import math

import jax
import jax.numpy as jnp
from jax import lax
from jax.experimental import pallas as pl
from jax.experimental.pallas import tpu as pltpu
from jax.sharding import PartitionSpec as P

HIGHEST = lax.Precision.HIGHEST
SLOT_GROUP = 64


def split_hi_lo(values, axis):
    high = lax.reduce_precision(values, exponent_bits=8, mantissa_bits=7)
    return jnp.stack([high, values - high], axis=axis).astype(jnp.bfloat16)


def unpack_bits(words):
    word_rows, edge = words.shape
    cube = jnp.broadcast_to(words[:, None, :], (word_rows, 8, edge))
    shifts = lax.broadcasted_iota(jnp.int32, (word_rows, 8, edge), 1)
    bits = jnp.bitwise_and(jnp.right_shift(cube, shifts), 1)
    return bits.reshape(word_rows * 8, edge)


def unpack_bit_major(words):
    return jnp.concatenate(
        [jnp.bitwise_and(jnp.right_shift(words, bit), 1) for bit in range(8)], axis=0
    )


def to_bit_major(rows, edge):
    count, width = rows.shape
    shaped = rows.reshape(count // edge, edge // 8, 8, width)
    return jnp.swapaxes(shaped, 1, 2).reshape(count, width)


def from_bit_major(rows, edge):
    count, width = rows.shape
    shaped = rows.reshape(count // edge, 8, edge // 8, width)
    return jnp.swapaxes(shaped, 1, 2).reshape(count, width)


def unpack_block(words):
    return unpack_bits(words).astype(jnp.float32)


UNROLL = 8


def live_chunk(live_ref, group):
    base = pl.program_id(0) * group
    return base, base < live_ref[0]


def slot_words(masks_ref, live_ref, base, k):
    keep = jnp.where(base + k < live_ref[0], -1, 0).astype(jnp.int32)
    return unpack_block(jnp.bitwise_and(masks_ref[k], keep)).astype(jnp.bfloat16)


def forward_kernel(live_ref, rows_ref, cols_ref, masks_ref, panel_ref, totals_ref, bits_ref):
    group, _, edge = masks_ref.shape
    row_limit = totals_ref.shape[0] // edge - 1
    col_limit = panel_ref.shape[1] // edge - 1

    @pl.when(pl.program_id(0) == 0)
    def _():
        totals_ref[...] = jnp.zeros_like(totals_ref)
        bits_ref[...] = jnp.zeros_like(bits_ref)

    base, active = live_chunk(live_ref, group)

    @pl.when(active)
    def _():
        def body(k, carry):
            slot = base + k
            row = jnp.clip(rows_ref[slot], 0, row_limit)
            col = jnp.clip(cols_ref[slot], 0, col_limit)
            keep = jnp.where(slot < live_ref[0], -1, 0).astype(jnp.int32)
            bits = unpack_bit_major(jnp.bitwise_and(masks_ref[k], keep))
            bits_ref[row] += bits
            dense = bits.astype(jnp.float32).astype(jnp.bfloat16)
            col_start = pl.multiple_of(col * edge, edge)
            tile = jnp.concatenate(
                [panel_ref[0, pl.ds(col_start, edge), :], panel_ref[1, pl.ds(col_start, edge), :]],
                axis=0,
            )
            prod = jnp.dot(
                jnp.concatenate([dense, dense], axis=1), tile, preferred_element_type=jnp.float32
            )
            start = pl.multiple_of(row * edge, edge)
            totals_ref[pl.ds(start, edge), :] += prod
            return carry

        lax.fori_loop(0, group, body, 0, unroll=UNROLL)


def backward_kernel(live_ref, rows_ref, cols_ref, masks_ref, lifted_ref, out_ref):
    group, _, edge = masks_ref.shape
    row_chunk = lifted_ref.shape[3] // edge
    col_chunk = out_ref.shape[2] // edge
    row_limit = lifted_ref.shape[0] * row_chunk - 1
    col_limit = out_ref.shape[0] * col_chunk - 1

    @pl.when(pl.program_id(0) == 0)
    def _():
        out_ref[...] = jnp.zeros_like(out_ref)

    base, active = live_chunk(live_ref, group)

    @pl.when(active)
    def _():
        def body(k, carry):
            slot = base + k
            row = jnp.clip(rows_ref[slot], 0, row_limit)
            col = jnp.clip(cols_ref[slot], 0, col_limit)
            keep = jnp.where(slot < live_ref[0], -1, 0).astype(jnp.int32)
            bits = unpack_bit_major(jnp.bitwise_and(masks_ref[k], keep))
            dense = bits.astype(jnp.float32).astype(jnp.bfloat16)
            row_start = pl.multiple_of((row % row_chunk) * edge, edge)
            chunk = row // row_chunk
            tile = jnp.concatenate(
                [
                    lifted_ref[chunk, 0, :, pl.ds(row_start, edge)],
                    lifted_ref[chunk, 1, :, pl.ds(row_start, edge)],
                ],
                axis=1,
            )
            prod = jnp.dot(
                tile, jnp.concatenate([dense, dense], axis=0), preferred_element_type=jnp.float32
            )
            col_start = pl.multiple_of((col % col_chunk) * edge, edge)
            out_ref[col // col_chunk, :, pl.ds(col_start, edge)] += prod
            return carry

        lax.fori_loop(0, group, body, 0, unroll=UNROLL)


def mask_spec(packed_masks, group):
    word_rows, edge = packed_masks.shape[1:]

    def index_map(chunk, live_ref, rows_ref, cols_ref):
        last = jnp.maximum(live_ref[0] - 1, 0) // group
        return (jnp.minimum(chunk, last), 0, 0)

    return pl.BlockSpec((group, word_rows, edge), index_map)


def whole_spec(shape):
    return pl.BlockSpec(shape, lambda chunk, live_ref, rows_ref, cols_ref: (0,) * len(shape))


def slot_pallas(kernel, live, block_rows, block_cols, packed_masks, dense_input, out_shapes):
    slot_total = packed_masks.shape[0]
    group = min(SLOT_GROUP, slot_total)
    grid_spec = pltpu.PrefetchScalarGridSpec(
        num_scalar_prefetch=3,
        grid=(slot_total // group,),
        in_specs=[mask_spec(packed_masks, group), whole_spec(dense_input.shape)],
        out_specs=[whole_spec(shape.shape) for shape in out_shapes],
    )
    return pl.pallas_call(
        kernel,
        grid_spec=grid_spec,
        out_shape=out_shapes,
        compiler_params=pltpu.CompilerParams(dimension_semantics=("arbitrary",)),
    )(live, block_rows, block_cols, packed_masks, dense_input)


def block_aggregate(live, block_rows, block_cols, packed_masks, panel_split, row_blocks):
    edge = packed_masks.shape[-1]
    totals_shape = jax.ShapeDtypeStruct((row_blocks * edge, panel_split.shape[2]), jnp.float32)
    bits_shape = jax.ShapeDtypeStruct((row_blocks, edge, edge), jnp.int32)
    totals, bit_sums = slot_pallas(
        forward_kernel, live, block_rows, block_cols, packed_masks, panel_split,
        [totals_shape, bits_shape],
    )
    counts = jnp.sum(bit_sums, axis=-1).astype(jnp.float32).reshape(-1, 1)
    return totals, from_bit_major(counts, edge).reshape(-1)


def block_transpose(live, block_rows, block_cols, packed_masks, lifted_chunks, cand_count):
    edge = packed_masks.shape[-1]
    split_t = split_hi_lo(lifted_chunks, 1)
    width = lifted_chunks.shape[1]
    panel_cols = lifted_chunks.shape[0] * lifted_chunks.shape[2]
    out_shape = jax.ShapeDtypeStruct((cand_count, width, panel_cols // cand_count), jnp.float32)
    (out_t,) = slot_pallas(
        backward_kernel, live, block_rows, block_cols, packed_masks, split_t, [out_shape]
    )
    return out_t


def axis_bits(axis):
    count = lax.axis_size(axis)
    bits = count.bit_length() - 1
    assert count == 1 << bits
    return bits


def exchange(values, axis, bit):
    count = lax.axis_size(axis)
    return lax.ppermute(values, axis, [(i, i ^ (1 << bit)) for i in range(count)])


def axis_bit(axis, bit):
    return (lax.axis_index(axis) >> bit) & 1


def gather_axis(values, axis, dim):
    if lax.axis_size(axis) != 2:
        return lax.all_gather(values, axis, axis=dim, tiled=True)
    other = exchange(values, axis, 0)
    first = lax.axis_index(axis) == 0
    return jnp.concatenate(
        [jnp.where(first, values, other), jnp.where(first, other, values)], axis=dim
    )


def halving_steps(values, axis, order):
    bits = axis_bits(axis)
    chunk = values.shape[0] >> bits
    data = values.reshape((2,) * bits + (chunk,) + values.shape[1:])
    remaining = list(reversed(range(bits)))
    for bit in order:
        position = remaining.index(bit)
        remaining.remove(bit)
        mine = axis_bit(axis, bit)
        keep = lax.dynamic_index_in_dim(data, mine, position, keepdims=False)
        send = lax.dynamic_index_in_dim(data, 1 - mine, position, keepdims=False)
        data = keep + exchange(send, axis, bit)
    return data


def doubling_steps(values, axis, order):
    data = values
    present = []
    for bit in order:
        position = sum(1 for other in present if other > bit)
        present.insert(position, bit)
        other = exchange(data, axis, bit)
        first = axis_bit(axis, bit) == 0
        data = jnp.where(
            first, jnp.stack([data, other], axis=position), jnp.stack([other, data], axis=position)
        )
    return data


def bit_orders(axis):
    bits = axis_bits(axis)
    ascending = list(range(bits))
    if bits < 2:
        return [ascending]
    return [ascending, [1, 0] + ascending[2:]]


def halving_scatter(values, axis):
    orders = bit_orders(axis)
    bits = axis_bits(axis)
    shaped = values.reshape((1 << bits, -1) + values.shape[1:])
    pieces = jnp.split(shaped, len(orders), axis=1)
    results = [
        halving_steps(piece.reshape((-1,) + values.shape[1:]), axis, order)
        for piece, order in zip(pieces, orders)
    ]
    return jnp.concatenate(results, axis=0)


def doubling_gather(values, axis):
    orders = [list(reversed(order)) for order in bit_orders(axis)]
    pieces = jnp.split(values, len(orders), axis=0)
    results = [doubling_steps(piece, axis, order) for piece, order in zip(pieces, orders)]
    stacked = jnp.concatenate(
        [result.reshape((-1,) + result.shape[-2:]) for result in results], axis=1
    )
    return stacked.reshape((-1,) + values.shape[1:])


def doubling_gather_lanes(values, axis):
    orders = [list(reversed(order)) for order in bit_orders(axis)]
    pieces = jnp.split(values, len(orders), axis=1)
    results = [doubling_steps(piece, axis, order) for piece, order in zip(pieces, orders)]
    return jnp.concatenate(
        [result.reshape((-1,) + result.shape[-2:]) for result in results], axis=2
    )


def butterfly_sum(values, axes):
    for axis in axes:
        for bit in range(axis_bits(axis)):
            values = values + exchange(values, axis, bit)
    return values


def scatter_totals_and_counts(row_totals, row_counts, test_count):
    width = row_totals.shape[1]
    chunk_rows = row_totals.shape[0] // test_count
    count_rows = chunk_rows // width
    padded = -(-count_rows // 16) * 16
    pieces = [
        row_totals.reshape(test_count, chunk_rows, width),
        row_counts.reshape(test_count, count_rows, width),
    ]
    if padded > count_rows:
        pieces.append(jnp.zeros((test_count, padded - count_rows, width), jnp.float32))
    combined = jnp.concatenate(pieces, axis=1).reshape(-1, width)
    own = halving_scatter(combined, "test")
    return own[:chunk_rows], own[chunk_rows : chunk_rows + count_rows].reshape(-1)


def local(x_test, x_cand, w_self, w_neigh, d_out, block_row, block_col, block_mask, block_live):
    packed_masks = block_mask.reshape(block_mask.shape[2:])
    block_rows = block_row.reshape(-1)
    block_cols = block_col.reshape(-1)
    live = jnp.clip(block_live.reshape(1), 0, packed_masks.shape[0])
    block_edge = packed_masks.shape[-1]
    cand_count = lax.axis_size("cand")
    test_count = lax.axis_size("test")
    feat_index = lax.axis_index("feat")
    half_width = x_cand.shape[1]
    row_blocks = x_cand.shape[0] * test_count // block_edge
    col_blocks = x_test.shape[0] * cand_count // block_edge
    panel = doubling_gather(x_test, "cand")
    cand_full = gather_axis(x_cand, "feat", 1)
    row_totals, row_counts = block_aggregate(
        live, block_rows, block_cols, packed_masks, split_hi_lo(panel, 0), row_blocks
    )
    own_totals, degree = scatter_totals_and_counts(row_totals, row_counts, test_count)
    aggregated = from_bit_major(own_totals, block_edge) / (1.0 + degree)[:, None]
    self_cols = lax.dynamic_slice_in_dim(w_self, feat_index * half_width, half_width, 1)
    neigh_cols = lax.dynamic_slice_in_dim(w_neigh, feat_index * half_width, half_width, 1)
    self_rows = lax.dynamic_slice_in_dim(w_self, feat_index * half_width, half_width, 0)
    neigh_rows = lax.dynamic_slice_in_dim(w_neigh, feat_index * half_width, half_width, 0)
    aggregated_full = gather_axis(aggregated, "feat", 1)
    pre_act = jnp.dot(cand_full, self_cols, precision=HIGHEST) + jnp.dot(
        aggregated_full, neigh_cols, precision=HIGHEST
    )
    output = jax.nn.silu(pre_act)
    sigmoid_z = jax.nn.sigmoid(pre_act)
    grad_pre = d_out * (sigmoid_z * (1.0 + pre_act * (1.0 - sigmoid_z)))
    grad_full = gather_axis(grad_pre, "feat", 1)
    self_part = jnp.einsum("rk,rh->kh", x_cand, grad_full, precision=HIGHEST)
    neigh_part = jnp.einsum("rk,rh->kh", aggregated, grad_full, precision=HIGHEST)
    grad_w_pair = butterfly_sum(jnp.stack([self_part, neigh_part]), ("cand", "test"))
    root_count = math.sqrt(x_cand.shape[0] * cand_count * test_count)
    grad_x_cand = jnp.dot(grad_full, self_rows.T, precision=HIGHEST)
    grad_agg = jnp.dot(grad_full, neigh_rows.T, precision=HIGHEST)
    lifted = grad_agg / (1.0 + degree)[:, None]
    lifted_chunks = doubling_gather_lanes(to_bit_major(lifted, block_edge).T, "test")
    grad_w_pair, lifted_chunks = lax.optimization_barrier((grad_w_pair, lifted_chunks))
    grad_w_self = grad_w_pair[0] / root_count
    grad_w_neigh = grad_w_pair[1] / root_count
    out_t = block_transpose(live, block_rows, block_cols, packed_masks, lifted_chunks, cand_count)
    own_t = halving_scatter(out_t.reshape(-1, out_t.shape[2]), "cand")
    grad_x_test = own_t.T
    return (output, grad_w_self, grad_w_neigh, grad_x_cand, grad_x_test)


def solution(mesh):
    return jax.shard_map(
        local,
        mesh=mesh,
        in_specs=(
            P(("test", "cand"), "feat"),
            P(("cand", "test"), "feat"),
            P(),
            P(),
            P(("cand", "test"), "feat"),
            P("cand", "test", None),
            P("cand", "test", None),
            P("cand", "test", None, None, None),
            P("cand", "test"),
        ),
        out_specs=(
            P(("cand", "test"), "feat"),
            P("feat", None),
            P("feat", None),
            P(("cand", "test"), "feat"),
            P(("test", "cand"), "feat"),
        ),
        check_vma=False,
    )
```

```python
import math

import jax
import jax.numpy as jnp
from jax import lax
from jax.experimental import pallas as pl
from jax.experimental.pallas import tpu as pltpu
from jax.sharding import PartitionSpec as P

HIGHEST = lax.Precision.HIGHEST
SLOT_GROUP = 64


def split_hi_lo(values):
    high = lax.reduce_precision(values, exponent_bits=8, mantissa_bits=7)
    low = values - high
    return jnp.concatenate([high, low], axis=1).astype(jnp.bfloat16)


def unpack_bits(words):
    word_rows, edge = words.shape
    cube = jnp.broadcast_to(words[:, None, :], (word_rows, 8, edge))
    shifts = lax.broadcasted_iota(jnp.int32, (word_rows, 8, edge), 1)
    bits = jnp.bitwise_and(jnp.right_shift(cube, shifts), 1)
    return bits.reshape(word_rows * 8, edge)


def unpack_block(words):
    return unpack_bits(words).astype(jnp.float32)


UNROLL = 8


def live_chunk(live_ref, group):
    base = pl.program_id(0) * group
    return base, base < live_ref[0]


def slot_words(masks_ref, live_ref, base, k):
    keep = jnp.where(base + k < live_ref[0], -1, 0).astype(jnp.int32)
    return unpack_block(jnp.bitwise_and(masks_ref[k], keep)).astype(jnp.bfloat16)


def last_step():
    return pl.program_id(0) == pl.num_programs(0) - 1


def forward_kernel(
    live_ref, rows_ref, cols_ref, masks_ref, panel_ref, totals_ref, bits_ref, totals_odd, bits_odd
):
    group, _, edge = masks_ref.shape
    row_limit = totals_ref.shape[0] // edge - 1
    col_limit = panel_ref.shape[0] // edge - 1
    half = totals_ref.shape[1]

    @pl.when(pl.program_id(0) == 0)
    def _():
        totals_ref[...] = jnp.zeros_like(totals_ref)
        bits_ref[...] = jnp.zeros_like(bits_ref)
        totals_odd[...] = jnp.zeros_like(totals_odd)
        bits_odd[...] = jnp.zeros_like(bits_odd)

    base, active = live_chunk(live_ref, group)

    def one_slot(k, totals_acc, bits_acc):
        slot = base + k
        row = jnp.clip(rows_ref[slot], 0, row_limit)
        col = jnp.clip(cols_ref[slot], 0, col_limit)
        keep = jnp.where(slot < live_ref[0], -1, 0).astype(jnp.int32)
        bits = unpack_bits(jnp.bitwise_and(masks_ref[k], keep))
        bits_acc[row] += bits
        dense = bits.astype(jnp.float32).astype(jnp.bfloat16)
        tile = panel_ref[pl.ds(pl.multiple_of(col * edge, edge), edge), :]
        prod = jnp.dot(dense, tile, preferred_element_type=jnp.float32)
        start = pl.multiple_of(row * edge, edge)
        totals_acc[pl.ds(start, edge), :] += prod[:, :half] + prod[:, half:]

    @pl.when(active)
    def _():
        def body(pair, carry):
            one_slot(2 * pair, totals_ref, bits_ref)
            one_slot(2 * pair + 1, totals_odd, bits_odd)
            return carry

        lax.fori_loop(0, group // 2, body, 0, unroll=UNROLL // 2)

    @pl.when(last_step())
    def _():
        totals_ref[...] += totals_odd[...]
        bits_ref[...] += bits_odd[...]


def backward_kernel(live_ref, rows_ref, cols_ref, masks_ref, lifted_ref, out_ref, out_odd):
    group, _, edge = masks_ref.shape
    row_chunk = lifted_ref.shape[2] // edge
    col_chunk = out_ref.shape[2] // edge
    row_limit = lifted_ref.shape[0] * row_chunk - 1
    col_limit = out_ref.shape[0] * col_chunk - 1
    half = out_ref.shape[1]

    @pl.when(pl.program_id(0) == 0)
    def _():
        out_ref[...] = jnp.zeros_like(out_ref)
        out_odd[...] = jnp.zeros_like(out_odd)

    base, active = live_chunk(live_ref, group)

    def one_slot(k, out_acc):
        slot = base + k
        row = jnp.clip(rows_ref[slot], 0, row_limit)
        col = jnp.clip(cols_ref[slot], 0, col_limit)
        dense = slot_words(masks_ref, live_ref, base, k)
        row_start = pl.multiple_of((row % row_chunk) * edge, edge)
        tile = lifted_ref[row // row_chunk, :, pl.ds(row_start, edge)]
        prod = jnp.dot(tile, dense, preferred_element_type=jnp.float32)
        col_start = pl.multiple_of((col % col_chunk) * edge, edge)
        out_acc[col // col_chunk, :, pl.ds(col_start, edge)] += prod[:half] + prod[half:]

    @pl.when(active)
    def _():
        def body(pair, carry):
            one_slot(2 * pair, out_ref)
            one_slot(2 * pair + 1, out_odd)
            return carry

        lax.fori_loop(0, group // 2, body, 0, unroll=UNROLL // 2)

    @pl.when(last_step())
    def _():
        out_ref[...] += out_odd[...]


def mask_spec(packed_masks, group):
    word_rows, edge = packed_masks.shape[1:]

    def index_map(chunk, live_ref, rows_ref, cols_ref):
        last = jnp.maximum(live_ref[0] - 1, 0) // group
        return (jnp.minimum(chunk, last), 0, 0)

    return pl.BlockSpec((group, word_rows, edge), index_map)


def whole_spec(shape):
    return pl.BlockSpec(shape, lambda chunk, live_ref, rows_ref, cols_ref: (0,) * len(shape))


def slot_pallas(kernel, live, block_rows, block_cols, packed_masks, dense_input, out_shapes):
    slot_total = packed_masks.shape[0]
    group = min(SLOT_GROUP, slot_total)
    grid_spec = pltpu.PrefetchScalarGridSpec(
        num_scalar_prefetch=3,
        grid=(slot_total // group,),
        in_specs=[mask_spec(packed_masks, group), whole_spec(dense_input.shape)],
        out_specs=[whole_spec(shape.shape) for shape in out_shapes],
        scratch_shapes=[pltpu.VMEM(shape.shape, shape.dtype) for shape in out_shapes],
    )
    return pl.pallas_call(
        kernel,
        grid_spec=grid_spec,
        out_shape=out_shapes,
        compiler_params=pltpu.CompilerParams(dimension_semantics=("arbitrary",)),
    )(live, block_rows, block_cols, packed_masks, dense_input)


def block_aggregate(live, block_rows, block_cols, packed_masks, panel_split, row_blocks):
    edge = packed_masks.shape[-1]
    totals_shape = jax.ShapeDtypeStruct((row_blocks * edge, panel_split.shape[1] // 2), jnp.float32)
    bits_shape = jax.ShapeDtypeStruct((row_blocks, edge, edge), jnp.int32)
    totals, bit_sums = slot_pallas(
        forward_kernel, live, block_rows, block_cols, packed_masks, panel_split,
        [totals_shape, bits_shape],
    )
    return totals, jnp.sum(bit_sums, axis=-1).astype(jnp.float32).reshape(-1)


def block_transpose(live, block_rows, block_cols, packed_masks, lifted_chunks, cand_count):
    edge = packed_masks.shape[-1]
    high = lax.reduce_precision(lifted_chunks, exponent_bits=8, mantissa_bits=7)
    split_t = jnp.concatenate([high, lifted_chunks - high], axis=1).astype(jnp.bfloat16)
    width = lifted_chunks.shape[1]
    panel_cols = lifted_chunks.shape[0] * lifted_chunks.shape[2]
    out_shape = jax.ShapeDtypeStruct((cand_count, width, panel_cols // cand_count), jnp.float32)
    (out_t,) = slot_pallas(
        backward_kernel, live, block_rows, block_cols, packed_masks, split_t, [out_shape]
    )
    return out_t


def axis_bits(axis):
    count = lax.axis_size(axis)
    bits = count.bit_length() - 1
    assert count == 1 << bits
    return bits


def exchange(values, axis, bit):
    count = lax.axis_size(axis)
    return lax.ppermute(values, axis, [(i, i ^ (1 << bit)) for i in range(count)])


def axis_bit(axis, bit):
    return (lax.axis_index(axis) >> bit) & 1


def gather_axis(values, axis, dim):
    if lax.axis_size(axis) != 2:
        return lax.all_gather(values, axis, axis=dim, tiled=True)
    other = exchange(values, axis, 0)
    first = lax.axis_index(axis) == 0
    return jnp.concatenate(
        [jnp.where(first, values, other), jnp.where(first, other, values)], axis=dim
    )


def halving_steps(values, axis, order):
    bits = axis_bits(axis)
    chunk = values.shape[0] >> bits
    data = values.reshape((2,) * bits + (chunk,) + values.shape[1:])
    remaining = list(reversed(range(bits)))
    for bit in order:
        position = remaining.index(bit)
        remaining.remove(bit)
        mine = axis_bit(axis, bit)
        keep = lax.dynamic_index_in_dim(data, mine, position, keepdims=False)
        send = lax.dynamic_index_in_dim(data, 1 - mine, position, keepdims=False)
        data = keep + exchange(send, axis, bit)
    return data


def doubling_steps(values, axis, order):
    data = values
    present = []
    for bit in order:
        position = sum(1 for other in present if other > bit)
        present.insert(position, bit)
        other = exchange(data, axis, bit)
        first = axis_bit(axis, bit) == 0
        data = jnp.where(
            first, jnp.stack([data, other], axis=position), jnp.stack([other, data], axis=position)
        )
    return data


def bit_orders(axis):
    bits = axis_bits(axis)
    ascending = list(range(bits))
    if bits < 2:
        return [ascending]
    return [ascending, [1, 0] + ascending[2:]]


def halving_scatter(values, axis):
    orders = bit_orders(axis)
    bits = axis_bits(axis)
    shaped = values.reshape((1 << bits, -1) + values.shape[1:])
    pieces = jnp.split(shaped, len(orders), axis=1)
    results = [
        halving_steps(piece.reshape((-1,) + values.shape[1:]), axis, order)
        for piece, order in zip(pieces, orders)
    ]
    return jnp.concatenate(results, axis=0)


def doubling_gather(values, axis):
    orders = [list(reversed(order)) for order in bit_orders(axis)]
    pieces = jnp.split(values, len(orders), axis=0)
    results = [doubling_steps(piece, axis, order) for piece, order in zip(pieces, orders)]
    stacked = jnp.concatenate(
        [result.reshape((-1,) + result.shape[-2:]) for result in results], axis=1
    )
    return stacked.reshape((-1,) + values.shape[1:])


def doubling_gather_lanes(values, axis):
    orders = [list(reversed(order)) for order in bit_orders(axis)]
    pieces = jnp.split(values, len(orders), axis=1)
    results = [doubling_steps(piece, axis, order) for piece, order in zip(pieces, orders)]
    return jnp.concatenate(
        [result.reshape((-1,) + result.shape[-2:]) for result in results], axis=2
    )


def butterfly_sum(values, axes):
    for axis in axes:
        for bit in range(axis_bits(axis)):
            values = values + exchange(values, axis, bit)
    return values


def scatter_totals_and_counts(row_totals, row_counts, test_count):
    width = row_totals.shape[1]
    chunk_rows = row_totals.shape[0] // test_count
    count_rows = chunk_rows // width
    padded = -(-count_rows // 16) * 16
    pieces = [
        row_totals.reshape(test_count, chunk_rows, width),
        row_counts.reshape(test_count, count_rows, width),
    ]
    if padded > count_rows:
        pieces.append(jnp.zeros((test_count, padded - count_rows, width), jnp.float32))
    combined = jnp.concatenate(pieces, axis=1).reshape(-1, width)
    own = halving_scatter(combined, "test")
    return own[:chunk_rows], own[chunk_rows : chunk_rows + count_rows].reshape(-1)


def local(x_test, x_cand, w_self, w_neigh, d_out, block_row, block_col, block_mask, block_live):
    packed_masks = block_mask.reshape(block_mask.shape[2:])
    block_rows = block_row.reshape(-1)
    block_cols = block_col.reshape(-1)
    live = jnp.clip(block_live.reshape(1), 0, packed_masks.shape[0])
    block_edge = packed_masks.shape[-1]
    cand_count = lax.axis_size("cand")
    test_count = lax.axis_size("test")
    feat_index = lax.axis_index("feat")
    half_width = x_cand.shape[1]
    row_blocks = x_cand.shape[0] * test_count // block_edge
    col_blocks = x_test.shape[0] * cand_count // block_edge
    panel = doubling_gather(x_test, "cand")
    cand_full = gather_axis(x_cand, "feat", 1)
    row_totals, row_counts = block_aggregate(
        live, block_rows, block_cols, packed_masks, split_hi_lo(panel), row_blocks
    )
    own_totals, degree = scatter_totals_and_counts(row_totals, row_counts, test_count)
    aggregated = own_totals / (1.0 + degree)[:, None]
    self_cols = lax.dynamic_slice_in_dim(w_self, feat_index * half_width, half_width, 1)
    neigh_cols = lax.dynamic_slice_in_dim(w_neigh, feat_index * half_width, half_width, 1)
    self_rows = lax.dynamic_slice_in_dim(w_self, feat_index * half_width, half_width, 0)
    neigh_rows = lax.dynamic_slice_in_dim(w_neigh, feat_index * half_width, half_width, 0)
    aggregated_full = gather_axis(aggregated, "feat", 1)
    pre_act = jnp.dot(cand_full, self_cols, precision=HIGHEST) + jnp.dot(
        aggregated_full, neigh_cols, precision=HIGHEST
    )
    output = jax.nn.silu(pre_act)
    sigmoid_z = jax.nn.sigmoid(pre_act)
    grad_pre = d_out * (sigmoid_z * (1.0 + pre_act * (1.0 - sigmoid_z)))
    grad_full = gather_axis(grad_pre, "feat", 1)
    self_part = jnp.einsum("rk,rh->kh", x_cand, grad_full, precision=HIGHEST)
    neigh_part = jnp.einsum("rk,rh->kh", aggregated, grad_full, precision=HIGHEST)
    grad_w_pair = butterfly_sum(jnp.stack([self_part, neigh_part]), ("cand", "test"))
    root_count = math.sqrt(x_cand.shape[0] * cand_count * test_count)
    grad_x_cand = jnp.dot(grad_full, self_rows.T, precision=HIGHEST)
    grad_agg = jnp.dot(grad_full, neigh_rows.T, precision=HIGHEST)
    lifted = grad_agg / (1.0 + degree)[:, None]
    lifted_chunks = doubling_gather_lanes(lifted.T, "test")
    grad_w_pair, lifted_chunks = lax.optimization_barrier((grad_w_pair, lifted_chunks))
    grad_w_self = grad_w_pair[0] / root_count
    grad_w_neigh = grad_w_pair[1] / root_count
    out_t = block_transpose(live, block_rows, block_cols, packed_masks, lifted_chunks, cand_count)
    own_t = halving_scatter(out_t.reshape(-1, out_t.shape[2]), "cand")
    grad_x_test = own_t.T
    return (output, grad_w_self, grad_w_neigh, grad_x_cand, grad_x_test)


def solution(mesh):
    return jax.shard_map(
        local,
        mesh=mesh,
        in_specs=(
            P(("test", "cand"), "feat"),
            P(("cand", "test"), "feat"),
            P(),
            P(),
            P(("cand", "test"), "feat"),
            P("cand", "test", None),
            P("cand", "test", None),
            P("cand", "test", None, None, None),
            P("cand", "test"),
        ),
        out_specs=(
            P(("cand", "test"), "feat"),
            P("feat", None),
            P("feat", None),
            P(("cand", "test"), "feat"),
            P(("test", "cand"), "feat"),
        ),
        check_vma=False,
    )
```

```python
import math

import jax
import jax.numpy as jnp
from jax import lax
from jax.experimental import pallas as pl
from jax.experimental.pallas import tpu as pltpu
from jax.sharding import PartitionSpec as P

HIGHEST = lax.Precision.HIGHEST
SLOT_GROUP = 64


def split_hi_lo(values):
    high = lax.reduce_precision(values, exponent_bits=8, mantissa_bits=7)
    low = values - high
    return jnp.concatenate([high, low], axis=1).astype(jnp.bfloat16)


def unpack_bits(words):
    word_rows, edge = words.shape
    cube = jnp.broadcast_to(words[:, None, :], (word_rows, 8, edge))
    shifts = lax.broadcasted_iota(jnp.int32, (word_rows, 8, edge), 1)
    bits = jnp.bitwise_and(jnp.right_shift(cube, shifts), 1)
    return bits.reshape(word_rows * 8, edge)


def unpack_block(words):
    return unpack_bits(words).astype(jnp.float32)


UNROLL = 8


def live_chunk(live_ref, group):
    base = pl.program_id(0) * group
    return base, base < live_ref[0]


def slot_words(masks_ref, live_ref, base, k):
    keep = jnp.where(base + k < live_ref[0], -1, 0).astype(jnp.int32)
    return unpack_block(jnp.bitwise_and(masks_ref[k], keep)).astype(jnp.bfloat16)


def forward_kernel(live_ref, rows_ref, cols_ref, masks_ref, panel_ref, totals_ref, bits_ref):
    group, _, edge = masks_ref.shape
    row_limit = totals_ref.shape[0] // edge - 1
    col_limit = panel_ref.shape[0] // edge - 1
    half = totals_ref.shape[1]

    @pl.when(pl.program_id(0) == 0)
    def _():
        totals_ref[...] = jnp.zeros_like(totals_ref)
        bits_ref[...] = jnp.zeros_like(bits_ref)

    base, active = live_chunk(live_ref, group)

    @pl.when(active)
    def _():
        def body(k, carry):
            slot = base + k
            row = jnp.clip(rows_ref[slot], 0, row_limit)
            col = jnp.clip(cols_ref[slot], 0, col_limit)
            keep = jnp.where(slot < live_ref[0], -1, 0).astype(jnp.int32)
            bits = unpack_bits(jnp.bitwise_and(masks_ref[k], keep))
            bits_ref[row] += bits
            dense = bits.astype(jnp.float32).astype(jnp.bfloat16)
            tile = panel_ref[pl.ds(pl.multiple_of(col * edge, edge), edge), :]
            prod = jnp.dot(dense, tile, preferred_element_type=jnp.float32)
            start = pl.multiple_of(row * edge, edge)
            totals_ref[pl.ds(start, edge), :] += prod[:, :half] + prod[:, half:]
            return carry

        lax.fori_loop(0, group, body, 0, unroll=UNROLL)


def backward_kernel(live_ref, rows_ref, cols_ref, masks_ref, lifted_ref, out_ref):
    group, _, edge = masks_ref.shape
    row_chunk = lifted_ref.shape[2] // edge
    col_chunk = out_ref.shape[2] // edge
    row_limit = lifted_ref.shape[0] * row_chunk - 1
    col_limit = out_ref.shape[0] * col_chunk - 1
    half = out_ref.shape[1]

    @pl.when(pl.program_id(0) == 0)
    def _():
        out_ref[...] = jnp.zeros_like(out_ref)

    base, active = live_chunk(live_ref, group)

    @pl.when(active)
    def _():
        def body(k, carry):
            slot = base + k
            row = jnp.clip(rows_ref[slot], 0, row_limit)
            col = jnp.clip(cols_ref[slot], 0, col_limit)
            dense = slot_words(masks_ref, live_ref, base, k)
            row_start = pl.multiple_of((row % row_chunk) * edge, edge)
            tile = lifted_ref[row // row_chunk, :, pl.ds(row_start, edge)]
            prod = jnp.dot(tile, dense, preferred_element_type=jnp.float32)
            col_start = pl.multiple_of((col % col_chunk) * edge, edge)
            out_ref[col // col_chunk, :, pl.ds(col_start, edge)] += prod[:half] + prod[half:]
            return carry

        lax.fori_loop(0, group, body, 0, unroll=UNROLL)


def mask_spec(packed_masks, group):
    word_rows, edge = packed_masks.shape[1:]

    def index_map(chunk, live_ref, rows_ref, cols_ref):
        last = jnp.maximum(live_ref[0] - 1, 0) // group
        return (jnp.minimum(chunk, last), 0, 0)

    return pl.BlockSpec((group, word_rows, edge), index_map)


def whole_spec(shape):
    return pl.BlockSpec(shape, lambda chunk, live_ref, rows_ref, cols_ref: (0,) * len(shape))


def slot_pallas(kernel, live, block_rows, block_cols, packed_masks, dense_input, out_shapes):
    slot_total = packed_masks.shape[0]
    group = min(SLOT_GROUP, slot_total)
    grid_spec = pltpu.PrefetchScalarGridSpec(
        num_scalar_prefetch=3,
        grid=(slot_total // group,),
        in_specs=[mask_spec(packed_masks, group), whole_spec(dense_input.shape)],
        out_specs=[whole_spec(shape.shape) for shape in out_shapes],
    )
    return pl.pallas_call(
        kernel,
        grid_spec=grid_spec,
        out_shape=out_shapes,
        compiler_params=pltpu.CompilerParams(dimension_semantics=("arbitrary",)),
    )(live, block_rows, block_cols, packed_masks, dense_input)


def block_aggregate(live, block_rows, block_cols, packed_masks, panel_split, row_blocks):
    edge = packed_masks.shape[-1]
    totals_shape = jax.ShapeDtypeStruct((row_blocks * edge, panel_split.shape[1] // 2), jnp.float32)
    bits_shape = jax.ShapeDtypeStruct((row_blocks, edge, edge), jnp.int32)
    totals, bit_sums = slot_pallas(
        forward_kernel, live, block_rows, block_cols, packed_masks, panel_split,
        [totals_shape, bits_shape],
    )
    return totals, jnp.sum(bit_sums, axis=-1).astype(jnp.float32).reshape(-1)


def block_transpose(live, block_rows, block_cols, packed_masks, lifted_chunks, cand_count):
    edge = packed_masks.shape[-1]
    high = lax.reduce_precision(lifted_chunks, exponent_bits=8, mantissa_bits=7)
    split_t = jnp.concatenate([high, lifted_chunks - high], axis=1).astype(jnp.bfloat16)
    width = lifted_chunks.shape[1]
    panel_cols = lifted_chunks.shape[0] * lifted_chunks.shape[2]
    out_shape = jax.ShapeDtypeStruct((cand_count, width, panel_cols // cand_count), jnp.float32)
    (out_t,) = slot_pallas(
        backward_kernel, live, block_rows, block_cols, packed_masks, split_t, [out_shape]
    )
    return out_t


def axis_bits(axis):
    count = lax.axis_size(axis)
    bits = count.bit_length() - 1
    assert count == 1 << bits
    return bits


def exchange(values, axis, bit):
    count = lax.axis_size(axis)
    return lax.ppermute(values, axis, [(i, i ^ (1 << bit)) for i in range(count)])


def axis_bit(axis, bit):
    return (lax.axis_index(axis) >> bit) & 1


def gather_axis(values, axis, dim):
    if lax.axis_size(axis) != 2:
        return lax.all_gather(values, axis, axis=dim, tiled=True)
    other = exchange(values, axis, 0)
    first = lax.axis_index(axis) == 0
    return jnp.concatenate(
        [jnp.where(first, values, other), jnp.where(first, other, values)], axis=dim
    )


def exchange_all(sends, axis, bits):
    if len(sends) > 1 and len(set(bits)) == 1:
        received = exchange(jnp.stack(sends), axis, bits[0])
        return [received[i] for i in range(len(sends))]
    return [exchange(send, axis, bit) for send, bit in zip(sends, bits)]


def halving_steps(pieces, axis, orders):
    bits = axis_bits(axis)
    datas = [
        piece.reshape((2,) * bits + (piece.shape[0] >> bits,) + piece.shape[1:]) for piece in pieces
    ]
    remaining = [list(reversed(range(bits))) for _ in pieces]
    for step in range(bits):
        keeps, sends, step_bits = [], [], []
        for index, order in enumerate(orders):
            bit = order[step]
            position = remaining[index].index(bit)
            remaining[index].remove(bit)
            mine = axis_bit(axis, bit)
            keeps.append(lax.dynamic_index_in_dim(datas[index], mine, position, keepdims=False))
            sends.append(lax.dynamic_index_in_dim(datas[index], 1 - mine, position, keepdims=False))
            step_bits.append(bit)
        received = exchange_all(sends, axis, step_bits)
        datas = [keep + other for keep, other in zip(keeps, received)]
    return datas


def doubling_steps(pieces, axis, orders):
    datas = list(pieces)
    present = [[] for _ in pieces]
    for step in range(len(orders[0])):
        step_bits = [order[step] for order in orders]
        received = exchange_all(datas, axis, step_bits)
        for index, bit in enumerate(step_bits):
            position = sum(1 for other in present[index] if other > bit)
            present[index].insert(position, bit)
            first = axis_bit(axis, bit) == 0
            data, other = datas[index], received[index]
            datas[index] = jnp.where(
                first,
                jnp.stack([data, other], axis=position),
                jnp.stack([other, data], axis=position),
            )
    return datas


def bit_orders(axis):
    bits = axis_bits(axis)
    ascending = list(range(bits))
    if bits < 2:
        return [ascending]
    return [ascending, [1, 0] + ascending[2:]]


def halving_scatter(values, axis):
    orders = bit_orders(axis)
    bits = axis_bits(axis)
    shaped = values.reshape((1 << bits, -1) + values.shape[1:])
    pieces = [
        piece.reshape((-1,) + values.shape[1:]) for piece in jnp.split(shaped, len(orders), axis=1)
    ]
    return jnp.concatenate(halving_steps(pieces, axis, orders), axis=0)


def doubling_gather(values, axis):
    orders = [list(reversed(order)) for order in bit_orders(axis)]
    results = doubling_steps(jnp.split(values, len(orders), axis=0), axis, orders)
    stacked = jnp.concatenate(
        [result.reshape((-1,) + result.shape[-2:]) for result in results], axis=1
    )
    return stacked.reshape((-1,) + values.shape[1:])


def doubling_gather_lanes(values, axis):
    orders = [list(reversed(order)) for order in bit_orders(axis)]
    results = doubling_steps(jnp.split(values, len(orders), axis=1), axis, orders)
    return jnp.concatenate(
        [result.reshape((-1,) + result.shape[-2:]) for result in results], axis=2
    )


def butterfly_sum(values, axes):
    for axis in axes:
        for bit in range(axis_bits(axis)):
            values = values + exchange(values, axis, bit)
    return values


def scatter_totals_and_counts(row_totals, row_counts, test_count):
    width = row_totals.shape[1]
    chunk_rows = row_totals.shape[0] // test_count
    count_rows = chunk_rows // width
    padded = -(-count_rows // 16) * 16
    pieces = [
        row_totals.reshape(test_count, chunk_rows, width),
        row_counts.reshape(test_count, count_rows, width),
    ]
    if padded > count_rows:
        pieces.append(jnp.zeros((test_count, padded - count_rows, width), jnp.float32))
    combined = jnp.concatenate(pieces, axis=1).reshape(-1, width)
    own = halving_scatter(combined, "test")
    return own[:chunk_rows], own[chunk_rows : chunk_rows + count_rows].reshape(-1)


def local(x_test, x_cand, w_self, w_neigh, d_out, block_row, block_col, block_mask, block_live):
    packed_masks = block_mask.reshape(block_mask.shape[2:])
    block_rows = block_row.reshape(-1)
    block_cols = block_col.reshape(-1)
    live = jnp.clip(block_live.reshape(1), 0, packed_masks.shape[0])
    block_edge = packed_masks.shape[-1]
    cand_count = lax.axis_size("cand")
    test_count = lax.axis_size("test")
    feat_index = lax.axis_index("feat")
    half_width = x_cand.shape[1]
    row_blocks = x_cand.shape[0] * test_count // block_edge
    col_blocks = x_test.shape[0] * cand_count // block_edge
    panel = doubling_gather(x_test, "cand")
    cand_full = gather_axis(x_cand, "feat", 1)
    row_totals, row_counts = block_aggregate(
        live, block_rows, block_cols, packed_masks, split_hi_lo(panel), row_blocks
    )
    own_totals, degree = scatter_totals_and_counts(row_totals, row_counts, test_count)
    aggregated = own_totals / (1.0 + degree)[:, None]
    self_cols = lax.dynamic_slice_in_dim(w_self, feat_index * half_width, half_width, 1)
    neigh_cols = lax.dynamic_slice_in_dim(w_neigh, feat_index * half_width, half_width, 1)
    self_rows = lax.dynamic_slice_in_dim(w_self, feat_index * half_width, half_width, 0)
    neigh_rows = lax.dynamic_slice_in_dim(w_neigh, feat_index * half_width, half_width, 0)
    aggregated_full = gather_axis(aggregated, "feat", 1)
    pre_act = jnp.dot(cand_full, self_cols, precision=HIGHEST) + jnp.dot(
        aggregated_full, neigh_cols, precision=HIGHEST
    )
    output = jax.nn.silu(pre_act)
    sigmoid_z = jax.nn.sigmoid(pre_act)
    grad_pre = d_out * (sigmoid_z * (1.0 + pre_act * (1.0 - sigmoid_z)))
    grad_full = gather_axis(grad_pre, "feat", 1)
    self_part = jnp.einsum("rk,rh->kh", x_cand, grad_full, precision=HIGHEST)
    neigh_part = jnp.einsum("rk,rh->kh", aggregated, grad_full, precision=HIGHEST)
    grad_w_pair = butterfly_sum(jnp.stack([self_part, neigh_part]), ("cand", "test"))
    root_count = math.sqrt(x_cand.shape[0] * cand_count * test_count)
    grad_x_cand = jnp.dot(grad_full, self_rows.T, precision=HIGHEST)
    grad_agg = jnp.dot(grad_full, neigh_rows.T, precision=HIGHEST)
    lifted = grad_agg / (1.0 + degree)[:, None]
    lifted_chunks = doubling_gather_lanes(lifted.T, "test")
    grad_w_pair, lifted_chunks = lax.optimization_barrier((grad_w_pair, lifted_chunks))
    grad_w_self = grad_w_pair[0] / root_count
    grad_w_neigh = grad_w_pair[1] / root_count
    out_t = block_transpose(live, block_rows, block_cols, packed_masks, lifted_chunks, cand_count)
    own_t = halving_scatter(out_t.reshape(-1, out_t.shape[2]), "cand")
    grad_x_test = own_t.T
    return (output, grad_w_self, grad_w_neigh, grad_x_cand, grad_x_test)


def solution(mesh):
    return jax.shard_map(
        local,
        mesh=mesh,
        in_specs=(
            P(("test", "cand"), "feat"),
            P(("cand", "test"), "feat"),
            P(),
            P(),
            P(("cand", "test"), "feat"),
            P("cand", "test", None),
            P("cand", "test", None),
            P("cand", "test", None, None, None),
            P("cand", "test"),
        ),
        out_specs=(
            P(("cand", "test"), "feat"),
            P("feat", None),
            P("feat", None),
            P(("cand", "test"), "feat"),
            P(("test", "cand"), "feat"),
        ),
        check_vma=False,
    )
```

```python
import math

import jax
import jax.numpy as jnp
from jax import lax
from jax.experimental import pallas as pl
from jax.experimental.pallas import tpu as pltpu
from jax.sharding import PartitionSpec as P

HIGHEST = lax.Precision.HIGHEST
SLOT_GROUP = 64


def split_hi_lo(values):
    high = lax.reduce_precision(values, exponent_bits=8, mantissa_bits=7)
    low = values - high
    return jnp.concatenate([high, low], axis=1).astype(jnp.bfloat16)


def unpack_bits(words):
    word_rows, edge = words.shape
    cube = jnp.broadcast_to(words[:, None, :], (word_rows, 8, edge))
    shifts = lax.broadcasted_iota(jnp.int32, (word_rows, 8, edge), 1)
    bits = jnp.bitwise_and(jnp.right_shift(cube, shifts), 1)
    return bits.reshape(word_rows * 8, edge)


def split_tile(tile, axis):
    high = tile.astype(jnp.bfloat16)
    low = (tile - high.astype(jnp.float32)).astype(jnp.bfloat16)
    return jnp.concatenate([high, low], axis=axis)


def unpack_block(words):
    return unpack_bits(words).astype(jnp.float32)


UNROLL = 8


def live_chunk(live_ref, group):
    base = pl.program_id(0) * group
    return base, base < live_ref[0]


def slot_words(masks_ref, live_ref, base, k):
    keep = jnp.where(base + k < live_ref[0], -1, 0).astype(jnp.int32)
    return unpack_block(jnp.bitwise_and(masks_ref[k], keep)).astype(jnp.bfloat16)


def forward_kernel(live_ref, rows_ref, cols_ref, masks_ref, panel_ref, totals_ref, bits_ref):
    group, _, edge = masks_ref.shape
    row_limit = totals_ref.shape[0] // edge - 1
    col_limit = panel_ref.shape[0] // edge - 1
    half = totals_ref.shape[1]

    @pl.when(pl.program_id(0) == 0)
    def _():
        totals_ref[...] = jnp.zeros_like(totals_ref)
        bits_ref[...] = jnp.zeros_like(bits_ref)

    base, active = live_chunk(live_ref, group)

    @pl.when(active)
    def _():
        def body(k, carry):
            slot = base + k
            row = jnp.clip(rows_ref[slot], 0, row_limit)
            col = jnp.clip(cols_ref[slot], 0, col_limit)
            keep = jnp.where(slot < live_ref[0], -1, 0).astype(jnp.int32)
            bits = unpack_bits(jnp.bitwise_and(masks_ref[k], keep))
            bits_ref[row] += bits
            dense = bits.astype(jnp.float32).astype(jnp.bfloat16)
            tile = split_tile(panel_ref[pl.ds(pl.multiple_of(col * edge, edge), edge), :], 1)
            prod = jnp.dot(dense, tile, preferred_element_type=jnp.float32)
            start = pl.multiple_of(row * edge, edge)
            totals_ref[pl.ds(start, edge), :] += prod[:, :half] + prod[:, half:]
            return carry

        lax.fori_loop(0, group, body, 0, unroll=UNROLL)


def backward_kernel(live_ref, rows_ref, cols_ref, masks_ref, lifted_ref, out_ref):
    group, _, edge = masks_ref.shape
    row_chunk = lifted_ref.shape[2] // edge
    col_chunk = out_ref.shape[2] // edge
    row_limit = lifted_ref.shape[0] * row_chunk - 1
    col_limit = out_ref.shape[0] * col_chunk - 1
    half = out_ref.shape[1]

    @pl.when(pl.program_id(0) == 0)
    def _():
        out_ref[...] = jnp.zeros_like(out_ref)

    base, active = live_chunk(live_ref, group)

    @pl.when(active)
    def _():
        def body(k, carry):
            slot = base + k
            row = jnp.clip(rows_ref[slot], 0, row_limit)
            col = jnp.clip(cols_ref[slot], 0, col_limit)
            dense = slot_words(masks_ref, live_ref, base, k)
            row_start = pl.multiple_of((row % row_chunk) * edge, edge)
            tile = split_tile(lifted_ref[row // row_chunk, :, pl.ds(row_start, edge)], 0)
            prod = jnp.dot(tile, dense, preferred_element_type=jnp.float32)
            col_start = pl.multiple_of((col % col_chunk) * edge, edge)
            relative = jnp.bitwise_xor(col // col_chunk, live_ref[1])
            out_ref[relative, :, pl.ds(col_start, edge)] += prod[:half] + prod[half:]
            return carry

        lax.fori_loop(0, group, body, 0, unroll=UNROLL)


def mask_spec(packed_masks, group):
    word_rows, edge = packed_masks.shape[1:]

    def index_map(chunk, live_ref, rows_ref, cols_ref):
        last = jnp.maximum(live_ref[0] - 1, 0) // group
        return (jnp.minimum(chunk, last), 0, 0)

    return pl.BlockSpec((group, word_rows, edge), index_map)


def whole_spec(shape):
    return pl.BlockSpec(shape, lambda chunk, live_ref, rows_ref, cols_ref: (0,) * len(shape))


def slot_pallas(kernel, live, block_rows, block_cols, packed_masks, dense_input, out_shapes):
    slot_total = packed_masks.shape[0]
    group = min(SLOT_GROUP, slot_total)
    grid_spec = pltpu.PrefetchScalarGridSpec(
        num_scalar_prefetch=3,
        grid=(slot_total // group,),
        in_specs=[mask_spec(packed_masks, group), whole_spec(dense_input.shape)],
        out_specs=[whole_spec(shape.shape) for shape in out_shapes],
    )
    return pl.pallas_call(
        kernel,
        grid_spec=grid_spec,
        out_shape=out_shapes,
        compiler_params=pltpu.CompilerParams(dimension_semantics=("arbitrary",)),
    )(live, block_rows, block_cols, packed_masks, dense_input)


def block_aggregate(live, block_rows, block_cols, packed_masks, panel_split, row_blocks):
    edge = packed_masks.shape[-1]
    totals_shape = jax.ShapeDtypeStruct((row_blocks * edge, panel_split.shape[1]), jnp.float32)
    bits_shape = jax.ShapeDtypeStruct((row_blocks, edge, edge), jnp.int32)
    totals, bit_sums = slot_pallas(
        forward_kernel, live, block_rows, block_cols, packed_masks, panel_split,
        [totals_shape, bits_shape],
    )
    return totals, jnp.sum(bit_sums, axis=-1).astype(jnp.float32).reshape(-1)


def block_transpose(live, block_rows, block_cols, packed_masks, lifted_chunks, cand_count):
    edge = packed_masks.shape[-1]
    split_t = lifted_chunks
    width = lifted_chunks.shape[1]
    panel_cols = lifted_chunks.shape[0] * lifted_chunks.shape[2]
    out_shape = jax.ShapeDtypeStruct((cand_count, width, panel_cols // cand_count), jnp.float32)
    (out_t,) = slot_pallas(
        backward_kernel, live, block_rows, block_cols, packed_masks, split_t, [out_shape]
    )
    return out_t


def axis_bits(axis):
    count = lax.axis_size(axis)
    bits = count.bit_length() - 1
    assert count == 1 << bits
    return bits


def exchange(values, axis, bit):
    count = lax.axis_size(axis)
    return lax.ppermute(values, axis, [(i, i ^ (1 << bit)) for i in range(count)])


def axis_bit(axis, bit):
    return (lax.axis_index(axis) >> bit) & 1


def gather_axis(values, axis, dim):
    if lax.axis_size(axis) != 2:
        return lax.all_gather(values, axis, axis=dim, tiled=True)
    other = exchange(values, axis, 0)
    first = lax.axis_index(axis) == 0
    return jnp.concatenate(
        [jnp.where(first, values, other), jnp.where(first, other, values)], axis=dim
    )


def halving_steps(values, axis, order):
    bits = axis_bits(axis)
    chunk = values.shape[0] >> bits
    data = values.reshape((2,) * bits + (chunk,) + values.shape[1:])
    remaining = list(reversed(range(bits)))
    for bit in order:
        position = remaining.index(bit)
        remaining.remove(bit)
        mine = axis_bit(axis, bit)
        keep = lax.dynamic_index_in_dim(data, mine, position, keepdims=False)
        send = lax.dynamic_index_in_dim(data, 1 - mine, position, keepdims=False)
        data = keep + exchange(send, axis, bit)
    return data


def doubling_steps(values, axis, order):
    data = values
    present = []
    for bit in order:
        position = sum(1 for other in present if other > bit)
        present.insert(position, bit)
        other = exchange(data, axis, bit)
        first = axis_bit(axis, bit) == 0
        data = jnp.where(
            first, jnp.stack([data, other], axis=position), jnp.stack([other, data], axis=position)
        )
    return data


def bit_orders(axis):
    bits = axis_bits(axis)
    ascending = list(range(bits))
    if bits < 2:
        return [ascending]
    return [ascending, [1, 0] + ascending[2:]]


def halving_scatter(values, axis):
    orders = bit_orders(axis)
    bits = axis_bits(axis)
    shaped = values.reshape((1 << bits, -1) + values.shape[1:])
    pieces = jnp.split(shaped, len(orders), axis=1)
    results = [
        halving_steps(piece.reshape((-1,) + values.shape[1:]), axis, order)
        for piece, order in zip(pieces, orders)
    ]
    return jnp.concatenate(results, axis=0)


def doubling_gather(values, axis):
    orders = [list(reversed(order)) for order in bit_orders(axis)]
    pieces = jnp.split(values, len(orders), axis=0)
    results = [doubling_steps(piece, axis, order) for piece, order in zip(pieces, orders)]
    stacked = jnp.concatenate(
        [result.reshape((-1,) + result.shape[-2:]) for result in results], axis=1
    )
    return stacked.reshape((-1,) + values.shape[1:])


def doubling_gather_lanes(values, axis):
    orders = [list(reversed(order)) for order in bit_orders(axis)]
    pieces = jnp.split(values, len(orders), axis=1)
    results = [doubling_steps(piece, axis, order) for piece, order in zip(pieces, orders)]
    return jnp.concatenate(
        [result.reshape((-1,) + result.shape[-2:]) for result in results], axis=2
    )


def halving_relative(chunks, axis):
    bits = axis_bits(axis)
    data = chunks.reshape((2,) * bits + chunks.shape[1:])
    remaining = list(reversed(range(bits)))
    for bit in range(bits):
        position = remaining.index(bit)
        remaining.remove(bit)
        keep = lax.index_in_dim(data, 0, position, keepdims=False)
        send = lax.index_in_dim(data, 1, position, keepdims=False)
        data = keep + exchange(send, axis, bit)
    return data


def butterfly_sum(values, axes):
    for axis in axes:
        for bit in range(axis_bits(axis)):
            values = values + exchange(values, axis, bit)
    return values


def scatter_totals_and_counts(row_totals, row_counts, test_count):
    width = row_totals.shape[1]
    chunk_rows = row_totals.shape[0] // test_count
    count_rows = chunk_rows // width
    padded = -(-count_rows // 16) * 16
    pieces = [
        row_totals.reshape(test_count, chunk_rows, width),
        row_counts.reshape(test_count, count_rows, width),
    ]
    if padded > count_rows:
        pieces.append(jnp.zeros((test_count, padded - count_rows, width), jnp.float32))
    combined = jnp.concatenate(pieces, axis=1).reshape(-1, width)
    own = halving_scatter(combined, "test")
    return own[:chunk_rows], own[chunk_rows : chunk_rows + count_rows].reshape(-1)


def local(x_test, x_cand, w_self, w_neigh, d_out, block_row, block_col, block_mask, block_live):
    packed_masks = block_mask.reshape(block_mask.shape[2:])
    block_rows = block_row.reshape(-1)
    block_cols = block_col.reshape(-1)
    live = jnp.concatenate(
        [jnp.clip(block_live.reshape(1), 0, packed_masks.shape[0]), lax.axis_index("cand").reshape(1)]
    ).astype(jnp.int32)
    block_edge = packed_masks.shape[-1]
    cand_count = lax.axis_size("cand")
    test_count = lax.axis_size("test")
    feat_index = lax.axis_index("feat")
    half_width = x_cand.shape[1]
    row_blocks = x_cand.shape[0] * test_count // block_edge
    col_blocks = x_test.shape[0] * cand_count // block_edge
    panel = doubling_gather(x_test, "cand")
    cand_full = gather_axis(x_cand, "feat", 1)
    row_totals, row_counts = block_aggregate(
        live, block_rows, block_cols, packed_masks, panel, row_blocks
    )
    own_totals, degree = scatter_totals_and_counts(row_totals, row_counts, test_count)
    aggregated = own_totals / (1.0 + degree)[:, None]
    self_cols = lax.dynamic_slice_in_dim(w_self, feat_index * half_width, half_width, 1)
    neigh_cols = lax.dynamic_slice_in_dim(w_neigh, feat_index * half_width, half_width, 1)
    self_rows = lax.dynamic_slice_in_dim(w_self, feat_index * half_width, half_width, 0)
    neigh_rows = lax.dynamic_slice_in_dim(w_neigh, feat_index * half_width, half_width, 0)
    aggregated_full = gather_axis(aggregated, "feat", 1)
    pre_act = jnp.dot(cand_full, self_cols, precision=HIGHEST) + jnp.dot(
        aggregated_full, neigh_cols, precision=HIGHEST
    )
    output = jax.nn.silu(pre_act)
    sigmoid_z = jax.nn.sigmoid(pre_act)
    grad_pre = d_out * (sigmoid_z * (1.0 + pre_act * (1.0 - sigmoid_z)))
    grad_full = gather_axis(grad_pre, "feat", 1)
    self_part = jnp.einsum("rk,rh->kh", x_cand, grad_full, precision=HIGHEST)
    neigh_part = jnp.einsum("rk,rh->kh", aggregated, grad_full, precision=HIGHEST)
    grad_w_pair = butterfly_sum(jnp.stack([self_part, neigh_part]), ("cand", "test"))
    root_count = math.sqrt(x_cand.shape[0] * cand_count * test_count)
    grad_x_cand = jnp.dot(grad_full, self_rows.T, precision=HIGHEST)
    grad_agg = jnp.dot(grad_full, neigh_rows.T, precision=HIGHEST)
    lifted = grad_agg / (1.0 + degree)[:, None]
    lifted_chunks = doubling_gather_lanes(lifted.T, "test")
    grad_w_pair, lifted_chunks = lax.optimization_barrier((grad_w_pair, lifted_chunks))
    grad_w_self = grad_w_pair[0] / root_count
    grad_w_neigh = grad_w_pair[1] / root_count
    out_t = block_transpose(live, block_rows, block_cols, packed_masks, lifted_chunks, cand_count)
    own_t = halving_relative(out_t, "cand")
    grad_x_test = own_t.T
    return (output, grad_w_self, grad_w_neigh, grad_x_cand, grad_x_test)


def solution(mesh):
    return jax.shard_map(
        local,
        mesh=mesh,
        in_specs=(
            P(("test", "cand"), "feat"),
            P(("cand", "test"), "feat"),
            P(),
            P(),
            P(("cand", "test"), "feat"),
            P("cand", "test", None),
            P("cand", "test", None),
            P("cand", "test", None, None, None),
            P("cand", "test"),
        ),
        out_specs=(
            P(("cand", "test"), "feat"),
            P("feat", None),
            P("feat", None),
            P(("cand", "test"), "feat"),
            P(("test", "cand"), "feat"),
        ),
        check_vma=False,
    )
```

```python
import math

import jax
import jax.numpy as jnp
from jax import lax
from jax.experimental import pallas as pl
from jax.experimental.pallas import tpu as pltpu
from jax.sharding import PartitionSpec as P

HIGHEST = lax.Precision.HIGHEST
SLOT_GROUP = 64


def split_hi_lo(values):
    high = lax.reduce_precision(values, exponent_bits=8, mantissa_bits=7)
    low = values - high
    return jnp.concatenate([high, low], axis=1).astype(jnp.bfloat16)


def unpack_bits(words):
    word_rows, edge = words.shape
    cube = jnp.broadcast_to(words[:, None, :], (word_rows, 8, edge))
    shifts = lax.broadcasted_iota(jnp.int32, (word_rows, 8, edge), 1)
    bits = jnp.bitwise_and(jnp.right_shift(cube, shifts), 1)
    return bits.reshape(word_rows * 8, edge)


def unpack_block(words):
    return unpack_bits(words).astype(jnp.float32)


UNROLL = 8


def live_chunk(live_ref, group):
    base = pl.program_id(0) * group
    return base, base < live_ref[0]


def slot_words(masks_ref, live_ref, base, k):
    keep = jnp.where(base + k < live_ref[0], -1, 0).astype(jnp.int32)
    return unpack_block(jnp.bitwise_and(masks_ref[k], keep)).astype(jnp.bfloat16)


def forward_kernel(live_ref, rows_ref, cols_ref, masks_ref, panel_ref, totals_ref, bits_ref):
    group, _, edge = masks_ref.shape
    row_limit = totals_ref.shape[0] // edge - 1
    col_limit = panel_ref.shape[0] // edge - 1
    half = totals_ref.shape[1]

    @pl.when(pl.program_id(0) == 0)
    def _():
        totals_ref[...] = jnp.zeros_like(totals_ref)
        bits_ref[...] = jnp.zeros_like(bits_ref)

    base, active = live_chunk(live_ref, group)

    @pl.when(active)
    def _():
        def body(k, carry):
            slot = base + k
            row = jnp.clip(rows_ref[slot], 0, row_limit)
            col = jnp.clip(cols_ref[slot], 0, col_limit)
            keep = jnp.where(slot < live_ref[0], -1, 0).astype(jnp.int32)
            bits = unpack_bits(jnp.bitwise_and(masks_ref[k], keep))
            bits_ref[row] += bits
            dense = bits.astype(jnp.float32).astype(jnp.bfloat16)
            tile = panel_ref[pl.ds(pl.multiple_of(col * edge, edge), edge), :]
            prod = jnp.dot(dense, tile, preferred_element_type=jnp.float32)
            start = pl.multiple_of(row * edge, edge)
            totals_ref[pl.ds(start, edge), :] += prod[:, :half] + prod[:, half:]
            return carry

        lax.fori_loop(0, group, body, 0, unroll=UNROLL)


def backward_kernel(live_ref, rows_ref, cols_ref, masks_ref, lifted_ref, out_ref):
    group, _, edge = masks_ref.shape
    row_chunk = lifted_ref.shape[2] // edge
    col_chunk = out_ref.shape[2] // edge
    row_limit = lifted_ref.shape[0] * row_chunk - 1
    col_limit = out_ref.shape[0] * col_chunk - 1
    half = out_ref.shape[1]

    @pl.when(pl.program_id(0) == 0)
    def _():
        out_ref[...] = jnp.zeros_like(out_ref)

    base, active = live_chunk(live_ref, group)

    @pl.when(active)
    def _():
        def body(k, carry):
            slot = base + k
            row = jnp.clip(rows_ref[slot], 0, row_limit)
            col = jnp.clip(cols_ref[slot], 0, col_limit)
            dense = slot_words(masks_ref, live_ref, base, k)
            row_start = pl.multiple_of((row % row_chunk) * edge, edge)
            tile = lifted_ref[row // row_chunk, :, pl.ds(row_start, edge)]
            prod = jnp.dot(tile, dense, preferred_element_type=jnp.float32)
            col_start = pl.multiple_of((col % col_chunk) * edge, edge)
            out_ref[col // col_chunk, :, pl.ds(col_start, edge)] += prod[:half] + prod[half:]
            return carry

        lax.fori_loop(0, group, body, 0, unroll=UNROLL)


def mask_spec(packed_masks, group):
    word_rows, edge = packed_masks.shape[1:]

    def index_map(chunk, live_ref, rows_ref, cols_ref):
        last = jnp.maximum(live_ref[0] - 1, 0) // group
        return (jnp.minimum(chunk, last), 0, 0)

    return pl.BlockSpec((group, word_rows, edge), index_map)


def whole_spec(shape):
    return pl.BlockSpec(shape, lambda chunk, live_ref, rows_ref, cols_ref: (0,) * len(shape))


def slot_pallas(kernel, live, block_rows, block_cols, packed_masks, dense_input, out_shapes):
    slot_total = packed_masks.shape[0]
    group = min(SLOT_GROUP, slot_total)
    grid_spec = pltpu.PrefetchScalarGridSpec(
        num_scalar_prefetch=3,
        grid=(slot_total // group,),
        in_specs=[mask_spec(packed_masks, group), whole_spec(dense_input.shape)],
        out_specs=[whole_spec(shape.shape) for shape in out_shapes],
    )
    return pl.pallas_call(
        kernel,
        grid_spec=grid_spec,
        out_shape=out_shapes,
        compiler_params=pltpu.CompilerParams(dimension_semantics=("arbitrary",)),
    )(live, block_rows, block_cols, packed_masks, dense_input)


def block_aggregate(live, block_rows, block_cols, packed_masks, panel_split, row_blocks):
    edge = packed_masks.shape[-1]
    totals_shape = jax.ShapeDtypeStruct((row_blocks * edge, panel_split.shape[1] // 2), jnp.float32)
    bits_shape = jax.ShapeDtypeStruct((row_blocks, edge, edge), jnp.int32)
    totals, bit_sums = slot_pallas(
        forward_kernel, live, block_rows, block_cols, packed_masks, panel_split,
        [totals_shape, bits_shape],
    )
    return totals, jnp.sum(bit_sums, axis=-1).astype(jnp.float32).reshape(-1)


def block_transpose(live, block_rows, block_cols, packed_masks, lifted_chunks, cand_count):
    edge = packed_masks.shape[-1]
    high = lax.reduce_precision(lifted_chunks, exponent_bits=8, mantissa_bits=7)
    split_t = jnp.concatenate([high, lifted_chunks - high], axis=1).astype(jnp.bfloat16)
    width = lifted_chunks.shape[1]
    panel_cols = lifted_chunks.shape[0] * lifted_chunks.shape[2]
    out_shape = jax.ShapeDtypeStruct((cand_count, width, panel_cols // cand_count), jnp.float32)
    (out_t,) = slot_pallas(
        backward_kernel, live, block_rows, block_cols, packed_masks, split_t, [out_shape]
    )
    return out_t


def axis_bits(axis):
    count = lax.axis_size(axis)
    bits = count.bit_length() - 1
    assert count == 1 << bits
    return bits


def exchange(values, axis, bit):
    count = lax.axis_size(axis)
    return lax.ppermute(values, axis, [(i, i ^ (1 << bit)) for i in range(count)])


def axis_bit(axis, bit):
    return (lax.axis_index(axis) >> bit) & 1


def gather_axis(values, axis, dim):
    if lax.axis_size(axis) != 2:
        return lax.all_gather(values, axis, axis=dim, tiled=True)
    other = exchange(values, axis, 0)
    first = lax.axis_index(axis) == 0
    return jnp.concatenate(
        [jnp.where(first, values, other), jnp.where(first, other, values)], axis=dim
    )


def halving_steps(values, axis, order):
    bits = axis_bits(axis)
    chunk = values.shape[0] >> bits
    data = values.reshape((2,) * bits + (chunk,) + values.shape[1:])
    remaining = list(reversed(range(bits)))
    for bit in order:
        position = remaining.index(bit)
        remaining.remove(bit)
        mine = axis_bit(axis, bit)
        keep = lax.dynamic_index_in_dim(data, mine, position, keepdims=False)
        send = lax.dynamic_index_in_dim(data, 1 - mine, position, keepdims=False)
        data = keep + exchange(send, axis, bit)
    return data


def doubling_steps(values, axis, order):
    data = values
    present = []
    for bit in order:
        position = sum(1 for other in present if other > bit)
        present.insert(position, bit)
        other = exchange(data, axis, bit)
        first = axis_bit(axis, bit) == 0
        data = jnp.where(
            first, jnp.stack([data, other], axis=position), jnp.stack([other, data], axis=position)
        )
    return data


def bit_orders(axis):
    bits = axis_bits(axis)
    ascending = list(range(bits))
    if bits < 2:
        return [ascending]
    return [ascending, [1, 0] + ascending[2:]]


def halving_scatter(values, axis):
    orders = bit_orders(axis)
    bits = axis_bits(axis)
    shaped = values.reshape((1 << bits, -1) + values.shape[1:])
    pieces = jnp.split(shaped, len(orders), axis=1)
    results = [
        halving_steps(piece.reshape((-1,) + values.shape[1:]), axis, order)
        for piece, order in zip(pieces, orders)
    ]
    return jnp.concatenate(results, axis=0)


def doubling_gather(values, axis):
    orders = [list(reversed(order)) for order in bit_orders(axis)]
    pieces = jnp.split(values, len(orders), axis=0)
    results = [doubling_steps(piece, axis, order) for piece, order in zip(pieces, orders)]
    stacked = jnp.concatenate(
        [result.reshape((-1,) + result.shape[-2:]) for result in results], axis=1
    )
    return stacked.reshape((-1,) + values.shape[1:])


def doubling_gather_lanes(values, axis):
    orders = [list(reversed(order)) for order in bit_orders(axis)]
    pieces = jnp.split(values, len(orders), axis=1)
    results = [doubling_steps(piece, axis, order) for piece, order in zip(pieces, orders)]
    return jnp.concatenate(
        [result.reshape((-1,) + result.shape[-2:]) for result in results], axis=2
    )


def butterfly_sum(values, axes):
    for axis in axes:
        for bit in range(axis_bits(axis)):
            values = values + exchange(values, axis, bit)
    return values


def scatter_totals_and_counts(row_totals, row_counts, test_count):
    width = row_totals.shape[1]
    chunk_rows = row_totals.shape[0] // test_count
    count_rows = chunk_rows // width
    padded = -(-count_rows // 16) * 16
    pieces = [
        row_totals.reshape(test_count, chunk_rows, width),
        row_counts.reshape(test_count, count_rows, width),
    ]
    if padded > count_rows:
        pieces.append(jnp.zeros((test_count, padded - count_rows, width), jnp.float32))
    combined = jnp.concatenate(pieces, axis=1).reshape(-1, width)
    own = halving_scatter(combined, "test")
    return own[:chunk_rows], own[chunk_rows : chunk_rows + count_rows].reshape(-1)


def local(x_test, x_cand, w_self, w_neigh, d_out, block_row, block_col, block_mask, block_live):
    packed_masks = block_mask.reshape(block_mask.shape[2:])
    block_rows = block_row.reshape(-1)
    block_cols = block_col.reshape(-1)
    live = jnp.clip(block_live.reshape(1), 0, packed_masks.shape[0])
    block_edge = packed_masks.shape[-1]
    cand_count = lax.axis_size("cand")
    test_count = lax.axis_size("test")
    feat_index = lax.axis_index("feat")
    half_width = x_cand.shape[1]
    row_blocks = x_cand.shape[0] * test_count // block_edge
    col_blocks = x_test.shape[0] * cand_count // block_edge
    panel = doubling_gather(x_test, "cand")
    cand_full = gather_axis(x_cand, "feat", 1)
    row_totals, row_counts = block_aggregate(
        live, block_rows, block_cols, packed_masks, split_hi_lo(panel), row_blocks
    )
    own_totals, degree = scatter_totals_and_counts(row_totals, row_counts, test_count)
    aggregated = own_totals / (1.0 + degree)[:, None]
    self_cols = lax.dynamic_slice_in_dim(w_self, feat_index * half_width, half_width, 1)
    neigh_cols = lax.dynamic_slice_in_dim(w_neigh, feat_index * half_width, half_width, 1)
    self_rows = lax.dynamic_slice_in_dim(w_self, feat_index * half_width, half_width, 0)
    neigh_rows = lax.dynamic_slice_in_dim(w_neigh, feat_index * half_width, half_width, 0)
    aggregated_full = gather_axis(aggregated, "feat", 1)
    pre_act = jnp.dot(cand_full, self_cols, precision=HIGHEST) + jnp.dot(
        aggregated_full, neigh_cols, precision=HIGHEST
    )
    output = jax.nn.silu(pre_act)
    sigmoid_z = jax.nn.sigmoid(pre_act)
    grad_pre = d_out * (sigmoid_z * (1.0 + pre_act * (1.0 - sigmoid_z)))
    grad_full = gather_axis(grad_pre, "feat", 1)
    self_part = jnp.einsum("rk,rh->kh", x_cand, grad_full, precision=HIGHEST)
    neigh_part = jnp.einsum("rk,rh->kh", aggregated, grad_full, precision=HIGHEST)
    grad_w_stack = butterfly_sum(jnp.stack([self_part, neigh_part]), ("cand",))
    grad_w_rows = grad_w_stack.reshape(-1, grad_w_stack.shape[-1] // 2)
    grad_w_rows = doubling_gather(halving_scatter(grad_w_rows, "test"), "test")
    grad_w_pair = grad_w_rows.reshape(grad_w_stack.shape)
    root_count = math.sqrt(x_cand.shape[0] * cand_count * test_count)
    grad_x_cand = jnp.dot(grad_full, self_rows.T, precision=HIGHEST)
    grad_agg = jnp.dot(grad_full, neigh_rows.T, precision=HIGHEST)
    lifted = grad_agg / (1.0 + degree)[:, None]
    lifted_chunks = doubling_gather_lanes(lifted.T, "test")
    grad_w_pair, lifted_chunks = lax.optimization_barrier((grad_w_pair, lifted_chunks))
    grad_w_self = grad_w_pair[0] / root_count
    grad_w_neigh = grad_w_pair[1] / root_count
    out_t = block_transpose(live, block_rows, block_cols, packed_masks, lifted_chunks, cand_count)
    own_t = halving_scatter(out_t.reshape(-1, out_t.shape[2]), "cand")
    grad_x_test = own_t.T
    return (output, grad_w_self, grad_w_neigh, grad_x_cand, grad_x_test)


def solution(mesh):
    return jax.shard_map(
        local,
        mesh=mesh,
        in_specs=(
            P(("test", "cand"), "feat"),
            P(("cand", "test"), "feat"),
            P(),
            P(),
            P(("cand", "test"), "feat"),
            P("cand", "test", None),
            P("cand", "test", None),
            P("cand", "test", None, None, None),
            P("cand", "test"),
        ),
        out_specs=(
            P(("cand", "test"), "feat"),
            P("feat", None),
            P("feat", None),
            P(("cand", "test"), "feat"),
            P(("test", "cand"), "feat"),
        ),
        check_vma=False,
    )
```

```python
import math

import jax
import jax.numpy as jnp
from jax import lax
from jax.experimental import pallas as pl
from jax.experimental.pallas import tpu as pltpu
from jax.sharding import PartitionSpec as P

HIGHEST = lax.Precision.HIGHEST
SLOT_GROUP = 64


def split_hi_lo(values):
    high = lax.reduce_precision(values, exponent_bits=8, mantissa_bits=7)
    low = values - high
    return jnp.concatenate([high, low], axis=1).astype(jnp.bfloat16)


def unpack_bits(words):
    word_rows, edge = words.shape
    cube = jnp.broadcast_to(words[:, None, :], (word_rows, 8, edge))
    shifts = lax.broadcasted_iota(jnp.int32, (word_rows, 8, edge), 1)
    bits = jnp.bitwise_and(jnp.right_shift(cube, shifts), 1)
    return bits.reshape(word_rows * 8, edge)


def unpack_block(words):
    return unpack_bits(words).astype(jnp.float32)


UNROLL = 8


def live_chunk(live_ref, group):
    base = pl.program_id(0) * group
    return base, base < live_ref[0]


def slot_words(masks_ref, live_ref, base, k):
    keep = jnp.where(base + k < live_ref[0], -1, 0).astype(jnp.int32)
    return unpack_block(jnp.bitwise_and(masks_ref[k], keep)).astype(jnp.bfloat16)


def forward_kernel(live_ref, rows_ref, cols_ref, masks_ref, panel_ref, totals_ref, bits_ref):
    group, _, edge = masks_ref.shape
    row_limit = totals_ref.shape[0] // edge - 1
    col_limit = panel_ref.shape[0] // edge - 1
    half = totals_ref.shape[1]

    @pl.when(pl.program_id(0) == 0)
    def _():
        totals_ref[...] = jnp.zeros_like(totals_ref)
        bits_ref[...] = jnp.zeros_like(bits_ref)

    base, active = live_chunk(live_ref, group)

    @pl.when(active)
    def _():
        def body(k, carry):
            slot = base + k
            row = jnp.clip(rows_ref[slot], 0, row_limit)
            col = jnp.clip(cols_ref[slot], 0, col_limit)
            keep = jnp.where(slot < live_ref[0], -1, 0).astype(jnp.int32)
            bits = unpack_bits(jnp.bitwise_and(masks_ref[k], keep))
            bits_ref[row] += bits
            dense = bits.astype(jnp.float32).astype(jnp.bfloat16)
            tile = panel_ref[pl.ds(pl.multiple_of(col * edge, edge), edge), :]
            prod = jnp.dot(dense, tile, preferred_element_type=jnp.float32)
            start = pl.multiple_of(row * edge, edge)
            totals_ref[pl.ds(start, edge), :] += prod[:, :half] + prod[:, half:]
            return carry

        lax.fori_loop(0, group, body, 0, unroll=UNROLL)


def backward_kernel(live_ref, rows_ref, cols_ref, masks_ref, lifted_ref, out_ref):
    group, _, edge = masks_ref.shape
    row_chunk = lifted_ref.shape[2] // edge
    col_chunk = out_ref.shape[2] // edge
    row_limit = lifted_ref.shape[0] * row_chunk - 1
    col_limit = out_ref.shape[0] * col_chunk - 1
    half = out_ref.shape[1]

    @pl.when(pl.program_id(0) == 0)
    def _():
        out_ref[...] = jnp.zeros_like(out_ref)

    base, active = live_chunk(live_ref, group)

    @pl.when(active)
    def _():
        def body(k, carry):
            slot = base + k
            row = jnp.clip(rows_ref[slot], 0, row_limit)
            col = jnp.clip(cols_ref[slot], 0, col_limit)
            dense = slot_words(masks_ref, live_ref, base, k)
            row_start = pl.multiple_of((row % row_chunk) * edge, edge)
            tile = lifted_ref[row // row_chunk, :, pl.ds(row_start, edge)]
            prod = jnp.dot(tile, dense, preferred_element_type=jnp.float32)
            col_start = pl.multiple_of((col % col_chunk) * edge, edge)
            out_ref[col // col_chunk, :, pl.ds(col_start, edge)] += prod[:half] + prod[half:]
            return carry

        lax.fori_loop(0, group, body, 0, unroll=UNROLL)


def mask_spec(packed_masks, group):
    word_rows, edge = packed_masks.shape[1:]

    def index_map(chunk, live_ref, rows_ref, cols_ref):
        last = jnp.maximum(live_ref[0] - 1, 0) // group
        return (jnp.minimum(chunk, last), 0, 0)

    return pl.BlockSpec((group, word_rows, edge), index_map)


def whole_spec(shape):
    return pl.BlockSpec(shape, lambda chunk, live_ref, rows_ref, cols_ref: (0,) * len(shape))


def slot_pallas(kernel, live, block_rows, block_cols, packed_masks, dense_input, out_shapes):
    slot_total = packed_masks.shape[0]
    group = min(SLOT_GROUP, slot_total)
    grid_spec = pltpu.PrefetchScalarGridSpec(
        num_scalar_prefetch=3,
        grid=(slot_total // group,),
        in_specs=[mask_spec(packed_masks, group), whole_spec(dense_input.shape)],
        out_specs=[whole_spec(shape.shape) for shape in out_shapes],
    )
    return pl.pallas_call(
        kernel,
        grid_spec=grid_spec,
        out_shape=out_shapes,
        compiler_params=pltpu.CompilerParams(dimension_semantics=("arbitrary",)),
    )(live, block_rows, block_cols, packed_masks, dense_input)


def block_aggregate(live, block_rows, block_cols, packed_masks, panel_split, row_blocks):
    edge = packed_masks.shape[-1]
    totals_shape = jax.ShapeDtypeStruct((row_blocks * edge, panel_split.shape[1] // 2), jnp.float32)
    bits_shape = jax.ShapeDtypeStruct((row_blocks, edge, edge), jnp.int32)
    totals, bit_sums = slot_pallas(
        forward_kernel, live, block_rows, block_cols, packed_masks, panel_split,
        [totals_shape, bits_shape],
    )
    return totals, jnp.sum(bit_sums, axis=-1).astype(jnp.float32).reshape(-1)


def block_transpose(live, block_rows, block_cols, packed_masks, lifted_chunks, cand_count):
    edge = packed_masks.shape[-1]
    high = lax.reduce_precision(lifted_chunks, exponent_bits=8, mantissa_bits=7)
    split_t = jnp.concatenate([high, lifted_chunks - high], axis=1).astype(jnp.bfloat16)
    width = lifted_chunks.shape[1]
    panel_cols = lifted_chunks.shape[0] * lifted_chunks.shape[2]
    out_shape = jax.ShapeDtypeStruct((cand_count, width, panel_cols // cand_count), jnp.float32)
    (out_t,) = slot_pallas(
        backward_kernel, live, block_rows, block_cols, packed_masks, split_t, [out_shape]
    )
    return out_t


def axis_bits(axis):
    count = lax.axis_size(axis)
    bits = count.bit_length() - 1
    assert count == 1 << bits
    return bits


def exchange(values, axis, bit):
    count = lax.axis_size(axis)
    return lax.ppermute(values, axis, [(i, i ^ (1 << bit)) for i in range(count)])


def axis_bit(axis, bit):
    return (lax.axis_index(axis) >> bit) & 1


def gather_axis(values, axis, dim):
    if lax.axis_size(axis) != 2:
        return lax.all_gather(values, axis, axis=dim, tiled=True)
    other = exchange(values, axis, 0)
    first = lax.axis_index(axis) == 0
    return jnp.concatenate(
        [jnp.where(first, values, other), jnp.where(first, other, values)], axis=dim
    )


def halving_steps(values, axis, order):
    bits = axis_bits(axis)
    chunk = values.shape[0] >> bits
    data = values.reshape((2,) * bits + (chunk,) + values.shape[1:])
    remaining = list(reversed(range(bits)))
    for bit in order:
        position = remaining.index(bit)
        remaining.remove(bit)
        mine = axis_bit(axis, bit)
        keep = lax.dynamic_index_in_dim(data, mine, position, keepdims=False)
        send = lax.dynamic_index_in_dim(data, 1 - mine, position, keepdims=False)
        data = keep + exchange(send, axis, bit)
    return data


def doubling_steps(values, axis, order):
    data = values
    present = []
    for bit in order:
        position = sum(1 for other in present if other > bit)
        present.insert(position, bit)
        other = exchange(data, axis, bit)
        first = axis_bit(axis, bit) == 0
        data = jnp.where(
            first, jnp.stack([data, other], axis=position), jnp.stack([other, data], axis=position)
        )
    return data


def bit_orders(axis):
    bits = axis_bits(axis)
    ascending = list(range(bits))
    if bits < 2:
        return [ascending]
    return [ascending, [1, 0] + ascending[2:]]


def halving_scatter(values, axis):
    orders = bit_orders(axis)
    bits = axis_bits(axis)
    shaped = values.reshape((1 << bits, -1) + values.shape[1:])
    pieces = jnp.split(shaped, len(orders), axis=1)
    results = [
        halving_steps(piece.reshape((-1,) + values.shape[1:]), axis, order)
        for piece, order in zip(pieces, orders)
    ]
    return jnp.concatenate(results, axis=0)


def doubling_gather(values, axis):
    orders = [list(reversed(order)) for order in bit_orders(axis)]
    pieces = jnp.split(values, len(orders), axis=0)
    results = [doubling_steps(piece, axis, order) for piece, order in zip(pieces, orders)]
    stacked = jnp.concatenate(
        [result.reshape((-1,) + result.shape[-2:]) for result in results], axis=1
    )
    return stacked.reshape((-1,) + values.shape[1:])


def doubling_gather_lanes(values, axis):
    orders = [list(reversed(order)) for order in bit_orders(axis)]
    pieces = jnp.split(values, len(orders), axis=1)
    results = [doubling_steps(piece, axis, order) for piece, order in zip(pieces, orders)]
    return jnp.concatenate(
        [result.reshape((-1,) + result.shape[-2:]) for result in results], axis=2
    )


def butterfly_sum(values, axes):
    for axis in axes:
        for bit in range(axis_bits(axis)):
            values = values + exchange(values, axis, bit)
    return values


def scatter_totals_and_counts(row_totals, row_counts, test_count):
    width = row_totals.shape[1]
    chunk_rows = row_totals.shape[0] // test_count
    count_rows = chunk_rows // width
    padded = -(-count_rows // 16) * 16
    pieces = [
        row_totals.reshape(test_count, chunk_rows, width),
        row_counts.reshape(test_count, count_rows, width),
    ]
    if padded > count_rows:
        pieces.append(jnp.zeros((test_count, padded - count_rows, width), jnp.float32))
    combined = jnp.concatenate(pieces, axis=1).reshape(-1, width)
    own = halving_scatter(combined, "test")
    return own[:chunk_rows], own[chunk_rows : chunk_rows + count_rows].reshape(-1)


def local(x_test, x_cand, w_self, w_neigh, d_out, block_row, block_col, block_mask, block_live):
    packed_masks = block_mask.reshape(block_mask.shape[2:])
    block_rows = block_row.reshape(-1)
    block_cols = block_col.reshape(-1)
    live = jnp.clip(block_live.reshape(1), 0, packed_masks.shape[0])
    block_edge = packed_masks.shape[-1]
    cand_count = lax.axis_size("cand")
    test_count = lax.axis_size("test")
    feat_index = lax.axis_index("feat")
    half_width = x_cand.shape[1]
    row_blocks = x_cand.shape[0] * test_count // block_edge
    col_blocks = x_test.shape[0] * cand_count // block_edge
    if cand_count == 2:
        own_split = split_hi_lo(x_test)
        other_split = split_hi_lo(exchange(x_test, "cand", 0))
        first = lax.axis_index("cand") == 0
        panel_split = jnp.concatenate(
            [jnp.where(first, own_split, other_split), jnp.where(first, other_split, own_split)],
            axis=0,
        )
    else:
        panel_split = split_hi_lo(doubling_gather(x_test, "cand"))
    cand_full = gather_axis(x_cand, "feat", 1)
    row_totals, row_counts = block_aggregate(
        live, block_rows, block_cols, packed_masks, panel_split, row_blocks
    )
    own_totals, degree = scatter_totals_and_counts(row_totals, row_counts, test_count)
    aggregated = own_totals / (1.0 + degree)[:, None]
    self_cols = lax.dynamic_slice_in_dim(w_self, feat_index * half_width, half_width, 1)
    neigh_cols = lax.dynamic_slice_in_dim(w_neigh, feat_index * half_width, half_width, 1)
    self_rows = lax.dynamic_slice_in_dim(w_self, feat_index * half_width, half_width, 0)
    neigh_rows = lax.dynamic_slice_in_dim(w_neigh, feat_index * half_width, half_width, 0)
    aggregated_full = gather_axis(aggregated, "feat", 1)
    pre_act = jnp.dot(cand_full, self_cols, precision=HIGHEST) + jnp.dot(
        aggregated_full, neigh_cols, precision=HIGHEST
    )
    output = jax.nn.silu(pre_act)
    sigmoid_z = jax.nn.sigmoid(pre_act)
    grad_pre = d_out * (sigmoid_z * (1.0 + pre_act * (1.0 - sigmoid_z)))
    grad_full = gather_axis(grad_pre, "feat", 1)
    self_part = jnp.einsum("rk,rh->kh", x_cand, grad_full, precision=HIGHEST)
    neigh_part = jnp.einsum("rk,rh->kh", aggregated, grad_full, precision=HIGHEST)
    grad_w_pair = butterfly_sum(jnp.stack([self_part, neigh_part]), ("cand", "test"))
    root_count = math.sqrt(x_cand.shape[0] * cand_count * test_count)
    grad_x_cand = jnp.dot(grad_full, self_rows.T, precision=HIGHEST)
    grad_agg = jnp.dot(grad_full, neigh_rows.T, precision=HIGHEST)
    lifted = grad_agg / (1.0 + degree)[:, None]
    lifted_chunks = doubling_gather_lanes(lifted.T, "test")
    grad_w_pair, lifted_chunks = lax.optimization_barrier((grad_w_pair, lifted_chunks))
    grad_w_self = grad_w_pair[0] / root_count
    grad_w_neigh = grad_w_pair[1] / root_count
    out_t = block_transpose(live, block_rows, block_cols, packed_masks, lifted_chunks, cand_count)
    own_t = halving_scatter(out_t.reshape(-1, out_t.shape[2]), "cand")
    grad_x_test = own_t.T
    return (output, grad_w_self, grad_w_neigh, grad_x_cand, grad_x_test)


def solution(mesh):
    return jax.shard_map(
        local,
        mesh=mesh,
        in_specs=(
            P(("test", "cand"), "feat"),
            P(("cand", "test"), "feat"),
            P(),
            P(),
            P(("cand", "test"), "feat"),
            P("cand", "test", None),
            P("cand", "test", None),
            P("cand", "test", None, None, None),
            P("cand", "test"),
        ),
        out_specs=(
            P(("cand", "test"), "feat"),
            P("feat", None),
            P("feat", None),
            P(("cand", "test"), "feat"),
            P(("test", "cand"), "feat"),
        ),
        check_vma=False,
    )
```

```python
import math

import jax
import jax.numpy as jnp
from jax import lax
from jax.experimental import pallas as pl
from jax.experimental.pallas import tpu as pltpu
from jax.sharding import PartitionSpec as P

HIGHEST = lax.Precision.HIGHEST
SLOT_GROUP = 64


def split_hi_lo(values):
    high = lax.reduce_precision(values, exponent_bits=8, mantissa_bits=7)
    low = values - high
    return jnp.concatenate([high, low], axis=1).astype(jnp.bfloat16)


def unpack_bits(words):
    word_rows, edge = words.shape
    cube = jnp.broadcast_to(words[:, None, :], (word_rows, 8, edge))
    shifts = lax.broadcasted_iota(jnp.int32, (word_rows, 8, edge), 1)
    bits = jnp.bitwise_and(jnp.right_shift(cube, shifts), 1)
    return bits.reshape(word_rows * 8, edge)


def unpack_block(words):
    return unpack_bits(words).astype(jnp.float32)


UNROLL = 8


def live_chunk(live_ref, group):
    base = pl.program_id(0) * group
    return base, base < live_ref[0]


def slot_words(masks_ref, live_ref, base, k):
    keep = jnp.where(base + k < live_ref[0], -1, 0).astype(jnp.int32)
    return unpack_block(jnp.bitwise_and(masks_ref[k], keep)).astype(jnp.bfloat16)


def forward_kernel(live_ref, rows_ref, cols_ref, masks_ref, panel_ref, totals_ref, bits_ref):
    group, _, edge = masks_ref.shape
    row_limit = totals_ref.shape[0] // edge - 1
    col_limit = panel_ref.shape[0] // edge - 1
    half = totals_ref.shape[1]

    @pl.when(pl.program_id(0) == 0)
    def _():
        totals_ref[...] = jnp.zeros_like(totals_ref)
        bits_ref[...] = jnp.zeros_like(bits_ref)

    base, active = live_chunk(live_ref, group)

    @pl.when(active)
    def _():
        def body(k, carry):
            slot = base + k
            row = jnp.clip(rows_ref[slot], 0, row_limit)
            col = jnp.clip(cols_ref[slot], 0, col_limit)
            keep = jnp.where(slot < live_ref[0], -1, 0).astype(jnp.int32)
            bits = unpack_bits(jnp.bitwise_and(masks_ref[k], keep))
            bits_ref[row] += bits
            dense = bits.astype(jnp.float32).astype(jnp.bfloat16)
            tile = panel_ref[pl.ds(pl.multiple_of(col * edge, edge), edge), :]
            prod = jnp.dot(dense, tile, preferred_element_type=jnp.float32)
            start = pl.multiple_of(row * edge, edge)
            totals_ref[pl.ds(start, edge), :] += prod[:, :half] + prod[:, half:]
            return carry

        lax.fori_loop(0, group, body, 0, unroll=UNROLL)


def backward_kernel(live_ref, rows_ref, cols_ref, masks_ref, lifted_ref, out_ref):
    group, _, edge = masks_ref.shape
    row_chunk = lifted_ref.shape[2] // edge
    col_chunk = out_ref.shape[2] // edge
    row_limit = lifted_ref.shape[0] * row_chunk - 1
    col_limit = out_ref.shape[0] * col_chunk - 1
    half = out_ref.shape[1]

    @pl.when(pl.program_id(0) == 0)
    def _():
        out_ref[...] = jnp.zeros_like(out_ref)

    base, active = live_chunk(live_ref, group)

    @pl.when(active)
    def _():
        def body(k, carry):
            slot = base + k
            row = jnp.clip(rows_ref[slot], 0, row_limit)
            col = jnp.clip(cols_ref[slot], 0, col_limit)
            dense = slot_words(masks_ref, live_ref, base, k)
            row_start = pl.multiple_of((row % row_chunk) * edge, edge)
            tile = lifted_ref[row // row_chunk, :, pl.ds(row_start, edge)]
            prod = jnp.dot(tile, dense, preferred_element_type=jnp.float32)
            col_start = pl.multiple_of((col % col_chunk) * edge, edge)
            out_ref[col // col_chunk, :, pl.ds(col_start, edge)] += prod[:half] + prod[half:]
            return carry

        lax.fori_loop(0, group, body, 0, unroll=UNROLL)


def mask_spec(packed_masks, group):
    word_rows, edge = packed_masks.shape[1:]

    def index_map(chunk, live_ref, rows_ref, cols_ref):
        last = jnp.maximum(live_ref[0] - 1, 0) // group
        return (jnp.minimum(chunk, last), 0, 0)

    return pl.BlockSpec((group, word_rows, edge), index_map)


def whole_spec(shape):
    return pl.BlockSpec(shape, lambda chunk, live_ref, rows_ref, cols_ref: (0,) * len(shape))


def slot_pallas(kernel, live, block_rows, block_cols, packed_masks, dense_input, out_shapes):
    slot_total = packed_masks.shape[0]
    group = min(SLOT_GROUP, slot_total)
    grid_spec = pltpu.PrefetchScalarGridSpec(
        num_scalar_prefetch=3,
        grid=(slot_total // group,),
        in_specs=[mask_spec(packed_masks, group), whole_spec(dense_input.shape)],
        out_specs=[whole_spec(shape.shape) for shape in out_shapes],
    )
    return pl.pallas_call(
        kernel,
        grid_spec=grid_spec,
        out_shape=out_shapes,
        compiler_params=pltpu.CompilerParams(dimension_semantics=("arbitrary",)),
    )(live, block_rows, block_cols, packed_masks, dense_input)


def block_aggregate(live, block_rows, block_cols, packed_masks, panel_split, row_blocks):
    edge = packed_masks.shape[-1]
    totals_shape = jax.ShapeDtypeStruct((row_blocks * edge, panel_split.shape[1] // 2), jnp.float32)
    bits_shape = jax.ShapeDtypeStruct((row_blocks, edge, edge), jnp.int32)
    totals, bit_sums = slot_pallas(
        forward_kernel, live, block_rows, block_cols, packed_masks, panel_split,
        [totals_shape, bits_shape],
    )
    return totals, jnp.sum(bit_sums, axis=-1).astype(jnp.float32).reshape(-1)


def block_transpose(live, block_rows, block_cols, packed_masks, lifted_chunks, cand_count):
    edge = packed_masks.shape[-1]
    split_t = lifted_chunks
    width = lifted_chunks.shape[1] // 2
    panel_cols = lifted_chunks.shape[0] * lifted_chunks.shape[2]
    out_shape = jax.ShapeDtypeStruct((cand_count, width, panel_cols // cand_count), jnp.float32)
    (out_t,) = slot_pallas(
        backward_kernel, live, block_rows, block_cols, packed_masks, split_t, [out_shape]
    )
    return out_t


def axis_bits(axis):
    count = lax.axis_size(axis)
    bits = count.bit_length() - 1
    assert count == 1 << bits
    return bits


def exchange(values, axis, bit):
    count = lax.axis_size(axis)
    return lax.ppermute(values, axis, [(i, i ^ (1 << bit)) for i in range(count)])


def axis_bit(axis, bit):
    return (lax.axis_index(axis) >> bit) & 1


def gather_axis(values, axis, dim):
    if lax.axis_size(axis) != 2:
        return lax.all_gather(values, axis, axis=dim, tiled=True)
    other = exchange(values, axis, 0)
    first = lax.axis_index(axis) == 0
    return jnp.concatenate(
        [jnp.where(first, values, other), jnp.where(first, other, values)], axis=dim
    )


def halving_steps(values, axis, order):
    bits = axis_bits(axis)
    chunk = values.shape[0] >> bits
    data = values.reshape((2,) * bits + (chunk,) + values.shape[1:])
    remaining = list(reversed(range(bits)))
    for bit in order:
        position = remaining.index(bit)
        remaining.remove(bit)
        mine = axis_bit(axis, bit)
        keep = lax.dynamic_index_in_dim(data, mine, position, keepdims=False)
        send = lax.dynamic_index_in_dim(data, 1 - mine, position, keepdims=False)
        data = keep + exchange(send, axis, bit)
    return data


def doubling_steps(values, axis, order, finish=None):
    data = values
    present = []
    for step, bit in enumerate(order):
        position = sum(1 for other in present if other > bit)
        present.insert(position, bit)
        other = exchange(data, axis, bit)
        if finish is not None and step == len(order) - 1:
            data, other = finish(data), finish(other)
        first = axis_bit(axis, bit) == 0
        data = jnp.where(
            first, jnp.stack([data, other], axis=position), jnp.stack([other, data], axis=position)
        )
    return data


def bit_orders(axis):
    bits = axis_bits(axis)
    ascending = list(range(bits))
    if bits < 2:
        return [ascending]
    return [ascending, [1, 0] + ascending[2:]]


def halving_scatter(values, axis):
    orders = bit_orders(axis)
    bits = axis_bits(axis)
    shaped = values.reshape((1 << bits, -1) + values.shape[1:])
    pieces = jnp.split(shaped, len(orders), axis=1)
    results = [
        halving_steps(piece.reshape((-1,) + values.shape[1:]), axis, order)
        for piece, order in zip(pieces, orders)
    ]
    return jnp.concatenate(results, axis=0)


def doubling_gather(values, axis):
    orders = [list(reversed(order)) for order in bit_orders(axis)]
    pieces = jnp.split(values, len(orders), axis=0)
    results = [doubling_steps(piece, axis, order) for piece, order in zip(pieces, orders)]
    stacked = jnp.concatenate(
        [result.reshape((-1,) + result.shape[-2:]) for result in results], axis=1
    )
    return stacked.reshape((-1,) + values.shape[1:])


def split_rows(values):
    high = lax.reduce_precision(values, exponent_bits=8, mantissa_bits=7)
    return jnp.concatenate([high, values - high], axis=-2).astype(jnp.bfloat16)


def doubling_gather_lanes(values, axis):
    orders = [list(reversed(order)) for order in bit_orders(axis)]
    pieces = jnp.split(values, len(orders), axis=1)
    results = [
        doubling_steps(piece, axis, order, split_rows) for piece, order in zip(pieces, orders)
    ]
    return jnp.concatenate(
        [result.reshape((-1,) + result.shape[-2:]) for result in results], axis=2
    )


def butterfly_sum(values, axes):
    for axis in axes:
        for bit in range(axis_bits(axis)):
            values = values + exchange(values, axis, bit)
    return values


def scatter_totals_and_counts(row_totals, row_counts, test_count):
    width = row_totals.shape[1]
    chunk_rows = row_totals.shape[0] // test_count
    count_rows = chunk_rows // width
    padded = -(-count_rows // 16) * 16
    pieces = [
        row_totals.reshape(test_count, chunk_rows, width),
        row_counts.reshape(test_count, count_rows, width),
    ]
    if padded > count_rows:
        pieces.append(jnp.zeros((test_count, padded - count_rows, width), jnp.float32))
    combined = jnp.concatenate(pieces, axis=1).reshape(-1, width)
    own = halving_scatter(combined, "test")
    return own[:chunk_rows], own[chunk_rows : chunk_rows + count_rows].reshape(-1)


def local(x_test, x_cand, w_self, w_neigh, d_out, block_row, block_col, block_mask, block_live):
    packed_masks = block_mask.reshape(block_mask.shape[2:])
    block_rows = block_row.reshape(-1)
    block_cols = block_col.reshape(-1)
    live = jnp.clip(block_live.reshape(1), 0, packed_masks.shape[0])
    block_edge = packed_masks.shape[-1]
    cand_count = lax.axis_size("cand")
    test_count = lax.axis_size("test")
    feat_index = lax.axis_index("feat")
    half_width = x_cand.shape[1]
    row_blocks = x_cand.shape[0] * test_count // block_edge
    col_blocks = x_test.shape[0] * cand_count // block_edge
    if cand_count == 2:
        own_split = split_hi_lo(x_test)
        other_split = split_hi_lo(exchange(x_test, "cand", 0))
        first = lax.axis_index("cand") == 0
        panel_split = jnp.concatenate(
            [jnp.where(first, own_split, other_split), jnp.where(first, other_split, own_split)],
            axis=0,
        )
    else:
        panel_split = split_hi_lo(doubling_gather(x_test, "cand"))
    cand_full = gather_axis(x_cand, "feat", 1)
    row_totals, row_counts = block_aggregate(
        live, block_rows, block_cols, packed_masks, panel_split, row_blocks
    )
    own_totals, degree = scatter_totals_and_counts(row_totals, row_counts, test_count)
    aggregated = own_totals / (1.0 + degree)[:, None]
    self_cols = lax.dynamic_slice_in_dim(w_self, feat_index * half_width, half_width, 1)
    neigh_cols = lax.dynamic_slice_in_dim(w_neigh, feat_index * half_width, half_width, 1)
    self_rows = lax.dynamic_slice_in_dim(w_self, feat_index * half_width, half_width, 0)
    neigh_rows = lax.dynamic_slice_in_dim(w_neigh, feat_index * half_width, half_width, 0)
    aggregated_full = gather_axis(aggregated, "feat", 1)
    pre_act = jnp.dot(cand_full, self_cols, precision=HIGHEST) + jnp.dot(
        aggregated_full, neigh_cols, precision=HIGHEST
    )
    output = jax.nn.silu(pre_act)
    sigmoid_z = jax.nn.sigmoid(pre_act)
    grad_pre = d_out * (sigmoid_z * (1.0 + pre_act * (1.0 - sigmoid_z)))
    grad_full = gather_axis(grad_pre, "feat", 1)
    self_part = jnp.einsum("rk,rh->kh", x_cand, grad_full, precision=HIGHEST)
    neigh_part = jnp.einsum("rk,rh->kh", aggregated, grad_full, precision=HIGHEST)
    grad_w_pair = butterfly_sum(jnp.stack([self_part, neigh_part]), ("cand", "test"))
    root_count = math.sqrt(x_cand.shape[0] * cand_count * test_count)
    grad_x_cand = jnp.dot(grad_full, self_rows.T, precision=HIGHEST)
    grad_agg = jnp.dot(grad_full, neigh_rows.T, precision=HIGHEST)
    lifted = grad_agg / (1.0 + degree)[:, None]
    lifted_chunks = doubling_gather_lanes(lifted.T, "test")
    grad_w_pair, lifted_chunks = lax.optimization_barrier((grad_w_pair, lifted_chunks))
    grad_w_self = grad_w_pair[0] / root_count
    grad_w_neigh = grad_w_pair[1] / root_count
    out_t = block_transpose(live, block_rows, block_cols, packed_masks, lifted_chunks, cand_count)
    own_t = halving_scatter(out_t.reshape(-1, out_t.shape[2]), "cand")
    grad_x_test = own_t.T
    return (output, grad_w_self, grad_w_neigh, grad_x_cand, grad_x_test)


def solution(mesh):
    return jax.shard_map(
        local,
        mesh=mesh,
        in_specs=(
            P(("test", "cand"), "feat"),
            P(("cand", "test"), "feat"),
            P(),
            P(),
            P(("cand", "test"), "feat"),
            P("cand", "test", None),
            P("cand", "test", None),
            P("cand", "test", None, None, None),
            P("cand", "test"),
        ),
        out_specs=(
            P(("cand", "test"), "feat"),
            P("feat", None),
            P("feat", None),
            P(("cand", "test"), "feat"),
            P(("test", "cand"), "feat"),
        ),
        check_vma=False,
    )
```

```python
import math

import jax
import jax.numpy as jnp
from jax import lax
from jax.experimental import pallas as pl
from jax.experimental.pallas import tpu as pltpu
from jax.sharding import PartitionSpec as P

HIGHEST = lax.Precision.HIGHEST
SLOT_GROUP = 64


def split_hi_lo(values):
    high = lax.reduce_precision(values, exponent_bits=8, mantissa_bits=7)
    low = values - high
    return jnp.concatenate([high, low], axis=1).astype(jnp.bfloat16)


def unpack_bits(words):
    word_rows, edge = words.shape
    cube = jnp.broadcast_to(words[:, None, :], (word_rows, 8, edge))
    shifts = lax.broadcasted_iota(jnp.int32, (word_rows, 8, edge), 1)
    bits = jnp.bitwise_and(jnp.right_shift(cube, shifts), 1)
    return bits.reshape(word_rows * 8, edge)


def unpack_block(words):
    return unpack_bits(words).astype(jnp.float32)


UNROLL = 8


def live_chunk(live_ref, group):
    base = pl.program_id(0) * group
    return base, base < live_ref[0]


def slot_words(masks_ref, live_ref, base, k):
    keep = jnp.where(base + k < live_ref[0], -1, 0).astype(jnp.int32)
    return unpack_block(jnp.bitwise_and(masks_ref[k], keep)).astype(jnp.bfloat16)


def forward_kernel(live_ref, rows_ref, cols_ref, masks_ref, panel_ref, totals_ref, bits_ref):
    group, _, edge = masks_ref.shape
    row_limit = totals_ref.shape[0] // edge - 1
    col_limit = panel_ref.shape[0] // edge - 1
    half = totals_ref.shape[1]

    @pl.when(pl.program_id(0) == 0)
    def _():
        totals_ref[...] = jnp.zeros_like(totals_ref)
        bits_ref[...] = jnp.zeros_like(bits_ref)

    base, active = live_chunk(live_ref, group)

    @pl.when(active)
    def _():
        def body(k, carry):
            slot = base + k
            row = jnp.clip(rows_ref[slot], 0, row_limit)
            col = jnp.clip(cols_ref[slot], 0, col_limit)
            keep = jnp.where(slot < live_ref[0], -1, 0).astype(jnp.int32)
            bits = unpack_bits(jnp.bitwise_and(masks_ref[k], keep))
            bits_ref[row] += bits
            dense = bits.astype(jnp.float32).astype(jnp.bfloat16)
            tile = panel_ref[pl.ds(pl.multiple_of(col * edge, edge), edge), :]
            prod = jnp.dot(dense, tile, preferred_element_type=jnp.float32)
            start = pl.multiple_of(row * edge, edge)
            totals_ref[pl.ds(start, edge), :] += prod[:, :half] + prod[:, half:]
            return carry

        lax.fori_loop(0, group, body, 0, unroll=UNROLL)


def backward_kernel(live_ref, rows_ref, cols_ref, masks_ref, lifted_ref, out_ref):
    group, _, edge = masks_ref.shape
    row_chunk = lifted_ref.shape[2] // edge
    col_chunk = out_ref.shape[2] // edge
    row_limit = lifted_ref.shape[0] * row_chunk - 1
    col_limit = out_ref.shape[0] * col_chunk - 1
    half = out_ref.shape[1]

    @pl.when(pl.program_id(0) == 0)
    def _():
        out_ref[...] = jnp.zeros_like(out_ref)

    base, active = live_chunk(live_ref, group)

    @pl.when(active)
    def _():
        def body(k, carry):
            slot = base + k
            row = jnp.clip(rows_ref[slot], 0, row_limit)
            col = jnp.clip(cols_ref[slot], 0, col_limit)
            dense = slot_words(masks_ref, live_ref, base, k)
            row_start = pl.multiple_of((row % row_chunk) * edge, edge)
            tile = lifted_ref[row // row_chunk, :, pl.ds(row_start, edge)]
            prod = jnp.dot(tile, dense, preferred_element_type=jnp.float32)
            col_start = pl.multiple_of((col % col_chunk) * edge, edge)
            chunk = jnp.bitwise_xor(col // col_chunk, live_ref[1])
            out_ref[chunk, :, pl.ds(col_start, edge)] += prod[:half] + prod[half:]
            return carry

        lax.fori_loop(0, group, body, 0, unroll=UNROLL)


def backward_pair_kernel(live_ref, rows_ref, cols_ref, masks_ref, lifted_ref, own_ref, other_ref, acc_ref):
    backward_kernel(live_ref, rows_ref, cols_ref, masks_ref, lifted_ref, acc_ref)

    @pl.when(pl.program_id(0) == pl.num_programs(0) - 1)
    def _():
        own_ref[...] = acc_ref[0]
        other_ref[...] = acc_ref[1]


def mask_spec(packed_masks, group):
    word_rows, edge = packed_masks.shape[1:]

    def index_map(chunk, live_ref, rows_ref, cols_ref):
        last = jnp.maximum(live_ref[0] - 1, 0) // group
        return (jnp.minimum(chunk, last), 0, 0)

    return pl.BlockSpec((group, word_rows, edge), index_map)


def whole_spec(shape):
    return pl.BlockSpec(shape, lambda chunk, live_ref, rows_ref, cols_ref: (0,) * len(shape))


def slot_pallas(kernel, live, block_rows, block_cols, packed_masks, dense_input, out_shapes):
    slot_total = packed_masks.shape[0]
    group = min(SLOT_GROUP, slot_total)
    grid_spec = pltpu.PrefetchScalarGridSpec(
        num_scalar_prefetch=3,
        grid=(slot_total // group,),
        in_specs=[mask_spec(packed_masks, group), whole_spec(dense_input.shape)],
        out_specs=[whole_spec(shape.shape) for shape in out_shapes],
    )
    return pl.pallas_call(
        kernel,
        grid_spec=grid_spec,
        out_shape=out_shapes,
        compiler_params=pltpu.CompilerParams(dimension_semantics=("arbitrary",)),
    )(live, block_rows, block_cols, packed_masks, dense_input)


def block_aggregate(live, block_rows, block_cols, packed_masks, panel_split, row_blocks):
    edge = packed_masks.shape[-1]
    totals_shape = jax.ShapeDtypeStruct((row_blocks * edge, panel_split.shape[1] // 2), jnp.float32)
    bits_shape = jax.ShapeDtypeStruct((row_blocks, edge, edge), jnp.int32)
    totals, bit_sums = slot_pallas(
        forward_kernel, live, block_rows, block_cols, packed_masks, panel_split,
        [totals_shape, bits_shape],
    )
    return totals, jnp.sum(bit_sums, axis=-1).astype(jnp.float32).reshape(-1)


def block_transpose(live, block_rows, block_cols, packed_masks, lifted_chunks, cand_count):
    split_t = lifted_chunks
    width = lifted_chunks.shape[1] // 2
    panel_cols = lifted_chunks.shape[0] * lifted_chunks.shape[2]
    acc_shape = (cand_count, width, panel_cols // cand_count)
    if cand_count != 2:
        out_shape = jax.ShapeDtypeStruct(acc_shape, jnp.float32)
        (out_t,) = slot_pallas(
            backward_kernel, live, block_rows, block_cols, packed_masks, split_t, [out_shape]
        )
        return [out_t]
    slot_total = packed_masks.shape[0]
    group = min(SLOT_GROUP, slot_total)
    half_shape = jax.ShapeDtypeStruct(acc_shape[1:], jnp.float32)
    grid_spec = pltpu.PrefetchScalarGridSpec(
        num_scalar_prefetch=3,
        grid=(slot_total // group,),
        in_specs=[mask_spec(packed_masks, group), whole_spec(split_t.shape)],
        out_specs=[whole_spec(acc_shape[1:]), whole_spec(acc_shape[1:])],
        scratch_shapes=[pltpu.VMEM(acc_shape, jnp.float32)],
    )
    return pl.pallas_call(
        backward_pair_kernel,
        grid_spec=grid_spec,
        out_shape=[half_shape, half_shape],
        compiler_params=pltpu.CompilerParams(dimension_semantics=("arbitrary",)),
    )(live, block_rows, block_cols, packed_masks, split_t)


def axis_bits(axis):
    count = lax.axis_size(axis)
    bits = count.bit_length() - 1
    assert count == 1 << bits
    return bits


def exchange(values, axis, bit):
    count = lax.axis_size(axis)
    return lax.ppermute(values, axis, [(i, i ^ (1 << bit)) for i in range(count)])


def axis_bit(axis, bit):
    return (lax.axis_index(axis) >> bit) & 1


def gather_axis(values, axis, dim):
    if lax.axis_size(axis) != 2:
        return lax.all_gather(values, axis, axis=dim, tiled=True)
    other = exchange(values, axis, 0)
    first = lax.axis_index(axis) == 0
    return jnp.concatenate(
        [jnp.where(first, values, other), jnp.where(first, other, values)], axis=dim
    )


def halving_steps(values, axis, order):
    bits = axis_bits(axis)
    chunk = values.shape[0] >> bits
    data = values.reshape((2,) * bits + (chunk,) + values.shape[1:])
    remaining = list(reversed(range(bits)))
    for bit in order:
        position = remaining.index(bit)
        remaining.remove(bit)
        mine = axis_bit(axis, bit)
        keep = lax.dynamic_index_in_dim(data, mine, position, keepdims=False)
        send = lax.dynamic_index_in_dim(data, 1 - mine, position, keepdims=False)
        data = keep + exchange(send, axis, bit)
    return data


def doubling_steps(values, axis, order, finish=None):
    data = values
    present = []
    for step, bit in enumerate(order):
        position = sum(1 for other in present if other > bit)
        present.insert(position, bit)
        other = exchange(data, axis, bit)
        if finish is not None and step == len(order) - 1:
            data, other = finish(data), finish(other)
        first = axis_bit(axis, bit) == 0
        data = jnp.where(
            first, jnp.stack([data, other], axis=position), jnp.stack([other, data], axis=position)
        )
    return data


def bit_orders(axis):
    bits = axis_bits(axis)
    ascending = list(range(bits))
    if bits < 2:
        return [ascending]
    return [ascending, [1, 0] + ascending[2:]]


def halving_scatter(values, axis):
    orders = bit_orders(axis)
    bits = axis_bits(axis)
    shaped = values.reshape((1 << bits, -1) + values.shape[1:])
    pieces = jnp.split(shaped, len(orders), axis=1)
    results = [
        halving_steps(piece.reshape((-1,) + values.shape[1:]), axis, order)
        for piece, order in zip(pieces, orders)
    ]
    return jnp.concatenate(results, axis=0)


def doubling_gather(values, axis):
    orders = [list(reversed(order)) for order in bit_orders(axis)]
    pieces = jnp.split(values, len(orders), axis=0)
    results = [doubling_steps(piece, axis, order) for piece, order in zip(pieces, orders)]
    stacked = jnp.concatenate(
        [result.reshape((-1,) + result.shape[-2:]) for result in results], axis=1
    )
    return stacked.reshape((-1,) + values.shape[1:])


def split_rows(values):
    high = lax.reduce_precision(values, exponent_bits=8, mantissa_bits=7)
    return jnp.concatenate([high, values - high], axis=-2).astype(jnp.bfloat16)


def doubling_gather_lanes(values, axis):
    orders = [list(reversed(order)) for order in bit_orders(axis)]
    pieces = jnp.split(values, len(orders), axis=1)
    results = [
        doubling_steps(piece, axis, order, split_rows) for piece, order in zip(pieces, orders)
    ]
    return jnp.concatenate(
        [result.reshape((-1,) + result.shape[-2:]) for result in results], axis=2
    )


def halving_relative(chunks, axis):
    bits = axis_bits(axis)
    data = chunks.reshape((2,) * bits + chunks.shape[1:])
    remaining = list(reversed(range(bits)))
    for bit in range(bits):
        position = remaining.index(bit)
        remaining.remove(bit)
        keep = lax.index_in_dim(data, 0, position, keepdims=False)
        send = lax.index_in_dim(data, 1, position, keepdims=False)
        data = keep + exchange(send, axis, bit)
    return data


def butterfly_sum(values, axes):
    for axis in axes:
        for bit in range(axis_bits(axis)):
            values = values + exchange(values, axis, bit)
    return values


def scatter_totals_and_counts(row_totals, row_counts, test_count):
    width = row_totals.shape[1]
    chunk_rows = row_totals.shape[0] // test_count
    count_rows = chunk_rows // width
    padded = -(-count_rows // 16) * 16
    pieces = [
        row_totals.reshape(test_count, chunk_rows, width),
        row_counts.reshape(test_count, count_rows, width),
    ]
    if padded > count_rows:
        pieces.append(jnp.zeros((test_count, padded - count_rows, width), jnp.float32))
    combined = jnp.concatenate(pieces, axis=1).reshape(-1, width)
    own = halving_scatter(combined, "test")
    return own[:chunk_rows], own[chunk_rows : chunk_rows + count_rows].reshape(-1)


def local(x_test, x_cand, w_self, w_neigh, d_out, block_row, block_col, block_mask, block_live):
    packed_masks = block_mask.reshape(block_mask.shape[2:])
    block_rows = block_row.reshape(-1)
    block_cols = block_col.reshape(-1)
    live = jnp.concatenate(
        [jnp.clip(block_live.reshape(1), 0, packed_masks.shape[0]), lax.axis_index("cand").reshape(1)]
    ).astype(jnp.int32)
    block_edge = packed_masks.shape[-1]
    cand_count = lax.axis_size("cand")
    test_count = lax.axis_size("test")
    feat_index = lax.axis_index("feat")
    half_width = x_cand.shape[1]
    row_blocks = x_cand.shape[0] * test_count // block_edge
    col_blocks = x_test.shape[0] * cand_count // block_edge
    if cand_count == 2:
        own_split = split_hi_lo(x_test)
        other_split = split_hi_lo(exchange(x_test, "cand", 0))
        first = lax.axis_index("cand") == 0
        panel_split = jnp.concatenate(
            [jnp.where(first, own_split, other_split), jnp.where(first, other_split, own_split)],
            axis=0,
        )
    else:
        panel_split = split_hi_lo(doubling_gather(x_test, "cand"))
    cand_full = gather_axis(x_cand, "feat", 1)
    row_totals, row_counts = block_aggregate(
        live, block_rows, block_cols, packed_masks, panel_split, row_blocks
    )
    own_totals, degree = scatter_totals_and_counts(row_totals, row_counts, test_count)
    aggregated = own_totals / (1.0 + degree)[:, None]
    self_cols = lax.dynamic_slice_in_dim(w_self, feat_index * half_width, half_width, 1)
    neigh_cols = lax.dynamic_slice_in_dim(w_neigh, feat_index * half_width, half_width, 1)
    self_rows = lax.dynamic_slice_in_dim(w_self, feat_index * half_width, half_width, 0)
    neigh_rows = lax.dynamic_slice_in_dim(w_neigh, feat_index * half_width, half_width, 0)
    aggregated_full = gather_axis(aggregated, "feat", 1)
    pre_act = jnp.dot(cand_full, self_cols, precision=HIGHEST) + jnp.dot(
        aggregated_full, neigh_cols, precision=HIGHEST
    )
    output = jax.nn.silu(pre_act)
    sigmoid_z = jax.nn.sigmoid(pre_act)
    grad_pre = d_out * (sigmoid_z * (1.0 + pre_act * (1.0 - sigmoid_z)))
    grad_full = gather_axis(grad_pre, "feat", 1)
    self_part = jnp.einsum("rk,rh->kh", x_cand, grad_full, precision=HIGHEST)
    neigh_part = jnp.einsum("rk,rh->kh", aggregated, grad_full, precision=HIGHEST)
    grad_w_pair = butterfly_sum(jnp.stack([self_part, neigh_part]), ("cand", "test"))
    root_count = math.sqrt(x_cand.shape[0] * cand_count * test_count)
    grad_x_cand = jnp.dot(grad_full, self_rows.T, precision=HIGHEST)
    grad_agg = jnp.dot(grad_full, neigh_rows.T, precision=HIGHEST)
    lifted = grad_agg / (1.0 + degree)[:, None]
    lifted_chunks = doubling_gather_lanes(lifted.T, "test")
    grad_w_pair, lifted_chunks = lax.optimization_barrier((grad_w_pair, lifted_chunks))
    grad_w_self = grad_w_pair[0] / root_count
    grad_w_neigh = grad_w_pair[1] / root_count
    outs = block_transpose(live, block_rows, block_cols, packed_masks, lifted_chunks, cand_count)
    if len(outs) == 2:
        own_t = outs[0] + exchange(outs[1], "cand", 0)
    else:
        own_t = halving_relative(outs[0], "cand")
    grad_x_test = own_t.T
    return (output, grad_w_self, grad_w_neigh, grad_x_cand, grad_x_test)


def solution(mesh):
    return jax.shard_map(
        local,
        mesh=mesh,
        in_specs=(
            P(("test", "cand"), "feat"),
            P(("cand", "test"), "feat"),
            P(),
            P(),
            P(("cand", "test"), "feat"),
            P("cand", "test", None),
            P("cand", "test", None),
            P("cand", "test", None, None, None),
            P("cand", "test"),
        ),
        out_specs=(
            P(("cand", "test"), "feat"),
            P("feat", None),
            P("feat", None),
            P(("cand", "test"), "feat"),
            P(("test", "cand"), "feat"),
        ),
        check_vma=False,
    )
```

```python
import math

import jax
import jax.numpy as jnp
from jax import lax
from jax.experimental import pallas as pl
from jax.experimental.pallas import tpu as pltpu
from jax.sharding import PartitionSpec as P

HIGHEST = lax.Precision.HIGHEST
SLOT_GROUP = 64


def split_hi_lo(values):
    high = lax.reduce_precision(values, exponent_bits=8, mantissa_bits=7)
    low = values - high
    return jnp.concatenate([high, low], axis=1).astype(jnp.bfloat16)


def unpack_bits(words):
    word_rows, edge = words.shape
    cube = jnp.broadcast_to(words[:, None, :], (word_rows, 8, edge))
    shifts = lax.broadcasted_iota(jnp.int32, (word_rows, 8, edge), 1)
    bits = jnp.bitwise_and(jnp.right_shift(cube, shifts), 1)
    return bits.reshape(word_rows * 8, edge)


def unpack_block(words):
    return unpack_bits(words).astype(jnp.float32)


UNROLL = 8


def live_chunk(live_ref, group):
    base = pl.program_id(0) * group
    return base, base < live_ref[0]


def slot_words(masks_ref, live_ref, base, k):
    keep = jnp.where(base + k < live_ref[0], -1, 0).astype(jnp.int32)
    return unpack_block(jnp.bitwise_and(masks_ref[k], keep)).astype(jnp.bfloat16)


def forward_counts_kernel(
    live_ref, rows_ref, cols_ref, masks_ref, panel_ref, totals_ref, counts_ref, bits_ref
):
    forward_kernel(live_ref, rows_ref, cols_ref, masks_ref, panel_ref, totals_ref, bits_ref)

    @pl.when(pl.program_id(0) == pl.num_programs(0) - 1)
    def _():
        counts_ref[...] = jnp.sum(bits_ref[...], axis=-1).astype(jnp.float32)


def forward_kernel(live_ref, rows_ref, cols_ref, masks_ref, panel_ref, totals_ref, bits_ref):
    group, _, edge = masks_ref.shape
    row_limit = totals_ref.shape[0] // edge - 1
    col_limit = panel_ref.shape[0] // edge - 1
    half = totals_ref.shape[1]

    @pl.when(pl.program_id(0) == 0)
    def _():
        totals_ref[...] = jnp.zeros_like(totals_ref)
        bits_ref[...] = jnp.zeros_like(bits_ref)

    base, active = live_chunk(live_ref, group)

    @pl.when(active)
    def _():
        def body(k, carry):
            slot = base + k
            row = jnp.clip(rows_ref[slot], 0, row_limit)
            col = jnp.clip(cols_ref[slot], 0, col_limit)
            keep = jnp.where(slot < live_ref[0], -1, 0).astype(jnp.int32)
            bits = unpack_bits(jnp.bitwise_and(masks_ref[k], keep))
            bits_ref[row] += bits
            dense = bits.astype(jnp.float32).astype(jnp.bfloat16)
            tile = panel_ref[pl.ds(pl.multiple_of(col * edge, edge), edge), :]
            prod = jnp.dot(dense, tile, preferred_element_type=jnp.float32)
            start = pl.multiple_of(row * edge, edge)
            totals_ref[pl.ds(start, edge), :] += prod[:, :half] + prod[:, half:]
            return carry

        lax.fori_loop(0, group, body, 0, unroll=UNROLL)


def backward_kernel(live_ref, rows_ref, cols_ref, masks_ref, lifted_ref, out_ref):
    group, _, edge = masks_ref.shape
    row_chunk = lifted_ref.shape[2] // edge
    col_chunk = out_ref.shape[2] // edge
    row_limit = lifted_ref.shape[0] * row_chunk - 1
    col_limit = out_ref.shape[0] * col_chunk - 1
    half = out_ref.shape[1]

    @pl.when(pl.program_id(0) == 0)
    def _():
        out_ref[...] = jnp.zeros_like(out_ref)

    base, active = live_chunk(live_ref, group)

    @pl.when(active)
    def _():
        def body(k, carry):
            slot = base + k
            row = jnp.clip(rows_ref[slot], 0, row_limit)
            col = jnp.clip(cols_ref[slot], 0, col_limit)
            dense = slot_words(masks_ref, live_ref, base, k)
            row_start = pl.multiple_of((row % row_chunk) * edge, edge)
            tile = lifted_ref[row // row_chunk, :, pl.ds(row_start, edge)]
            prod = jnp.dot(tile, dense, preferred_element_type=jnp.float32)
            col_start = pl.multiple_of((col % col_chunk) * edge, edge)
            chunk = jnp.bitwise_xor(col // col_chunk, live_ref[1])
            out_ref[chunk, :, pl.ds(col_start, edge)] += prod[:half] + prod[half:]
            return carry

        lax.fori_loop(0, group, body, 0, unroll=UNROLL)


def backward_pair_kernel(live_ref, rows_ref, cols_ref, masks_ref, lifted_ref, own_ref, other_ref, acc_ref):
    backward_kernel(live_ref, rows_ref, cols_ref, masks_ref, lifted_ref, acc_ref)

    @pl.when(pl.program_id(0) == pl.num_programs(0) - 1)
    def _():
        own_ref[...] = acc_ref[0]
        other_ref[...] = acc_ref[1]


def mask_spec(packed_masks, group):
    word_rows, edge = packed_masks.shape[1:]

    def index_map(chunk, live_ref, rows_ref, cols_ref):
        last = jnp.maximum(live_ref[0] - 1, 0) // group
        return (jnp.minimum(chunk, last), 0, 0)

    return pl.BlockSpec((group, word_rows, edge), index_map)


def whole_spec(shape):
    return pl.BlockSpec(shape, lambda chunk, live_ref, rows_ref, cols_ref: (0,) * len(shape))


def slot_pallas(kernel, live, block_rows, block_cols, packed_masks, dense_input, out_shapes):
    slot_total = packed_masks.shape[0]
    group = min(SLOT_GROUP, slot_total)
    grid_spec = pltpu.PrefetchScalarGridSpec(
        num_scalar_prefetch=3,
        grid=(slot_total // group,),
        in_specs=[mask_spec(packed_masks, group), whole_spec(dense_input.shape)],
        out_specs=[whole_spec(shape.shape) for shape in out_shapes],
    )
    return pl.pallas_call(
        kernel,
        grid_spec=grid_spec,
        out_shape=out_shapes,
        compiler_params=pltpu.CompilerParams(dimension_semantics=("arbitrary",)),
    )(live, block_rows, block_cols, packed_masks, dense_input)


def block_aggregate(live, block_rows, block_cols, packed_masks, panel_split, row_blocks):
    slot_total, _, edge = packed_masks.shape
    group = min(SLOT_GROUP, slot_total)
    totals_shape = (row_blocks * edge, panel_split.shape[1] // 2)
    grid_spec = pltpu.PrefetchScalarGridSpec(
        num_scalar_prefetch=3,
        grid=(slot_total // group,),
        in_specs=[mask_spec(packed_masks, group), whole_spec(panel_split.shape)],
        out_specs=[whole_spec(totals_shape), whole_spec((row_blocks, edge))],
        scratch_shapes=[pltpu.VMEM((row_blocks, edge, edge), jnp.int32)],
    )
    totals, counts = pl.pallas_call(
        forward_counts_kernel,
        grid_spec=grid_spec,
        out_shape=[
            jax.ShapeDtypeStruct(totals_shape, jnp.float32),
            jax.ShapeDtypeStruct((row_blocks, edge), jnp.float32),
        ],
        compiler_params=pltpu.CompilerParams(dimension_semantics=("arbitrary",)),
    )(live, block_rows, block_cols, packed_masks, panel_split)
    return totals, counts.reshape(-1)


def block_transpose(live, block_rows, block_cols, packed_masks, lifted_chunks, cand_count):
    split_t = lifted_chunks
    width = lifted_chunks.shape[1] // 2
    panel_cols = lifted_chunks.shape[0] * lifted_chunks.shape[2]
    acc_shape = (cand_count, width, panel_cols // cand_count)
    if cand_count != 2:
        out_shape = jax.ShapeDtypeStruct(acc_shape, jnp.float32)
        (out_t,) = slot_pallas(
            backward_kernel, live, block_rows, block_cols, packed_masks, split_t, [out_shape]
        )
        return [out_t]
    slot_total = packed_masks.shape[0]
    group = min(SLOT_GROUP, slot_total)
    half_shape = jax.ShapeDtypeStruct(acc_shape[1:], jnp.float32)
    grid_spec = pltpu.PrefetchScalarGridSpec(
        num_scalar_prefetch=3,
        grid=(slot_total // group,),
        in_specs=[mask_spec(packed_masks, group), whole_spec(split_t.shape)],
        out_specs=[whole_spec(acc_shape[1:]), whole_spec(acc_shape[1:])],
        scratch_shapes=[pltpu.VMEM(acc_shape, jnp.float32)],
    )
    return pl.pallas_call(
        backward_pair_kernel,
        grid_spec=grid_spec,
        out_shape=[half_shape, half_shape],
        compiler_params=pltpu.CompilerParams(dimension_semantics=("arbitrary",)),
    )(live, block_rows, block_cols, packed_masks, split_t)


def axis_bits(axis):
    count = lax.axis_size(axis)
    bits = count.bit_length() - 1
    assert count == 1 << bits
    return bits


def exchange(values, axis, bit):
    count = lax.axis_size(axis)
    return lax.ppermute(values, axis, [(i, i ^ (1 << bit)) for i in range(count)])


def axis_bit(axis, bit):
    return (lax.axis_index(axis) >> bit) & 1


def gather_axis(values, axis, dim):
    if lax.axis_size(axis) != 2:
        return lax.all_gather(values, axis, axis=dim, tiled=True)
    other = exchange(values, axis, 0)
    first = lax.axis_index(axis) == 0
    return jnp.concatenate(
        [jnp.where(first, values, other), jnp.where(first, other, values)], axis=dim
    )


def halving_steps(values, axis, order):
    bits = axis_bits(axis)
    chunk = values.shape[0] >> bits
    data = values.reshape((2,) * bits + (chunk,) + values.shape[1:])
    remaining = list(reversed(range(bits)))
    for bit in order:
        position = remaining.index(bit)
        remaining.remove(bit)
        mine = axis_bit(axis, bit)
        keep = lax.dynamic_index_in_dim(data, mine, position, keepdims=False)
        send = lax.dynamic_index_in_dim(data, 1 - mine, position, keepdims=False)
        data = keep + exchange(send, axis, bit)
    return data


def doubling_steps(values, axis, order, finish=None):
    data = values
    present = []
    for step, bit in enumerate(order):
        position = sum(1 for other in present if other > bit)
        present.insert(position, bit)
        other = exchange(data, axis, bit)
        if finish is not None and step == len(order) - 1:
            data, other = finish(data), finish(other)
        first = axis_bit(axis, bit) == 0
        data = jnp.where(
            first, jnp.stack([data, other], axis=position), jnp.stack([other, data], axis=position)
        )
    return data


def bit_orders(axis):
    bits = axis_bits(axis)
    ascending = list(range(bits))
    if bits < 2:
        return [ascending]
    return [ascending, [1, 0] + ascending[2:]]


def halving_scatter(values, axis):
    orders = bit_orders(axis)
    bits = axis_bits(axis)
    shaped = values.reshape((1 << bits, -1) + values.shape[1:])
    pieces = jnp.split(shaped, len(orders), axis=1)
    results = [
        halving_steps(piece.reshape((-1,) + values.shape[1:]), axis, order)
        for piece, order in zip(pieces, orders)
    ]
    return jnp.concatenate(results, axis=0)


def doubling_gather(values, axis):
    orders = [list(reversed(order)) for order in bit_orders(axis)]
    pieces = jnp.split(values, len(orders), axis=0)
    results = [doubling_steps(piece, axis, order) for piece, order in zip(pieces, orders)]
    stacked = jnp.concatenate(
        [result.reshape((-1,) + result.shape[-2:]) for result in results], axis=1
    )
    return stacked.reshape((-1,) + values.shape[1:])


def split_rows(values):
    high = lax.reduce_precision(values, exponent_bits=8, mantissa_bits=7)
    return jnp.concatenate([high, values - high], axis=-2).astype(jnp.bfloat16)


def doubling_gather_lanes(values, axis):
    orders = [list(reversed(order)) for order in bit_orders(axis)]
    pieces = jnp.split(values, len(orders), axis=1)
    results = [
        doubling_steps(piece, axis, order, split_rows) for piece, order in zip(pieces, orders)
    ]
    return jnp.concatenate(
        [result.reshape((-1,) + result.shape[-2:]) for result in results], axis=2
    )


def halving_relative(chunks, axis):
    bits = axis_bits(axis)
    data = chunks.reshape((2,) * bits + chunks.shape[1:])
    remaining = list(reversed(range(bits)))
    for bit in range(bits):
        position = remaining.index(bit)
        remaining.remove(bit)
        keep = lax.index_in_dim(data, 0, position, keepdims=False)
        send = lax.index_in_dim(data, 1, position, keepdims=False)
        data = keep + exchange(send, axis, bit)
    return data


def butterfly_sum(values, axes):
    for axis in axes:
        for bit in range(axis_bits(axis)):
            values = values + exchange(values, axis, bit)
    return values


def scatter_totals_and_counts(row_totals, row_counts, test_count):
    width = row_totals.shape[1]
    chunk_rows = row_totals.shape[0] // test_count
    count_rows = chunk_rows // width
    padded = -(-count_rows // 16) * 16
    pieces = [
        row_totals.reshape(test_count, chunk_rows, width),
        row_counts.reshape(test_count, count_rows, width),
    ]
    if padded > count_rows:
        pieces.append(jnp.zeros((test_count, padded - count_rows, width), jnp.float32))
    combined = jnp.concatenate(pieces, axis=1).reshape(-1, width)
    own = halving_scatter(combined, "test")
    return own[:chunk_rows], own[chunk_rows : chunk_rows + count_rows].reshape(-1)


def local(x_test, x_cand, w_self, w_neigh, d_out, block_row, block_col, block_mask, block_live):
    packed_masks = block_mask.reshape(block_mask.shape[2:])
    block_rows = block_row.reshape(-1)
    block_cols = block_col.reshape(-1)
    live = jnp.concatenate(
        [jnp.clip(block_live.reshape(1), 0, packed_masks.shape[0]), lax.axis_index("cand").reshape(1)]
    ).astype(jnp.int32)
    block_edge = packed_masks.shape[-1]
    cand_count = lax.axis_size("cand")
    test_count = lax.axis_size("test")
    feat_index = lax.axis_index("feat")
    half_width = x_cand.shape[1]
    row_blocks = x_cand.shape[0] * test_count // block_edge
    col_blocks = x_test.shape[0] * cand_count // block_edge
    if cand_count == 2:
        own_split = split_hi_lo(x_test)
        other_split = split_hi_lo(exchange(x_test, "cand", 0))
        first = lax.axis_index("cand") == 0
        panel_split = jnp.concatenate(
            [jnp.where(first, own_split, other_split), jnp.where(first, other_split, own_split)],
            axis=0,
        )
    else:
        panel_split = split_hi_lo(doubling_gather(x_test, "cand"))
    cand_full = gather_axis(x_cand, "feat", 1)
    row_totals, row_counts = block_aggregate(
        live, block_rows, block_cols, packed_masks, panel_split, row_blocks
    )
    own_totals, degree = scatter_totals_and_counts(row_totals, row_counts, test_count)
    aggregated = own_totals / (1.0 + degree)[:, None]
    self_cols = lax.dynamic_slice_in_dim(w_self, feat_index * half_width, half_width, 1)
    neigh_cols = lax.dynamic_slice_in_dim(w_neigh, feat_index * half_width, half_width, 1)
    self_rows = lax.dynamic_slice_in_dim(w_self, feat_index * half_width, half_width, 0)
    neigh_rows = lax.dynamic_slice_in_dim(w_neigh, feat_index * half_width, half_width, 0)
    aggregated_full = gather_axis(aggregated, "feat", 1)
    pre_act = jnp.dot(cand_full, self_cols, precision=HIGHEST) + jnp.dot(
        aggregated_full, neigh_cols, precision=HIGHEST
    )
    output = jax.nn.silu(pre_act)
    sigmoid_z = jax.nn.sigmoid(pre_act)
    grad_pre = d_out * (sigmoid_z * (1.0 + pre_act * (1.0 - sigmoid_z)))
    grad_full = gather_axis(grad_pre, "feat", 1)
    self_part = jnp.einsum("rk,rh->kh", x_cand, grad_full, precision=HIGHEST)
    neigh_part = jnp.einsum("rk,rh->kh", aggregated, grad_full, precision=HIGHEST)
    grad_w_pair = butterfly_sum(jnp.stack([self_part, neigh_part]), ("cand", "test"))
    root_count = math.sqrt(x_cand.shape[0] * cand_count * test_count)
    grad_x_cand = jnp.dot(grad_full, self_rows.T, precision=HIGHEST)
    grad_agg = jnp.dot(grad_full, neigh_rows.T, precision=HIGHEST)
    lifted = grad_agg / (1.0 + degree)[:, None]
    lifted_chunks = doubling_gather_lanes(lifted.T, "test")
    grad_w_pair, lifted_chunks = lax.optimization_barrier((grad_w_pair, lifted_chunks))
    grad_w_self = grad_w_pair[0] / root_count
    grad_w_neigh = grad_w_pair[1] / root_count
    outs = block_transpose(live, block_rows, block_cols, packed_masks, lifted_chunks, cand_count)
    if len(outs) == 2:
        own_t = outs[0] + exchange(outs[1], "cand", 0)
    else:
        own_t = halving_relative(outs[0], "cand")
    grad_x_test = own_t.T
    return (output, grad_w_self, grad_w_neigh, grad_x_cand, grad_x_test)


def solution(mesh):
    return jax.shard_map(
        local,
        mesh=mesh,
        in_specs=(
            P(("test", "cand"), "feat"),
            P(("cand", "test"), "feat"),
            P(),
            P(),
            P(("cand", "test"), "feat"),
            P("cand", "test", None),
            P("cand", "test", None),
            P("cand", "test", None, None, None),
            P("cand", "test"),
        ),
        out_specs=(
            P(("cand", "test"), "feat"),
            P("feat", None),
            P("feat", None),
            P(("cand", "test"), "feat"),
            P(("test", "cand"), "feat"),
        ),
        check_vma=False,
    )
```
